32 devices in a mesh: box: 8 (over z, y), rep: 4 (over x, core).
Axes of the slice: x: 2, y: 2, z: 4, core: 2. Of those that a mesh axis runs over, the one named last changes fastest.
Arguments:
- targets: float32 [128, 256], P('box'), may hold values from -6 to 6
- noise_var: float32 [128, 256], P('box'), may hold values from 1 to 4
- near_tiles: bfloat16 [128, 8, 256, 256], P('box', 'rep'), may hold values from -1 to 1
- near_partners: int32 [128, 8], P('box', 'rep'), may hold values from -1 to 127, as said below
- leaf_bases: bfloat16 [128, 64, 256], P('box'), may hold values from -0.375 to 0.375
- transfer: bfloat16 [128, 64, 64], P('box'), may hold values from -0.375 to 0.375
- parents: int32 [128], P('box'), may hold values from 0 to 31, as said below
- coupling: bfloat16 [160, 16, 64, 64], P('box', 'rep'), may hold values from -0.109375 to 0.109375
- coupling_partners: int32 [160, 16], P('box', 'rep'), may hold values from -1 to 159, as said below
Outputs:
- weights: float32 [128, 256], P('box')
- residual: float32 [128, 256], P('box')
The draws below stay inside these ranges and needn't reach their ends.
Inputs may be any that keep to these rules, and one draw needn't show every extreme that they name: `near_partners`: the first slot of each box's row is the box itself; every other entry is -1 or a box at most 16 boxes after the row's box. `coupling_partners`: each entry is -1 or a node of the same level as the row's node (leaf box or parent) with a higher number. The parents of the boxes of one index of box are that index's 4 parents. Along those boxes the parent number never decreases, so each parent's children are one contiguous run of one box or more.
All inputs are finite; a program needn't handle non-finite values.
Results may differ from the reference program's by a relative error of at most 0.006.
Values may be sent and summed in bfloat16 or wider, within the bound.
No kernel may reach another device: no remote copies, remote signals or barrier semaphores. Data moves between devices by JAX's collectives and lax.ppermute only.
A program may use at most 64 MiB of HBM per device.

```python
import math
import jax
import jax.numpy as jnp
from jax import lax

LEAF = 256
RANK = 64
BOX_DEV = 16
PAR_DEV = 4
NODE_DEV = 20
ITERS = 2
NBOX = 128
NPAR = 32
NNODE = 160
NEAR = 8
COUP = 16
N_BOX = 8


def near_pairs(key):
    offset = jax.random.randint(jax.random.fold_in(key, 11), (NBOX, NEAR), 1, BOX_DEV + 1)
    keeper = jax.random.randint(jax.random.fold_in(key, 12), (NBOX, NEAR), 0, 4) > 0
    row_ids = jnp.arange(NBOX, dtype=jnp.int32)[:, None]
    partner = row_ids + offset
    partner = jnp.where(keeper & (partner < NBOX), partner, -1)
    slot_ids = jnp.arange(NEAR, dtype=jnp.int32)[None, :]
    partner = jnp.where(slot_ids == 0, row_ids, partner)
    partner = partner.at[0, 1].set(BOX_DEV)
    return partner.astype(jnp.int32)


def draw_near_partners(key, part):
    return near_pairs(key)


def draw_near_tiles(key, part):
    partner = near_pairs(key)
    slot_ids = jnp.arange(NEAR, dtype=jnp.int32)[None, :]
    valid = ((partner >= 0) & (slot_ids > 0)).astype(jnp.int32)
    forward = jnp.sum(valid, axis=1)
    landing = jnp.where(partner >= 0, partner, 0).astype(jnp.int32)
    incoming = jnp.zeros((NBOX,), jnp.int32).at[landing.reshape(-1)].add(valid.reshape(-1))
    degree = (forward + incoming).astype(jnp.float32)
    shape = (NBOX, NEAR, LEAF, LEAF)
    level = 0.2 / LEAF
    rough = jnp.clip(jax.random.normal(jax.random.fold_in(key, 51), shape, jnp.float32), -4.0, 4.0)
    self_mean = level * (0.5 * degree + 1.0)
    mean_table = jnp.where(slot_ids == 0, self_mean[:, None], jnp.float32(level) * jnp.ones((NBOX, NEAR), jnp.float32))
    return (mean_table[:, :, None, None] + rough * (100.0 * LEAF) ** (-0.5)).astype(jnp.bfloat16)


def draw_targets(key, part):
    box_level = 1.0 + 0.5 * jax.random.uniform(jax.random.fold_in(key, 41), (NBOX, 1), jnp.float32, -1.0, 1.0)
    sign_value = (2 * jax.random.randint(jax.random.fold_in(key, 42), (), 0, 2) - 1).astype(jnp.float32)
    rough = jnp.clip(jax.random.normal(jax.random.fold_in(key, 43), (NBOX, LEAF), jnp.float32), -4.0, 4.0)
    return sign_value * box_level + rough


def draw_coupling_partners(key, part):
    node_ids = jnp.arange(NNODE, dtype=jnp.int32)
    device_ids = node_ids // NODE_DEV
    local_ids = node_ids % NODE_DEV
    is_leaf = local_ids < BOX_DEV
    level_index = jnp.where(is_leaf, device_ids * BOX_DEV + local_ids, device_ids * PAR_DEV + local_ids - BOX_DEV)
    level_count = jnp.where(is_leaf, NBOX, NPAR)
    bit_span = int(NBOX).bit_length()
    scale_bits = jax.random.randint(jax.random.fold_in(key, 21), (NNODE, COUP), 0, bit_span)
    raw_bits = jax.random.randint(jax.random.fold_in(key, 22), (NNODE, COUP), 0, 2 ** 30)
    offset = 1 + raw_bits % jnp.left_shift(jnp.ones((), jnp.int32), scale_bits)
    keeper = jax.random.randint(jax.random.fold_in(key, 23), (NNODE, COUP), 0, 4) > 0
    target_ids = level_index[:, None] + offset
    usable = keeper & (target_ids < level_count[:, None])
    leaf_node = target_ids // BOX_DEV * NODE_DEV + target_ids % BOX_DEV
    parent_node = target_ids // PAR_DEV * NODE_DEV + BOX_DEV + target_ids % PAR_DEV
    node_pick = jnp.where(is_leaf[:, None], leaf_node, parent_node)
    result = jnp.where(usable, node_pick, -1).astype(jnp.int32)
    result = result.at[NNODE - 2, 1].set(NNODE - 1)
    return result.astype(jnp.int32)


def draw_parents(key, part):
    row_count = NBOX // BOX_DEV
    key_rows = jax.random.split(jax.random.fold_in(key, 31), row_count)

    def cut_row(row_key):
        return jax.random.permutation(row_key, BOX_DEV - 1)[:PAR_DEV - 1] + 1
    cut_points = jax.vmap(cut_row)(key_rows).astype(jnp.int32)
    positions = jnp.arange(BOX_DEV, dtype=jnp.int32)
    local_parent = jnp.sum((cut_points[:, None, :] <= positions[None, :, None]).astype(jnp.int32), axis=2)
    global_parent = local_parent + jnp.arange(row_count, dtype=jnp.int32)[:, None] * PAR_DEV
    return global_parent.reshape(NBOX).astype(jnp.int32)


def level_of(key, shape, shards, smallest, top_value):
    level = 1.0
    for position, parts in shards:
        heights = jax.random.uniform(jax.random.fold_in(jax.random.fold_in(key, 6), position), (parts,), jnp.float32, smallest / len(shards), top_value / len(shards))
        level = level * jnp.repeat(jnp.exp(heights), shape[position] // parts).reshape((-1,) + (1,) * (len(shape) - 1 - position))
    return level


def noise(stream_key, extent, scale, limit, cuts=(), held_as=jnp.bfloat16):
    drawn = scale * jax.random.normal(stream_key, extent, jnp.float32)
    if cuts:
        drawn = drawn * level_of(stream_key, extent, cuts, -0.22, 0.18)
    return jnp.clip(drawn, -limit, limit).astype(held_as)


def setup_inputs(seed: int = 0) -> dict:
    streams_of = jax.random.split(jax.random.key(seed), 10)
    return {
        "targets": draw_targets(jax.random.fold_in(streams_of[9], 71), 0),
        "noise_var": jnp.clip(jnp.exp(math.log(4.0) - 1.3862944 * jax.random.uniform(streams_of[1], (NBOX, LEAF), jnp.float32) ** level_of(streams_of[1], (NBOX, LEAF), ((0, 8),), -0.2, 0.2)), 1.0, 4.0),
        "near_tiles": draw_near_tiles(jax.random.fold_in(streams_of[9], 71), 0),
        "near_partners": draw_near_partners(jax.random.fold_in(streams_of[9], 71), 0),
        "leaf_bases": noise(streams_of[4], (NBOX, RANK, LEAF), LEAF ** -0.5, 0.375, ((0, 8),)),
        "transfer": noise(streams_of[5], (NBOX, RANK, RANK), (4 * RANK) ** -0.5, 0.375, ((0, 8),)),
        "parents": draw_parents(jax.random.fold_in(streams_of[9], 71), 0),
        "coupling": noise(streams_of[7], (NNODE, COUP, RANK, RANK), (50 * RANK) ** -0.5, 0.109375, ((0, 8), (1, 4))),
        "coupling_partners": draw_coupling_partners(jax.random.fold_in(streams_of[9], 71), 0),
    }


def apply_operator(field, noise_var, near_tiles, near_partners, leaf_bases, transfer, parents, coupling, coupling_partners):
    rounded = field.astype(jnp.bfloat16)
    near_valid = near_partners >= 0
    near_index = jnp.where(near_valid, near_partners, 0).astype(jnp.int32)
    near_in = jnp.where(near_valid[:, :, None], rounded[near_index], jnp.zeros((), jnp.bfloat16))
    block_count = NBOX // BOX_DEV

    def near_block(pieces):
        tile_block, partner_block, self_block = pieces
        tile_wide = tile_block.astype(jnp.float32)
        forward = jnp.einsum("bsij,bsj->bi", tile_wide, partner_block.astype(jnp.float32))
        mirrored = jnp.einsum("bsij,bi->bsj", tile_wide, self_block.astype(jnp.float32))
        return forward, mirrored

    forward, mirrored = lax.map(near_block, (near_tiles.reshape(block_count, BOX_DEV, NEAR, LEAF, LEAF),
                                              near_in.reshape(block_count, BOX_DEV, NEAR, LEAF),
                                              rounded.reshape(block_count, BOX_DEV, LEAF)))
    forward = forward.reshape(NBOX, LEAF)
    mirrored = mirrored.reshape(NBOX * NEAR, LEAF) * near_valid.reshape(-1, 1).astype(jnp.float32)
    near_y = forward + jnp.zeros((NBOX, LEAF), jnp.float32).at[near_index.reshape(-1)].add(mirrored)

    bases_wide = leaf_bases.astype(jnp.float32)
    transfer_wide = transfer.astype(jnp.float32)
    leaf_coef = jnp.einsum("brl,bl->br", bases_wide, rounded.astype(jnp.float32)).astype(jnp.bfloat16)
    upward = jnp.einsum("brq,br->bq", transfer_wide, leaf_coef.astype(jnp.float32))
    parent_coef = jax.ops.segment_sum(upward, parents, num_segments=NPAR).astype(jnp.bfloat16)
    node_coef = jnp.concatenate([leaf_coef.reshape(N_BOX, BOX_DEV, RANK),
                                 parent_coef.reshape(N_BOX, PAR_DEV, RANK)], axis=1).reshape(NNODE, RANK)
    far_valid = coupling_partners >= 0
    far_index = jnp.where(far_valid, coupling_partners, 0).astype(jnp.int32)
    partner_coef = jnp.where(far_valid[:, :, None], node_coef[far_index], jnp.zeros((), jnp.bfloat16))

    def far_block(pieces):
        block_coupling, block_partner, block_self = pieces
        coupling_wide = block_coupling.astype(jnp.float32)
        forward_far = jnp.einsum("nsab,nsb->na", coupling_wide, block_partner.astype(jnp.float32))
        mirror_far = jnp.einsum("nsab,na->nsb", coupling_wide, block_self.astype(jnp.float32))
        return forward_far, mirror_far

    forward_far, mirror_far = lax.map(far_block, (coupling.reshape(N_BOX, NODE_DEV, COUP, RANK, RANK),
                                                  partner_coef.reshape(N_BOX, NODE_DEV, COUP, RANK),
                                                  node_coef.reshape(N_BOX, NODE_DEV, RANK)))
    forward_far = forward_far.reshape(NNODE, RANK)
    mirror_far = mirror_far.reshape(NNODE * COUP, RANK) * far_valid.reshape(-1, 1).astype(jnp.float32)
    node_out = forward_far + jnp.zeros((NNODE, RANK), jnp.float32).at[far_index.reshape(-1)].add(mirror_far)
    node_out = node_out.reshape(N_BOX, NODE_DEV, RANK)
    leaf_out = node_out[:, :BOX_DEV].reshape(NBOX, RANK)
    parent_out = node_out[:, BOX_DEV:].reshape(NPAR, RANK).astype(jnp.bfloat16)
    down_coef = (leaf_out + jnp.einsum("brq,bq->br", transfer_wide, parent_out[parents].astype(jnp.float32))).astype(jnp.bfloat16)
    far_y = jnp.einsum("brl,br->bl", bases_wide, down_coef.astype(jnp.float32))
    return noise_var * field + near_y + far_y


def reference(targets, noise_var, near_tiles, near_partners, leaf_bases, transfer, parents, coupling, coupling_partners):
    weights = jnp.zeros_like(targets)
    residual = targets
    direction = targets
    norm_now = jnp.sum(residual * residual)
    for iteration in range(ITERS):
        image_vec = apply_operator(direction, noise_var, near_tiles, near_partners, leaf_bases, transfer,
                                   parents, coupling, coupling_partners)
        step_size = norm_now / jnp.sum(direction * image_vec)
        weights = weights + step_size * direction
        residual = residual - step_size * image_vec
        norm_next = jnp.sum(residual * residual)
        direction = residual + (norm_next / norm_now) * direction
        norm_now = norm_next
    return weights, residual
```

```python
import jax
import jax.numpy as jnp
from jax import lax
from jax.sharding import PartitionSpec as P

ITERS = 2


def rep_sum(vector):
    count = lax.axis_size("rep")
    me = lax.axis_index("rep")
    pieces = [vector]
    for shift in range(1, count):
        pairs = [(i, (i + shift) % count) for i in range(count)]
        pieces.append(lax.ppermute(vector, "rep", pairs))
    stacked = jnp.stack(pieces)
    order = (me - jnp.arange(count)) % count
    ordered = stacked[order]
    total = ordered[0]
    for i in range(1, count):
        total = total + ordered[i]
    return total


def box_sum(values):
    count = lax.axis_size("box")
    sent = jnp.broadcast_to(values[None, :], (count, values.shape[0]))
    got = lax.all_to_all(sent, "box", 0, 0, tiled=True)
    total = got[0]
    for i in range(1, count):
        total = total + got[i]
    return total


def local(
    targets,
    noise_var,
    near_tiles,
    near_partners,
    leaf_bases,
    transfer,
    parents,
    coupling,
    coupling_partners,
):
    box_count, leaf = targets.shape
    node_count = coupling.shape[0]
    group_count = node_count - box_count
    rank_width = coupling.shape[2]
    box_devices = lax.axis_size("box")
    box_rank = lax.axis_index("box")
    all_nodes = box_devices * node_count
    near_valid = near_partners >= 0
    near_local = jnp.where(near_valid, near_partners - box_rank * box_count, 0)
    near_onehot = (
        (jnp.arange(2 * box_count, dtype=jnp.int32)[:, None] == near_local.reshape(1, -1))
        & near_valid.reshape(1, -1)
    ).astype(jnp.float32)
    parent_local = parents - box_rank * group_count
    parent_onehot = (
        jnp.arange(group_count, dtype=jnp.int32)[:, None] == parent_local[None, :]
    ).astype(jnp.float32)
    far_valid = coupling_partners >= 0
    far_index = jnp.where(far_valid, coupling_partners, 0)
    bf_zero = jnp.zeros((), jnp.bfloat16)
    devices = jnp.arange(box_devices, dtype=jnp.int32)
    below = (devices < box_rank)[:, None, None]
    above = (devices > box_rank)[:, None, None]
    is_next = (devices == box_rank + 1)[:, None, None]
    is_prev = (devices == box_rank - 1)[:, None, None]
    near_size = box_count * leaf
    far_size = node_count * rank_width

    weights = jnp.zeros_like(targets)
    residual = targets
    direction = targets
    norm_start = jnp.sum(targets * targets)
    norm_now = None
    for iteration in range(ITERS):
        rounded = direction.astype(jnp.bfloat16)
        mirrored = jnp.einsum(
            "bsij,bi->bsj", near_tiles, rounded, preferred_element_type=jnp.float32
        )
        landed = jnp.dot(
            near_onehot, mirrored.reshape(-1, mirrored.shape[2]), precision=lax.Precision.HIGHEST
        )
        leaf_coef = jnp.einsum(
            "brl,bl->br", leaf_bases, rounded, preferred_element_type=jnp.float32
        ).astype(jnp.bfloat16)
        upward = jnp.einsum("brq,br->bq", transfer, leaf_coef, preferred_element_type=jnp.float32)
        group_coef = jnp.dot(parent_onehot, upward, precision=lax.Precision.HIGHEST).astype(
            jnp.bfloat16
        )
        node_coef = jnp.concatenate([leaf_coef, group_coef], axis=0)
        far_mirror = jnp.einsum(
            "nsab,na->nsb", coupling, node_coef, preferred_element_type=jnp.float32
        )
        far_mirror = far_mirror * far_valid[:, :, None].astype(jnp.float32)
        spread = (
            jnp.zeros((all_nodes, rank_width), jnp.float32)
            .at[far_index.reshape(-1)]
            .add(far_mirror.reshape(-1, rank_width))
        ).reshape(box_devices, node_count, rank_width)
        coef_wide = node_coef.astype(jnp.float32)
        far_send = jnp.where(below, coef_wide[None], spread)
        near_send = jnp.where(
            is_prev,
            rounded.astype(jnp.float32)[None],
            jnp.where(is_next, landed[box_count:][None], 0.0),
        )
        send = jnp.concatenate(
            [near_send.reshape(box_devices, near_size), far_send.reshape(box_devices, far_size)],
            axis=1,
        )
        got = lax.all_to_all(send, "box", 0, 0, tiled=True)
        got_near = got[:, :near_size].reshape(box_devices, box_count, leaf)
        got_far = got[:, near_size:].reshape(box_devices, node_count, rank_width)
        following = jnp.sum(jnp.where(is_next, got_near, 0.0), axis=0).astype(jnp.bfloat16)
        arrived = jnp.sum(jnp.where(is_prev, got_near, 0.0), axis=0)
        mirror_in = jnp.sum(jnp.where(below, got_far, 0.0), axis=0)
        every_coef = jnp.where(
            above, got_far, jnp.where(devices[:, None, None] == box_rank, coef_wide[None], 0.0)
        ).astype(jnp.bfloat16).reshape(all_nodes, rank_width)

        extended = jnp.concatenate([rounded, following], axis=0)
        near_in = jnp.where(near_valid[:, :, None], extended[near_local], bf_zero)
        forward = jnp.einsum(
            "bsij,bsj->bi", near_tiles, near_in, preferred_element_type=jnp.float32
        )
        near_part = forward + landed[:box_count] + arrived
        partner_coef = jnp.where(far_valid[:, :, None], every_coef[far_index], bf_zero)
        far_forward = jnp.einsum(
            "nsab,nsb->na", coupling, partner_coef, preferred_element_type=jnp.float32
        )
        far_part = far_forward + spread[box_rank] + mirror_in
        both = rep_sum(jnp.concatenate([near_part.reshape(-1), far_part.reshape(-1)]))
        near_total = both[:near_size].reshape(box_count, leaf)
        far_total = both[near_size:].reshape(node_count, rank_width)
        group_out = far_total[box_count:].astype(jnp.bfloat16)
        from_parent = jnp.einsum(
            "brq,bq->br", transfer, group_out[parent_local], preferred_element_type=jnp.float32
        )
        downward = (far_total[:box_count] + from_parent).astype(jnp.bfloat16)
        far_field = jnp.einsum(
            "brl,br->bl", leaf_bases, downward, preferred_element_type=jnp.float32
        )
        image_vec = noise_var * direction + near_total + far_field
        curvature = jnp.sum(direction * image_vec)
        if norm_now is None:
            sums = box_sum(jnp.stack([curvature, norm_start]))
            curvature, norm_now = sums[0], sums[1]
        else:
            curvature = box_sum(curvature[None])[0]
        step_size = norm_now / curvature
        weights = weights + step_size * direction
        residual = residual - step_size * image_vec
        if iteration + 1 < ITERS:
            norm_next = box_sum(jnp.sum(residual * residual)[None])[0]
            direction = residual + norm_next / norm_now * direction
            norm_now = norm_next
    return (weights, residual)


def solution(mesh):
    placed = (
        P("box", None),
        P("box", None),
        P("box", "rep", None, None),
        P("box", "rep"),
        P("box", None, None),
        P("box", None, None),
        P("box"),
        P("box", "rep", None, None),
        P("box", "rep"),
    )
    return jax.shard_map(
        local,
        mesh=mesh,
        in_specs=placed,
        out_specs=(P("box", None), P("box", None)),
        check_vma=False,
    )
```

```python
import jax
import jax.numpy as jnp
from jax import lax
from jax.sharding import PartitionSpec as P

ITERS = 2


def rep_sum(vector):
    count = lax.axis_size("rep")
    if count & (count - 1) == 0:
        stride = 1
        while stride < count:
            pairs = [(i, i ^ stride) for i in range(count)]
            vector = vector + lax.ppermute(vector, "rep", pairs)
            stride *= 2
        return vector
    me = lax.axis_index("rep")
    pieces = [vector]
    for shift in range(1, count):
        pairs = [(i, (i + shift) % count) for i in range(count)]
        pieces.append(lax.ppermute(vector, "rep", pairs))
    ordered = jnp.stack(pieces)[(me - jnp.arange(count)) % count]
    return jnp.sum(ordered, axis=0)


def box_sum(values):
    count = lax.axis_size("box")
    sent = jnp.broadcast_to(values[None, :], (count, values.shape[0]))
    got = lax.all_to_all(sent, "box", 0, 0, tiled=True)
    return jnp.sum(got, axis=0)


def local(
    targets,
    noise_var,
    near_tiles,
    near_partners,
    leaf_bases,
    transfer,
    parents,
    coupling,
    coupling_partners,
):
    box_count, leaf = targets.shape
    node_count = coupling.shape[0]
    group_count = node_count - box_count
    rank_width = coupling.shape[2]
    box_devices = lax.axis_size("box")
    box_rank = lax.axis_index("box")
    all_nodes = box_devices * node_count
    near_valid = near_partners >= 0
    near_local = jnp.where(near_valid, near_partners - box_rank * box_count, 0)
    near_onehot = (
        (jnp.arange(2 * box_count, dtype=jnp.int32)[:, None] == near_local.reshape(1, -1))
        & near_valid.reshape(1, -1)
    ).astype(jnp.float32)
    parent_local = parents - box_rank * group_count
    parent_onehot = (
        jnp.arange(group_count, dtype=jnp.int32)[:, None] == parent_local[None, :]
    ).astype(jnp.float32)
    far_valid = coupling_partners >= 0
    far_index = jnp.where(far_valid, coupling_partners, 0)
    bf_zero = jnp.zeros((), jnp.bfloat16)
    devices = jnp.arange(box_devices, dtype=jnp.int32)
    below = (devices < box_rank)[:, None, None]
    above = (devices > box_rank)[:, None, None]
    near_size = box_count * leaf
    far_size = node_count * rank_width

    weights = jnp.zeros_like(targets)
    residual = targets
    direction = targets
    norm_now = None
    for iteration in range(ITERS):
        rounded = direction.astype(jnp.bfloat16)
        mirrored = jnp.einsum(
            "bsij,bi->bsj", near_tiles, rounded, preferred_element_type=jnp.float32
        )
        landed = jnp.dot(
            near_onehot, mirrored.reshape(-1, mirrored.shape[2]), precision=lax.Precision.HIGHEST
        )
        leaf_coef = jnp.einsum(
            "brl,bl->br", leaf_bases, rounded, preferred_element_type=jnp.float32
        ).astype(jnp.bfloat16)
        upward = jnp.einsum("brq,br->bq", transfer, leaf_coef, preferred_element_type=jnp.float32)
        group_coef = jnp.dot(parent_onehot, upward, precision=lax.Precision.HIGHEST).astype(
            jnp.bfloat16
        )
        node_coef = jnp.concatenate([leaf_coef, group_coef], axis=0)
        far_mirror = jnp.einsum(
            "nsab,na->nsb", coupling, node_coef, preferred_element_type=jnp.float32
        )
        far_mirror = far_mirror * far_valid[:, :, None].astype(jnp.float32)
        spread = (
            jnp.zeros((all_nodes, rank_width), jnp.float32)
            .at[far_index.reshape(-1)]
            .add(far_mirror.reshape(-1, rank_width))
        ).reshape(box_devices, node_count, rank_width)
        following = lax.ppermute(
            rounded, "box", [(i, i - 1) for i in range(1, box_devices)]
        )
        arrived = lax.ppermute(
            landed[box_count:], "box", [(i, i + 1) for i in range(box_devices - 1)]
        )
        coef_wide = node_coef.astype(jnp.float32)
        far_send = jnp.where(below, coef_wide[None], spread)
        got_far = lax.all_to_all(
            far_send.reshape(box_devices, far_size), "box", 0, 0, tiled=True
        ).reshape(box_devices, node_count, rank_width)
        mirror_in = jnp.sum(jnp.where(below, got_far, 0.0), axis=0)
        every_coef = jnp.where(
            above, got_far, jnp.where(devices[:, None, None] == box_rank, coef_wide[None], 0.0)
        ).astype(jnp.bfloat16).reshape(all_nodes, rank_width)

        extended = jnp.concatenate([rounded, following], axis=0)
        near_in = jnp.where(near_valid[:, :, None], extended[near_local], bf_zero)
        forward = jnp.einsum(
            "bsij,bsj->bi", near_tiles, near_in, preferred_element_type=jnp.float32
        )
        near_part = forward + landed[:box_count] + arrived
        partner_coef = jnp.where(far_valid[:, :, None], every_coef[far_index], bf_zero)
        far_forward = jnp.einsum(
            "nsab,nsb->na", coupling, partner_coef, preferred_element_type=jnp.float32
        )
        far_part = far_forward + spread[box_rank] + mirror_in
        both = rep_sum(jnp.concatenate([near_part.reshape(-1), far_part.reshape(-1)]))
        near_total = both[:near_size].reshape(box_count, leaf)
        far_total = both[near_size:].reshape(node_count, rank_width)
        group_out = far_total[box_count:].astype(jnp.bfloat16)
        from_parent = jnp.einsum(
            "brq,bq->br", transfer, group_out[parent_local], preferred_element_type=jnp.float32
        )
        downward = (far_total[:box_count] + from_parent).astype(jnp.bfloat16)
        far_field = jnp.einsum(
            "brl,br->bl", leaf_bases, downward, preferred_element_type=jnp.float32
        )
        image_vec = noise_var * direction + near_total + far_field
        if norm_now is None:
            sums = box_sum(jnp.sum(jnp.stack([direction * image_vec, targets * targets]), axis=(1, 2)))
            curvature, norm_now = sums[0:1], sums[1:2]
        else:
            curvature = box_sum(jnp.sum(direction * image_vec).reshape(1))
        step_size = (norm_now / curvature).reshape(1, 1)
        weights = weights + step_size * direction
        residual = residual - step_size * image_vec
        if iteration + 1 < ITERS:
            norm_next = box_sum(jnp.sum(residual * residual).reshape(1))
            direction = residual + (norm_next / norm_now).reshape(1, 1) * direction
            norm_now = norm_next
    return (weights, residual)


def solution(mesh):
    placed = (
        P("box", None),
        P("box", None),
        P("box", "rep", None, None),
        P("box", "rep"),
        P("box", None, None),
        P("box", None, None),
        P("box"),
        P("box", "rep", None, None),
        P("box", "rep"),
    )
    return jax.shard_map(
        local,
        mesh=mesh,
        in_specs=placed,
        out_specs=(P("box", None), P("box", None)),
        check_vma=False,
    )
```

```python
import jax
import jax.numpy as jnp
from jax import lax
from jax.sharding import PartitionSpec as P

ITERS = 2


def rep_sum(vector):
    count = lax.axis_size("rep")
    if count & (count - 1) == 0:
        stride = 1
        while stride < count:
            pairs = [(i, i ^ stride) for i in range(count)]
            vector = vector + lax.ppermute(vector, "rep", pairs)
            stride *= 2
        return vector
    me = lax.axis_index("rep")
    pieces = [vector]
    for shift in range(1, count):
        pairs = [(i, (i + shift) % count) for i in range(count)]
        pieces.append(lax.ppermute(vector, "rep", pairs))
    ordered = jnp.stack(pieces)[(me - jnp.arange(count)) % count]
    return jnp.sum(ordered, axis=0)


def box_sum(values):
    count = lax.axis_size("box")
    sent = jnp.broadcast_to(values[None, :], (count, values.shape[0]))
    got = lax.all_to_all(sent, "box", 0, 0, tiled=True)
    return jnp.sum(got, axis=0)


def local(
    targets,
    noise_var,
    near_tiles,
    near_partners,
    leaf_bases,
    transfer,
    parents,
    coupling,
    coupling_partners,
):
    box_count, leaf = targets.shape
    node_count = coupling.shape[0]
    group_count = node_count - box_count
    rank_width = coupling.shape[2]
    box_devices = lax.axis_size("box")
    box_rank = lax.axis_index("box")
    all_nodes = box_devices * node_count
    near_valid = near_partners >= 0
    near_local = jnp.where(near_valid, near_partners - box_rank * box_count, 0)
    near_onehot = (
        (jnp.arange(2 * box_count, dtype=jnp.int32)[:, None] == near_local.reshape(1, -1))
        & near_valid.reshape(1, -1)
    ).astype(jnp.float32)
    parent_local = parents - box_rank * group_count
    parent_onehot = (
        jnp.arange(group_count, dtype=jnp.int32)[:, None] == parent_local[None, :]
    ).astype(jnp.float32)
    far_valid = coupling_partners >= 0
    far_index = jnp.where(far_valid, coupling_partners, 0)
    bf_zero = jnp.zeros((), jnp.bfloat16)
    devices = jnp.arange(box_devices, dtype=jnp.int32)
    below = (devices < box_rank)[:, None, None]
    above = (devices > box_rank)[:, None, None]
    near_size = box_count * leaf
    far_size = node_count * rank_width

    weights = jnp.zeros_like(targets)
    residual = targets
    direction = targets
    norm_now = None
    for iteration in range(ITERS):
        rounded = direction.astype(jnp.bfloat16)
        mirrored = jnp.einsum(
            "bsij,bi->bsj", near_tiles, rounded, preferred_element_type=jnp.float32
        )
        landed = jnp.dot(
            near_onehot, mirrored.reshape(-1, mirrored.shape[2]), precision=lax.Precision.HIGHEST
        )
        leaf_coef = jnp.einsum(
            "brl,bl->br", leaf_bases, rounded, preferred_element_type=jnp.float32
        ).astype(jnp.bfloat16)
        upward = jnp.einsum("brq,br->bq", transfer, leaf_coef, preferred_element_type=jnp.float32)
        group_coef = jnp.dot(parent_onehot, upward, precision=lax.Precision.HIGHEST).astype(
            jnp.bfloat16
        )
        node_coef = jnp.concatenate([leaf_coef, group_coef], axis=0)
        far_mirror = jnp.einsum(
            "nsab,na->nsb", coupling, node_coef, preferred_element_type=jnp.float32
        )
        far_mirror = far_mirror * far_valid[:, :, None].astype(jnp.float32)
        spread = (
            jnp.zeros((all_nodes, rank_width), jnp.float32)
            .at[far_index.reshape(-1)]
            .add(far_mirror.reshape(-1, rank_width))
        ).reshape(box_devices, node_count, rank_width)
        following = lax.ppermute(
            rounded, "box", [(i, i - 1) for i in range(1, box_devices)]
        )
        arrived = lax.ppermute(
            landed[box_count:], "box", [(i, i + 1) for i in range(box_devices - 1)]
        )
        coef_wide = node_coef.astype(jnp.float32)
        far_send = jnp.where(below, coef_wide[None], spread)
        got_far = lax.all_to_all(
            far_send.reshape(box_devices, far_size), "box", 0, 0, tiled=True
        ).reshape(box_devices, node_count, rank_width)
        mirror_in = jnp.sum(jnp.where(below, got_far, 0.0), axis=0)
        every_coef = jnp.where(
            above, got_far, jnp.where(devices[:, None, None] == box_rank, coef_wide[None], 0.0)
        ).astype(jnp.bfloat16).reshape(all_nodes, rank_width)

        extended = jnp.concatenate([rounded, following], axis=0)
        near_in = jnp.where(near_valid[:, :, None], extended[near_local], bf_zero)
        forward = jnp.einsum(
            "bsij,bsj->bi", near_tiles, near_in, preferred_element_type=jnp.float32
        )
        near_part = forward + landed[:box_count] + arrived
        partner_coef = jnp.where(far_valid[:, :, None], every_coef[far_index], bf_zero)
        far_forward = jnp.einsum(
            "nsab,nsb->na", coupling, partner_coef, preferred_element_type=jnp.float32
        )
        far_part = far_forward + spread[box_rank] + mirror_in
        both = rep_sum(jnp.concatenate([near_part.reshape(-1), far_part.reshape(-1)]))
        near_total = both[:near_size].reshape(box_count, leaf)
        far_total = both[near_size:].reshape(node_count, rank_width)
        group_out = far_total[box_count:].astype(jnp.bfloat16)
        from_parent = jnp.einsum(
            "brq,bq->br", transfer, group_out[parent_local], preferred_element_type=jnp.float32
        )
        downward = (far_total[:box_count] + from_parent).astype(jnp.bfloat16)
        far_field = jnp.einsum(
            "brl,br->bl", leaf_bases, downward, preferred_element_type=jnp.float32
        )
        image_vec = noise_var * direction + near_total + far_field
        partials = [direction * image_vec]
        if norm_now is None:
            partials.append(targets * targets)
        if iteration + 1 < ITERS:
            partials += [residual * image_vec, image_vec * image_vec]
        sums = box_sum(jnp.sum(jnp.stack(partials), axis=(1, 2)))
        curvature = sums[0:1]
        if norm_now is None:
            norm_now = sums[1:2]
        step_size = norm_now / curvature
        weights = weights + step_size.reshape(1, 1) * direction
        residual = residual - step_size.reshape(1, 1) * image_vec
        if iteration + 1 < ITERS:
            cross, image_square = sums[-2:-1], sums[-1:]
            norm_next = norm_now - 2.0 * step_size * cross + step_size * step_size * image_square
            direction = residual + (norm_next / norm_now).reshape(1, 1) * direction
            norm_now = norm_next
    return (weights, residual)


def solution(mesh):
    placed = (
        P("box", None),
        P("box", None),
        P("box", "rep", None, None),
        P("box", "rep"),
        P("box", None, None),
        P("box", None, None),
        P("box"),
        P("box", "rep", None, None),
        P("box", "rep"),
    )
    return jax.shard_map(
        local,
        mesh=mesh,
        in_specs=placed,
        out_specs=(P("box", None), P("box", None)),
        check_vma=False,
    )
```

```python
import jax
import jax.numpy as jnp
from jax import lax
from jax.sharding import PartitionSpec as P

ITERS = 2


def rep_sum(vector):
    count = lax.axis_size("rep")
    if count & (count - 1) == 0:
        stride = 1
        while stride < count:
            pairs = [(i, i ^ stride) for i in range(count)]
            vector = vector + lax.ppermute(vector, "rep", pairs)
            stride *= 2
        return vector
    me = lax.axis_index("rep")
    pieces = [vector]
    for shift in range(1, count):
        pairs = [(i, (i + shift) % count) for i in range(count)]
        pieces.append(lax.ppermute(vector, "rep", pairs))
    ordered = jnp.stack(pieces)[(me - jnp.arange(count)) % count]
    return jnp.sum(ordered, axis=0)


def box_sum(values, width):
    count = lax.axis_size("box")
    sent = jnp.broadcast_to(values[None, :], (count, values.shape[0]))
    got = lax.all_to_all(sent, "box", 0, 0, tiled=True)
    wide = lax.optimization_barrier(jnp.broadcast_to(got[:, :, None], got.shape + (width,)))
    return jnp.sum(wide, axis=0)


def local(
    targets,
    noise_var,
    near_tiles,
    near_partners,
    leaf_bases,
    transfer,
    parents,
    coupling,
    coupling_partners,
):
    box_count, leaf = targets.shape
    node_count = coupling.shape[0]
    group_count = node_count - box_count
    rank_width = coupling.shape[2]
    box_devices = lax.axis_size("box")
    box_rank = lax.axis_index("box")
    all_nodes = box_devices * node_count
    near_valid = near_partners >= 0
    near_local = jnp.where(near_valid, near_partners - box_rank * box_count, 0)
    near_onehot = (
        (jnp.arange(2 * box_count, dtype=jnp.int32)[:, None] == near_local.reshape(1, -1))
        & near_valid.reshape(1, -1)
    ).astype(jnp.float32)
    parent_local = parents - box_rank * group_count
    parent_onehot = (
        jnp.arange(group_count, dtype=jnp.int32)[:, None] == parent_local[None, :]
    ).astype(jnp.float32)
    far_valid = coupling_partners >= 0
    far_index = jnp.where(far_valid, coupling_partners, 0)
    bf_zero = jnp.zeros((), jnp.bfloat16)
    devices = jnp.arange(box_devices, dtype=jnp.int32)
    below = (devices < box_rank)[:, None, None]
    above = (devices > box_rank)[:, None, None]
    near_size = box_count * leaf
    far_size = node_count * rank_width

    weights = jnp.zeros_like(targets)
    residual = targets
    direction = targets
    norm_now = None
    for iteration in range(ITERS):
        rounded = direction.astype(jnp.bfloat16)
        mirrored = jnp.einsum(
            "bsij,bi->bsj", near_tiles, rounded, preferred_element_type=jnp.float32
        )
        landed = jnp.dot(
            near_onehot, mirrored.reshape(-1, mirrored.shape[2]), precision=lax.Precision.HIGHEST
        )
        leaf_coef = jnp.einsum(
            "brl,bl->br", leaf_bases, rounded, preferred_element_type=jnp.float32
        ).astype(jnp.bfloat16)
        upward = jnp.einsum("brq,br->bq", transfer, leaf_coef, preferred_element_type=jnp.float32)
        group_coef = jnp.dot(parent_onehot, upward, precision=lax.Precision.HIGHEST).astype(
            jnp.bfloat16
        )
        node_coef = jnp.concatenate([leaf_coef, group_coef], axis=0)
        far_mirror = jnp.einsum(
            "nsab,na->nsb", coupling, node_coef, preferred_element_type=jnp.float32
        )
        far_mirror = far_mirror * far_valid[:, :, None].astype(jnp.float32)
        spread = (
            jnp.zeros((all_nodes, rank_width), jnp.float32)
            .at[far_index.reshape(-1)]
            .add(far_mirror.reshape(-1, rank_width))
        ).reshape(box_devices, node_count, rank_width)
        following = lax.ppermute(
            rounded, "box", [(i, i - 1) for i in range(1, box_devices)]
        )
        arrived = lax.ppermute(
            landed[box_count:], "box", [(i, i + 1) for i in range(box_devices - 1)]
        )
        coef_wide = node_coef.astype(jnp.float32)
        far_send = jnp.where(below, coef_wide[None], spread)
        got_far = lax.all_to_all(
            far_send.reshape(box_devices, far_size), "box", 0, 0, tiled=True
        ).reshape(box_devices, node_count, rank_width)
        mirror_in = jnp.sum(jnp.where(below, got_far, 0.0), axis=0)
        every_coef = jnp.where(
            above, got_far, jnp.where(devices[:, None, None] == box_rank, coef_wide[None], 0.0)
        ).astype(jnp.bfloat16).reshape(all_nodes, rank_width)

        extended = jnp.concatenate([rounded, following], axis=0)
        near_in = jnp.where(near_valid[:, :, None], extended[near_local], bf_zero)
        forward = jnp.einsum(
            "bsij,bsj->bi", near_tiles, near_in, preferred_element_type=jnp.float32
        )
        near_part = forward + landed[:box_count] + arrived
        partner_coef = jnp.where(far_valid[:, :, None], every_coef[far_index], bf_zero)
        far_forward = jnp.einsum(
            "nsab,nsb->na", coupling, partner_coef, preferred_element_type=jnp.float32
        )
        far_part = far_forward + spread[box_rank] + mirror_in
        both = rep_sum(jnp.concatenate([near_part.reshape(-1), far_part.reshape(-1)]))
        near_total = both[:near_size].reshape(box_count, leaf)
        far_total = both[near_size:].reshape(node_count, rank_width)
        group_out = far_total[box_count:].astype(jnp.bfloat16)
        from_parent = jnp.einsum(
            "brq,bq->br", transfer, group_out[parent_local], preferred_element_type=jnp.float32
        )
        downward = (far_total[:box_count] + from_parent).astype(jnp.bfloat16)
        far_field = jnp.einsum(
            "brl,br->bl", leaf_bases, downward, preferred_element_type=jnp.float32
        )
        image_vec = noise_var * direction + near_total + far_field
        partials = [direction * image_vec]
        if norm_now is None:
            partials.append(targets * targets)
        if iteration + 1 < ITERS:
            partials += [residual * image_vec, image_vec * image_vec]
        sums = box_sum(jnp.sum(jnp.stack(partials), axis=(1, 2)), leaf)
        curvature = sums[0:1]
        if norm_now is None:
            norm_now = sums[1:2]
        step_size = norm_now / curvature
        weights = weights + step_size * direction
        residual = residual - step_size * image_vec
        if iteration + 1 < ITERS:
            cross, image_square = sums[-2:-1], sums[-1:]
            norm_next = norm_now - 2.0 * step_size * cross + step_size * step_size * image_square
            direction = residual + (norm_next / norm_now) * direction
            norm_now = norm_next
    return (weights, residual)


def solution(mesh):
    placed = (
        P("box", None),
        P("box", None),
        P("box", "rep", None, None),
        P("box", "rep"),
        P("box", None, None),
        P("box", None, None),
        P("box"),
        P("box", "rep", None, None),
        P("box", "rep"),
    )
    return jax.shard_map(
        local,
        mesh=mesh,
        in_specs=placed,
        out_specs=(P("box", None), P("box", None)),
        check_vma=False,
    )
```

```python
import jax
import jax.numpy as jnp
from jax import lax
from jax.sharding import PartitionSpec as P

ITERS = 2


def rep_sum(vector):
    count = lax.axis_size("rep")
    if count & (count - 1) == 0:
        stride = 1
        while stride < count:
            pairs = [(i, i ^ stride) for i in range(count)]
            vector = vector + lax.ppermute(vector, "rep", pairs)
            stride *= 2
        return vector
    me = lax.axis_index("rep")
    pieces = [vector]
    for shift in range(1, count):
        pairs = [(i, (i + shift) % count) for i in range(count)]
        pieces.append(lax.ppermute(vector, "rep", pairs))
    ordered = jnp.stack(pieces)[(me - jnp.arange(count)) % count]
    return jnp.sum(ordered, axis=0)


def box_sum(values, width):
    count = lax.axis_size("box")
    sent = jnp.broadcast_to(values[None, :], (count, values.shape[0]))
    got = lax.all_to_all(sent, "box", 0, 0, tiled=True)
    wide = lax.optimization_barrier(jnp.broadcast_to(got[:, :, None], got.shape + (width,)))
    return jnp.sum(wide, axis=0)


def local(
    targets,
    noise_var,
    near_tiles,
    near_partners,
    leaf_bases,
    transfer,
    parents,
    coupling,
    coupling_partners,
):
    box_count, leaf = targets.shape
    node_count = coupling.shape[0]
    group_count = node_count - box_count
    rank_width = coupling.shape[2]
    box_devices = lax.axis_size("box")
    box_rank = lax.axis_index("box")
    all_nodes = box_devices * node_count
    near_valid = near_partners >= 0
    near_local = jnp.where(near_valid, near_partners - box_rank * box_count, 0)
    near_onehot = (
        (jnp.arange(2 * box_count, dtype=jnp.int32)[:, None] == near_local.reshape(1, -1))
        & near_valid.reshape(1, -1)
    ).astype(jnp.float32)
    parent_local = parents - box_rank * group_count
    parent_onehot = (
        jnp.arange(group_count, dtype=jnp.int32)[:, None] == parent_local[None, :]
    ).astype(jnp.float32)
    far_valid = coupling_partners >= 0
    far_index = jnp.where(far_valid, coupling_partners, 0)
    bf_zero = jnp.zeros((), jnp.bfloat16)
    devices = jnp.arange(box_devices, dtype=jnp.int32)
    below = (devices < box_rank)[:, None, None]
    above = (devices > box_rank)[:, None, None]
    near_size = box_count * leaf
    far_size = node_count * rank_width

    weights = jnp.zeros_like(targets)
    residual = targets
    direction = targets
    norm_now = None
    for iteration in range(ITERS):
        rounded = direction.astype(jnp.bfloat16)
        leaf_coef = jnp.einsum(
            "brl,bl->br", leaf_bases, rounded, preferred_element_type=jnp.float32
        ).astype(jnp.bfloat16)
        upward = jnp.einsum("brq,br->bq", transfer, leaf_coef, preferred_element_type=jnp.float32)
        group_coef = jnp.dot(parent_onehot, upward, precision=lax.Precision.HIGHEST).astype(
            jnp.bfloat16
        )
        node_coef = jnp.concatenate([leaf_coef, group_coef], axis=0)
        far_mirror = jnp.einsum(
            "nsab,na->nsb", coupling, node_coef, preferred_element_type=jnp.float32
        )
        far_mirror = far_mirror * far_valid[:, :, None].astype(jnp.float32)
        spread = (
            jnp.zeros((all_nodes, rank_width), jnp.float32)
            .at[far_index.reshape(-1)]
            .add(far_mirror.reshape(-1, rank_width))
        ).reshape(box_devices, node_count, rank_width)
        following = lax.ppermute(
            rounded, "box", [(i, i - 1) for i in range(1, box_devices)]
        )
        coef_wide = node_coef.astype(jnp.float32)
        far_send = jnp.where(below, coef_wide[None], spread)
        far_send, mirror_field = lax.optimization_barrier((far_send, rounded))
        mirrored = jnp.einsum(
            "bsij,bi->bsj", near_tiles, mirror_field, preferred_element_type=jnp.float32
        )
        landed = jnp.dot(
            near_onehot, mirrored.reshape(-1, mirrored.shape[2]), precision=lax.Precision.HIGHEST
        )
        arrived = lax.ppermute(
            landed[box_count:], "box", [(i, i + 1) for i in range(box_devices - 1)]
        )
        got_far = lax.all_to_all(
            far_send.reshape(box_devices, far_size), "box", 0, 0, tiled=True
        ).reshape(box_devices, node_count, rank_width)
        mirror_in = jnp.sum(jnp.where(below, got_far, 0.0), axis=0)
        every_coef = jnp.where(
            above, got_far, jnp.where(devices[:, None, None] == box_rank, coef_wide[None], 0.0)
        ).astype(jnp.bfloat16).reshape(all_nodes, rank_width)

        extended = jnp.concatenate([rounded, following], axis=0)
        near_in = jnp.where(near_valid[:, :, None], extended[near_local], bf_zero)
        forward = jnp.einsum(
            "bsij,bsj->bi", near_tiles, near_in, preferred_element_type=jnp.float32
        )
        near_part = forward + landed[:box_count] + arrived
        partner_coef = jnp.where(far_valid[:, :, None], every_coef[far_index], bf_zero)
        far_forward = jnp.einsum(
            "nsab,nsb->na", coupling, partner_coef, preferred_element_type=jnp.float32
        )
        far_part = far_forward + spread[box_rank] + mirror_in
        both = rep_sum(jnp.concatenate([near_part.reshape(-1), far_part.reshape(-1)]))
        near_total = both[:near_size].reshape(box_count, leaf)
        far_total = both[near_size:].reshape(node_count, rank_width)
        group_out = far_total[box_count:].astype(jnp.bfloat16)
        from_parent = jnp.einsum(
            "brq,bq->br", transfer, group_out[parent_local], preferred_element_type=jnp.float32
        )
        downward = (far_total[:box_count] + from_parent).astype(jnp.bfloat16)
        far_field = jnp.einsum(
            "brl,br->bl", leaf_bases, downward, preferred_element_type=jnp.float32
        )
        image_vec = noise_var * direction + near_total + far_field
        partials = [direction * image_vec]
        if norm_now is None:
            partials.append(targets * targets)
        if iteration + 1 < ITERS:
            partials += [residual * image_vec, image_vec * image_vec]
        sums = box_sum(jnp.sum(jnp.stack(partials), axis=(1, 2)), leaf)
        curvature = sums[0:1]
        if norm_now is None:
            norm_now = sums[1:2]
        step_size = norm_now / curvature
        weights = weights + step_size * direction
        residual = residual - step_size * image_vec
        if iteration + 1 < ITERS:
            cross, image_square = sums[-2:-1], sums[-1:]
            norm_next = norm_now - 2.0 * step_size * cross + step_size * step_size * image_square
            direction = residual + (norm_next / norm_now) * direction
            norm_now = norm_next
    return (weights, residual)


def solution(mesh):
    placed = (
        P("box", None),
        P("box", None),
        P("box", "rep", None, None),
        P("box", "rep"),
        P("box", None, None),
        P("box", None, None),
        P("box"),
        P("box", "rep", None, None),
        P("box", "rep"),
    )
    return jax.shard_map(
        local,
        mesh=mesh,
        in_specs=placed,
        out_specs=(P("box", None), P("box", None)),
        check_vma=False,
    )
```

```python
import jax
import jax.numpy as jnp
from jax import lax
from jax.sharding import PartitionSpec as P

ITERS = 2


def rep_sum(vector):
    count = lax.axis_size("rep")
    if count & (count - 1) == 0:
        stride = 1
        while stride < count:
            pairs = [(i, i ^ stride) for i in range(count)]
            vector = vector + lax.ppermute(vector, "rep", pairs)
            stride *= 2
        return vector
    me = lax.axis_index("rep")
    pieces = [vector]
    for shift in range(1, count):
        pairs = [(i, (i + shift) % count) for i in range(count)]
        pieces.append(lax.ppermute(vector, "rep", pairs))
    ordered = jnp.stack(pieces)[(me - jnp.arange(count)) % count]
    return jnp.sum(ordered, axis=0)


def box_sum(values, width):
    count = lax.axis_size("box")
    sent = jnp.broadcast_to(values[None, :], (count, values.shape[0]))
    got = lax.all_to_all(sent, "box", 0, 0, tiled=True)
    wide = lax.optimization_barrier(jnp.broadcast_to(got[:, :, None], got.shape + (width,)))
    return jnp.sum(wide, axis=0)


def local(
    targets,
    noise_var,
    near_tiles,
    near_partners,
    leaf_bases,
    transfer,
    parents,
    coupling,
    coupling_partners,
):
    box_count, leaf = targets.shape
    node_count = coupling.shape[0]
    group_count = node_count - box_count
    rank_width = coupling.shape[2]
    box_devices = lax.axis_size("box")
    box_rank = lax.axis_index("box")
    all_nodes = box_devices * node_count
    near_valid = near_partners >= 0
    near_local = jnp.where(near_valid, near_partners - box_rank * box_count, 0)
    near_onehot = (
        (jnp.arange(2 * box_count, dtype=jnp.int32)[:, None] == near_local.reshape(1, -1))
        & near_valid.reshape(1, -1)
    ).astype(jnp.float32)
    parent_local = parents - box_rank * group_count
    parent_onehot = (
        jnp.arange(group_count, dtype=jnp.int32)[:, None] == parent_local[None, :]
    ).astype(jnp.float32)
    far_valid = coupling_partners >= 0
    far_index = jnp.where(far_valid, coupling_partners, 0)
    bf_zero = jnp.zeros((), jnp.bfloat16)
    devices = jnp.arange(box_devices, dtype=jnp.int32)
    below = (devices < box_rank)[:, None, None]
    above = (devices > box_rank)[:, None, None]
    near_size = box_count * leaf
    far_size = node_count * rank_width

    weights = jnp.zeros_like(targets)
    residual = targets
    direction = targets
    norm_now = None
    for iteration in range(ITERS):
        rounded = direction.astype(jnp.bfloat16)
        leaf_coef = jnp.einsum(
            "brl,bl->br", leaf_bases, rounded, preferred_element_type=jnp.float32
        ).astype(jnp.bfloat16)
        upward = jnp.einsum("brq,br->bq", transfer, leaf_coef, preferred_element_type=jnp.float32)
        group_coef = jnp.dot(parent_onehot, upward, precision=lax.Precision.HIGHEST).astype(
            jnp.bfloat16
        )
        node_coef = jnp.concatenate([leaf_coef, group_coef], axis=0)
        far_mirror = jnp.einsum(
            "nsab,na->nsb", coupling, node_coef, preferred_element_type=jnp.float32
        )
        far_mirror = far_mirror * far_valid[:, :, None].astype(jnp.float32)
        spread = (
            jnp.zeros((all_nodes, rank_width), jnp.float32)
            .at[far_index.reshape(-1)]
            .add(far_mirror.reshape(-1, rank_width))
        ).reshape(box_devices, node_count, rank_width)
        following = lax.ppermute(
            rounded, "box", [(i, i - 1) for i in range(1, box_devices)]
        )
        coef_wide = node_coef.astype(jnp.float32)
        far_send = jnp.where(below, coef_wide[None], spread)
        mirror_field = rounded
        if iteration > 0:
            far_send, mirror_field = lax.optimization_barrier((far_send, rounded))
        mirrored = jnp.einsum(
            "bsij,bi->bsj", near_tiles, mirror_field, preferred_element_type=jnp.float32
        )
        landed = jnp.dot(
            near_onehot, mirrored.reshape(-1, mirrored.shape[2]), precision=lax.Precision.HIGHEST
        )
        arrived = lax.ppermute(
            landed[box_count:], "box", [(i, i + 1) for i in range(box_devices - 1)]
        )
        got_far = lax.all_to_all(
            far_send.reshape(box_devices, far_size), "box", 0, 0, tiled=True
        ).reshape(box_devices, node_count, rank_width)
        mirror_in = jnp.sum(jnp.where(below, got_far, 0.0), axis=0)
        every_coef = jnp.where(
            above, got_far, jnp.where(devices[:, None, None] == box_rank, coef_wide[None], 0.0)
        ).astype(jnp.bfloat16).reshape(all_nodes, rank_width)

        extended = jnp.concatenate([rounded, following], axis=0)
        near_in = jnp.where(near_valid[:, :, None], extended[near_local], bf_zero)
        forward = jnp.einsum(
            "bsij,bsj->bi", near_tiles, near_in, preferred_element_type=jnp.float32
        )
        near_part = forward + landed[:box_count] + arrived
        partner_coef = jnp.where(far_valid[:, :, None], every_coef[far_index], bf_zero)
        far_forward = jnp.einsum(
            "nsab,nsb->na", coupling, partner_coef, preferred_element_type=jnp.float32
        )
        far_part = far_forward + spread[box_rank] + mirror_in
        both = rep_sum(jnp.concatenate([near_part.reshape(-1), far_part.reshape(-1)]))
        near_total = both[:near_size].reshape(box_count, leaf)
        far_total = both[near_size:].reshape(node_count, rank_width)
        group_out = far_total[box_count:].astype(jnp.bfloat16)
        from_parent = jnp.einsum(
            "brq,bq->br", transfer, group_out[parent_local], preferred_element_type=jnp.float32
        )
        downward = (far_total[:box_count] + from_parent).astype(jnp.bfloat16)
        far_field = jnp.einsum(
            "brl,br->bl", leaf_bases, downward, preferred_element_type=jnp.float32
        )
        image_vec = noise_var * direction + near_total + far_field
        partials = [direction * image_vec]
        if norm_now is None:
            partials.append(targets * targets)
        if iteration + 1 < ITERS:
            partials += [residual * image_vec, image_vec * image_vec]
        sums = box_sum(jnp.sum(jnp.stack(partials), axis=(1, 2)), leaf)
        curvature = sums[0:1]
        if norm_now is None:
            norm_now = sums[1:2]
        step_size = norm_now / curvature
        weights = weights + step_size * direction
        residual = residual - step_size * image_vec
        if iteration + 1 < ITERS:
            cross, image_square = sums[-2:-1], sums[-1:]
            norm_next = norm_now - 2.0 * step_size * cross + step_size * step_size * image_square
            direction = residual + (norm_next / norm_now) * direction
            norm_now = norm_next
    return (weights, residual)


def solution(mesh):
    placed = (
        P("box", None),
        P("box", None),
        P("box", "rep", None, None),
        P("box", "rep"),
        P("box", None, None),
        P("box", None, None),
        P("box"),
        P("box", "rep", None, None),
        P("box", "rep"),
    )
    return jax.shard_map(
        local,
        mesh=mesh,
        in_specs=placed,
        out_specs=(P("box", None), P("box", None)),
        check_vma=False,
    )
```

```python
import jax
import jax.numpy as jnp
from jax import lax
from jax.sharding import PartitionSpec as P

ITERS = 2


def rep_sum(vector):
    count = lax.axis_size("rep")
    if count == 4:
        got = [
            lax.ppermute(vector, "rep", [(i, i ^ mask) for i in range(count)])
            for mask in (1, 2, 3)
        ]
        return (vector + got[0]) + (got[1] + got[2])
    if count & (count - 1) == 0:
        stride = 1
        while stride < count:
            pairs = [(i, i ^ stride) for i in range(count)]
            vector = vector + lax.ppermute(vector, "rep", pairs)
            stride *= 2
        return vector
    me = lax.axis_index("rep")
    pieces = [vector]
    for shift in range(1, count):
        pairs = [(i, (i + shift) % count) for i in range(count)]
        pieces.append(lax.ppermute(vector, "rep", pairs))
    ordered = jnp.stack(pieces)[(me - jnp.arange(count)) % count]
    return jnp.sum(ordered, axis=0)


def box_sum(values, width):
    count = lax.axis_size("box")
    sent = jnp.broadcast_to(values[None, :], (count, values.shape[0]))
    got = lax.all_to_all(sent, "box", 0, 0, tiled=True)
    wide = lax.optimization_barrier(jnp.broadcast_to(got[:, :, None], got.shape + (width,)))
    return jnp.sum(wide, axis=0)


def local(
    targets,
    noise_var,
    near_tiles,
    near_partners,
    leaf_bases,
    transfer,
    parents,
    coupling,
    coupling_partners,
):
    box_count, leaf = targets.shape
    node_count = coupling.shape[0]
    group_count = node_count - box_count
    rank_width = coupling.shape[2]
    box_devices = lax.axis_size("box")
    box_rank = lax.axis_index("box")
    all_nodes = box_devices * node_count
    near_valid = near_partners >= 0
    near_local = jnp.where(near_valid, near_partners - box_rank * box_count, 0)
    near_onehot = (
        (jnp.arange(2 * box_count, dtype=jnp.int32)[:, None] == near_local.reshape(1, -1))
        & near_valid.reshape(1, -1)
    ).astype(jnp.float32)
    parent_local = parents - box_rank * group_count
    parent_onehot = (
        jnp.arange(group_count, dtype=jnp.int32)[:, None] == parent_local[None, :]
    ).astype(jnp.float32)
    far_valid = coupling_partners >= 0
    far_index = jnp.where(far_valid, coupling_partners, 0)
    bf_zero = jnp.zeros((), jnp.bfloat16)
    devices = jnp.arange(box_devices, dtype=jnp.int32)
    below = (devices < box_rank)[:, None, None]
    above = (devices > box_rank)[:, None, None]
    near_size = box_count * leaf
    far_size = node_count * rank_width

    weights = jnp.zeros_like(targets)
    residual = targets
    direction = targets
    norm_now = None
    for iteration in range(ITERS):
        rounded = direction.astype(jnp.bfloat16)
        mirrored = jnp.einsum(
            "bsij,bi->bsj", near_tiles, rounded, preferred_element_type=jnp.float32
        )
        landed = jnp.dot(
            near_onehot, mirrored.reshape(-1, mirrored.shape[2]), precision=lax.Precision.HIGHEST
        )
        leaf_coef = jnp.einsum(
            "brl,bl->br", leaf_bases, rounded, preferred_element_type=jnp.float32
        ).astype(jnp.bfloat16)
        upward = jnp.einsum("brq,br->bq", transfer, leaf_coef, preferred_element_type=jnp.float32)
        group_coef = jnp.dot(parent_onehot, upward, precision=lax.Precision.HIGHEST).astype(
            jnp.bfloat16
        )
        node_coef = jnp.concatenate([leaf_coef, group_coef], axis=0)
        far_mirror = jnp.einsum(
            "nsab,na->nsb", coupling, node_coef, preferred_element_type=jnp.float32
        )
        far_mirror = far_mirror * far_valid[:, :, None].astype(jnp.float32)
        spread = (
            jnp.zeros((all_nodes, rank_width), jnp.float32)
            .at[far_index.reshape(-1)]
            .add(far_mirror.reshape(-1, rank_width))
        ).reshape(box_devices, node_count, rank_width)
        following = lax.ppermute(
            rounded, "box", [(i, i - 1) for i in range(1, box_devices)]
        )
        arrived = lax.ppermute(
            landed[box_count:], "box", [(i, i + 1) for i in range(box_devices - 1)]
        )
        coef_wide = node_coef.astype(jnp.float32)
        far_send = jnp.where(below, coef_wide[None], spread)
        got_far = lax.all_to_all(
            far_send.reshape(box_devices, far_size), "box", 0, 0, tiled=True
        ).reshape(box_devices, node_count, rank_width)
        mirror_in = jnp.sum(jnp.where(below, got_far, 0.0), axis=0)
        every_coef = jnp.where(
            above, got_far, jnp.where(devices[:, None, None] == box_rank, coef_wide[None], 0.0)
        ).astype(jnp.bfloat16).reshape(all_nodes, rank_width)

        extended = jnp.concatenate([rounded, following], axis=0)
        near_in = jnp.where(near_valid[:, :, None], extended[near_local], bf_zero)
        forward = jnp.einsum(
            "bsij,bsj->bi", near_tiles, near_in, preferred_element_type=jnp.float32
        )
        near_part = forward + landed[:box_count] + arrived
        partner_coef = jnp.where(far_valid[:, :, None], every_coef[far_index], bf_zero)
        far_forward = jnp.einsum(
            "nsab,nsb->na", coupling, partner_coef, preferred_element_type=jnp.float32
        )
        far_part = far_forward + spread[box_rank] + mirror_in
        both = rep_sum(jnp.concatenate([near_part.reshape(-1), far_part.reshape(-1)]))
        near_total = both[:near_size].reshape(box_count, leaf)
        far_total = both[near_size:].reshape(node_count, rank_width)
        group_out = far_total[box_count:].astype(jnp.bfloat16)
        from_parent = jnp.einsum(
            "brq,bq->br", transfer, group_out[parent_local], preferred_element_type=jnp.float32
        )
        downward = (far_total[:box_count] + from_parent).astype(jnp.bfloat16)
        far_field = jnp.einsum(
            "brl,br->bl", leaf_bases, downward, preferred_element_type=jnp.float32
        )
        image_vec = noise_var * direction + near_total + far_field
        partials = [direction * image_vec]
        if norm_now is None:
            partials.append(targets * targets)
        if iteration + 1 < ITERS:
            partials += [residual * image_vec, image_vec * image_vec]
        sums = box_sum(jnp.sum(jnp.stack(partials), axis=(1, 2)), leaf)
        curvature = sums[0:1]
        if norm_now is None:
            norm_now = sums[1:2]
        step_size = norm_now / curvature
        weights = weights + step_size * direction
        residual = residual - step_size * image_vec
        if iteration + 1 < ITERS:
            cross, image_square = sums[-2:-1], sums[-1:]
            norm_next = norm_now - 2.0 * step_size * cross + step_size * step_size * image_square
            direction = residual + (norm_next / norm_now) * direction
            norm_now = norm_next
    return (weights, residual)


def solution(mesh):
    placed = (
        P("box", None),
        P("box", None),
        P("box", "rep", None, None),
        P("box", "rep"),
        P("box", None, None),
        P("box", None, None),
        P("box"),
        P("box", "rep", None, None),
        P("box", "rep"),
    )
    return jax.shard_map(
        local,
        mesh=mesh,
        in_specs=placed,
        out_specs=(P("box", None), P("box", None)),
        check_vma=False,
    )
```

```python
import jax
import jax.numpy as jnp
from jax import lax
from jax.sharding import PartitionSpec as P

ITERS = 2


def rep_sum(vector):
    count = lax.axis_size("rep")
    if count == 4:
        got = [
            lax.ppermute(vector, "rep", [(i, i ^ mask) for i in range(count)])
            for mask in (1, 2, 3)
        ]
        return (vector + got[0]) + (got[1] + got[2])
    if count & (count - 1) == 0:
        stride = 1
        while stride < count:
            pairs = [(i, i ^ stride) for i in range(count)]
            vector = vector + lax.ppermute(vector, "rep", pairs)
            stride *= 2
        return vector
    me = lax.axis_index("rep")
    pieces = [vector]
    for shift in range(1, count):
        pairs = [(i, (i + shift) % count) for i in range(count)]
        pieces.append(lax.ppermute(vector, "rep", pairs))
    ordered = jnp.stack(pieces)[(me - jnp.arange(count)) % count]
    return jnp.sum(ordered, axis=0)


def box_sum(values, width):
    count = lax.axis_size("box")
    sent = jnp.broadcast_to(values[None, :], (count, values.shape[0]))
    got = lax.all_to_all(sent, "box", 0, 0, tiled=True)
    wide = lax.optimization_barrier(jnp.broadcast_to(got[:, :, None], got.shape + (width,)))
    return jnp.sum(wide, axis=0)


def local(
    targets,
    noise_var,
    near_tiles,
    near_partners,
    leaf_bases,
    transfer,
    parents,
    coupling,
    coupling_partners,
):
    box_count, leaf = targets.shape
    node_count = coupling.shape[0]
    group_count = node_count - box_count
    rank_width = coupling.shape[2]
    box_devices = lax.axis_size("box")
    box_rank = lax.axis_index("box")
    all_nodes = box_devices * node_count
    near_valid = near_partners >= 0
    near_local = jnp.where(near_valid, near_partners - box_rank * box_count, 0)
    near_onehot = (
        (jnp.arange(2 * box_count, dtype=jnp.int32)[:, None] == near_local.reshape(1, -1))
        & near_valid.reshape(1, -1)
    ).astype(jnp.float32)
    parent_local = parents - box_rank * group_count
    parent_onehot = (
        jnp.arange(group_count, dtype=jnp.int32)[:, None] == parent_local[None, :]
    ).astype(jnp.float32)
    far_valid = coupling_partners >= 0
    far_index = jnp.where(far_valid, coupling_partners, 0)
    far_pick = (
        (jnp.arange(all_nodes, dtype=jnp.int32)[:, None] == far_index.reshape(1, -1))
        & far_valid.reshape(1, -1)
    )
    bf_zero = jnp.zeros((), jnp.bfloat16)
    devices = jnp.arange(box_devices, dtype=jnp.int32)
    below = (devices < box_rank)[:, None, None]
    above = (devices > box_rank)[:, None, None]
    near_size = box_count * leaf
    far_size = node_count * rank_width

    weights = jnp.zeros_like(targets)
    residual = targets
    direction = targets
    norm_now = None
    for iteration in range(ITERS):
        rounded = direction.astype(jnp.bfloat16)
        mirrored = jnp.einsum(
            "bsij,bi->bsj", near_tiles, rounded, preferred_element_type=jnp.float32
        )
        landed = jnp.dot(
            near_onehot, mirrored.reshape(-1, mirrored.shape[2]), precision=lax.Precision.HIGHEST
        )
        leaf_coef = jnp.einsum(
            "brl,bl->br", leaf_bases, rounded, preferred_element_type=jnp.float32
        ).astype(jnp.bfloat16)
        upward = jnp.einsum("brq,br->bq", transfer, leaf_coef, preferred_element_type=jnp.float32)
        group_coef = jnp.dot(parent_onehot, upward, precision=lax.Precision.HIGHEST).astype(
            jnp.bfloat16
        )
        node_coef = jnp.concatenate([leaf_coef, group_coef], axis=0)
        far_mirror = jnp.einsum(
            "nsab,na->nsb", coupling, node_coef, preferred_element_type=jnp.float32
        )
        far_mirror = far_mirror * far_valid[:, :, None].astype(jnp.float32)
        spread = jnp.dot(
            far_pick.astype(jnp.float32), far_mirror.reshape(-1, rank_width),
            precision=lax.Precision.HIGHEST,
        ).reshape(box_devices, node_count, rank_width)
        following = lax.ppermute(
            rounded, "box", [(i, i - 1) for i in range(1, box_devices)]
        )
        arrived = lax.ppermute(
            landed[box_count:], "box", [(i, i + 1) for i in range(box_devices - 1)]
        )
        coef_wide = node_coef.astype(jnp.float32)
        far_send = jnp.where(below, coef_wide[None], spread)
        got_far = lax.all_to_all(far_send, "box", 0, 0, tiled=True)
        mirror_in = jnp.sum(jnp.where(below, got_far, 0.0), axis=0)
        every_coef = jnp.where(
            above, got_far, jnp.where(devices[:, None, None] == box_rank, coef_wide[None], 0.0)
        ).astype(jnp.bfloat16).reshape(all_nodes, rank_width)

        extended = jnp.concatenate([rounded, following], axis=0)
        near_in = jnp.where(near_valid[:, :, None], extended[near_local], bf_zero)
        forward = jnp.einsum(
            "bsij,bsj->bi", near_tiles, near_in, preferred_element_type=jnp.float32
        )
        near_part = forward + landed[:box_count] + arrived
        partner_coef = jnp.dot(
            far_pick.T.astype(jnp.bfloat16), every_coef, preferred_element_type=jnp.float32
        ).astype(jnp.bfloat16).reshape(node_count, -1, rank_width)
        far_forward = jnp.einsum(
            "nsab,nsb->na", coupling, partner_coef, preferred_element_type=jnp.float32
        )
        far_part = far_forward + spread[box_rank] + mirror_in
        both = rep_sum(jnp.concatenate([near_part.reshape(-1), far_part.reshape(-1)]))
        near_total = both[:near_size].reshape(box_count, leaf)
        far_total = both[near_size:].reshape(node_count, rank_width)
        group_out = far_total[box_count:].astype(jnp.bfloat16)
        parent_pick = jnp.zeros((box_count, rank_width), jnp.bfloat16)
        for group in range(group_count):
            parent_pick = jnp.where((parent_local == group)[:, None], group_out[group][None], parent_pick)
        from_parent = jnp.einsum(
            "brq,bq->br", transfer, parent_pick, preferred_element_type=jnp.float32
        )
        downward = (far_total[:box_count] + from_parent).astype(jnp.bfloat16)
        far_field = jnp.einsum(
            "brl,br->bl", leaf_bases, downward, preferred_element_type=jnp.float32
        )
        image_vec = noise_var * direction + near_total + far_field
        partials = [direction * image_vec]
        if norm_now is None:
            partials.append(targets * targets)
        if iteration + 1 < ITERS:
            partials += [residual * image_vec, image_vec * image_vec]
        sums = box_sum(jnp.sum(jnp.stack(partials), axis=(1, 2)), leaf)
        curvature = sums[0:1]
        if norm_now is None:
            norm_now = sums[1:2]
        step_size = norm_now / curvature
        weights = weights + step_size * direction
        residual = residual - step_size * image_vec
        if iteration + 1 < ITERS:
            cross, image_square = sums[-2:-1], sums[-1:]
            norm_next = norm_now - 2.0 * step_size * cross + step_size * step_size * image_square
            direction = residual + (norm_next / norm_now) * direction
            norm_now = norm_next
    return (weights, residual)


def solution(mesh):
    placed = (
        P("box", None),
        P("box", None),
        P("box", "rep", None, None),
        P("box", "rep"),
        P("box", None, None),
        P("box", None, None),
        P("box"),
        P("box", "rep", None, None),
        P("box", "rep"),
    )
    return jax.shard_map(
        local,
        mesh=mesh,
        in_specs=placed,
        out_specs=(P("box", None), P("box", None)),
        check_vma=False,
    )
```

```python
import jax
import jax.numpy as jnp
from jax import lax
from jax.sharding import PartitionSpec as P

ITERS = 2


def rep_sum(vector):
    count = lax.axis_size("rep")
    if count == 4:
        got = [
            lax.ppermute(vector, "rep", [(i, i ^ mask) for i in range(count)])
            for mask in (1, 2, 3)
        ]
        return (vector + got[0]) + (got[1] + got[2])
    if count & (count - 1) == 0:
        stride = 1
        while stride < count:
            pairs = [(i, i ^ stride) for i in range(count)]
            vector = vector + lax.ppermute(vector, "rep", pairs)
            stride *= 2
        return vector
    me = lax.axis_index("rep")
    pieces = [vector]
    for shift in range(1, count):
        pairs = [(i, (i + shift) % count) for i in range(count)]
        pieces.append(lax.ppermute(vector, "rep", pairs))
    ordered = jnp.stack(pieces)[(me - jnp.arange(count)) % count]
    return jnp.sum(ordered, axis=0)


def box_sum(values, width):
    count = lax.axis_size("box")
    sent = jnp.broadcast_to(values[None, :], (count, values.shape[0]))
    got = lax.all_to_all(sent, "box", 0, 0, tiled=True)
    wide = lax.optimization_barrier(jnp.broadcast_to(got[:, :, None], got.shape + (width,)))
    return jnp.sum(wide, axis=0)


def local(
    targets,
    noise_var,
    near_tiles,
    near_partners,
    leaf_bases,
    transfer,
    parents,
    coupling,
    coupling_partners,
):
    box_count, leaf = targets.shape
    node_count = coupling.shape[0]
    group_count = node_count - box_count
    rank_width = coupling.shape[2]
    box_devices = lax.axis_size("box")
    box_rank = lax.axis_index("box")
    all_nodes = box_devices * node_count
    near_valid = near_partners >= 0
    near_local = jnp.where(near_valid, near_partners - box_rank * box_count, 0)
    near_onehot = (
        (jnp.arange(2 * box_count, dtype=jnp.int32)[:, None] == near_local.reshape(1, -1))
        & near_valid.reshape(1, -1)
    ).astype(jnp.float32)
    parent_local = parents - box_rank * group_count
    parent_onehot = (
        jnp.arange(group_count, dtype=jnp.int32)[:, None] == parent_local[None, :]
    ).astype(jnp.float32)
    far_valid = coupling_partners >= 0
    far_index = jnp.where(far_valid, coupling_partners, 0)
    far_pick = (
        (jnp.arange(all_nodes, dtype=jnp.int32)[:, None] == far_index.reshape(1, -1))
        & far_valid.reshape(1, -1)
    )
    bf_zero = jnp.zeros((), jnp.bfloat16)
    devices = jnp.arange(box_devices, dtype=jnp.int32)
    below = (devices < box_rank)[:, None, None]
    above = (devices > box_rank)[:, None, None]
    near_size = box_count * leaf
    far_size = node_count * rank_width

    weights = jnp.zeros_like(targets)
    residual = targets
    direction = targets
    norm_now = None
    for iteration in range(ITERS):
        rounded = direction.astype(jnp.bfloat16)
        mirrored = jnp.einsum(
            "bsij,bi->bsj", near_tiles, rounded, preferred_element_type=jnp.float32
        )
        landed = jnp.dot(
            near_onehot, mirrored.reshape(-1, mirrored.shape[2]), precision=lax.Precision.HIGHEST
        )
        leaf_coef = jnp.einsum(
            "brl,bl->br", leaf_bases, rounded, preferred_element_type=jnp.float32
        ).astype(jnp.bfloat16)
        upward = jnp.einsum("brq,br->bq", transfer, leaf_coef, preferred_element_type=jnp.float32)
        group_coef = jnp.dot(parent_onehot, upward, precision=lax.Precision.HIGHEST).astype(
            jnp.bfloat16
        )
        node_coef = jnp.concatenate([leaf_coef, group_coef], axis=0)
        far_mirror = jnp.einsum(
            "nsab,na->nsb", coupling, node_coef, preferred_element_type=jnp.float32
        )
        far_mirror = far_mirror * far_valid[:, :, None].astype(jnp.float32)
        spread = jnp.dot(
            far_pick.astype(jnp.float32), far_mirror.reshape(-1, rank_width),
            precision=lax.Precision.HIGHEST,
        ).reshape(box_devices, node_count, rank_width)
        following = lax.ppermute(
            rounded, "box", [(i, i - 1) for i in range(1, box_devices)]
        )
        coef_wide = node_coef.astype(jnp.float32)
        far_send = jnp.where(below, coef_wide[None], spread)
        got_far = lax.all_to_all(far_send, "box", 0, 0, tiled=True)
        landed_next, got_far = lax.optimization_barrier((landed[box_count:], got_far))
        arrived = lax.ppermute(
            landed_next, "box", [(i, i + 1) for i in range(box_devices - 1)]
        )
        mirror_in = jnp.sum(jnp.where(below, got_far, 0.0), axis=0)
        every_coef = jnp.where(
            above, got_far, jnp.where(devices[:, None, None] == box_rank, coef_wide[None], 0.0)
        ).astype(jnp.bfloat16).reshape(all_nodes, rank_width)

        extended = jnp.concatenate([rounded, following], axis=0)
        near_in = jnp.where(near_valid[:, :, None], extended[near_local], bf_zero)
        forward = jnp.einsum(
            "bsij,bsj->bi", near_tiles, near_in, preferred_element_type=jnp.float32
        )
        near_part = forward + landed[:box_count] + arrived
        partner_coef = jnp.dot(
            far_pick.T.astype(jnp.bfloat16), every_coef, preferred_element_type=jnp.float32
        ).astype(jnp.bfloat16).reshape(node_count, -1, rank_width)
        far_forward = jnp.einsum(
            "nsab,nsb->na", coupling, partner_coef, preferred_element_type=jnp.float32
        )
        far_part = far_forward + spread[box_rank] + mirror_in
        both = rep_sum(jnp.concatenate([near_part.reshape(-1), far_part.reshape(-1)]))
        near_total = both[:near_size].reshape(box_count, leaf)
        far_total = both[near_size:].reshape(node_count, rank_width)
        group_out = far_total[box_count:].astype(jnp.bfloat16)
        parent_pick = jnp.zeros((box_count, rank_width), jnp.bfloat16)
        for group in range(group_count):
            parent_pick = jnp.where((parent_local == group)[:, None], group_out[group][None], parent_pick)
        from_parent = jnp.einsum(
            "brq,bq->br", transfer, parent_pick, preferred_element_type=jnp.float32
        )
        downward = (far_total[:box_count] + from_parent).astype(jnp.bfloat16)
        far_field = jnp.einsum(
            "brl,br->bl", leaf_bases, downward, preferred_element_type=jnp.float32
        )
        image_vec = noise_var * direction + near_total + far_field
        partials = [direction * image_vec]
        if norm_now is None:
            partials.append(targets * targets)
        if iteration + 1 < ITERS:
            partials += [residual * image_vec, image_vec * image_vec]
        sums = box_sum(jnp.sum(jnp.stack(partials), axis=(1, 2)), leaf)
        curvature = sums[0:1]
        if norm_now is None:
            norm_now = sums[1:2]
        step_size = norm_now / curvature
        weights = weights + step_size * direction
        residual = residual - step_size * image_vec
        if iteration + 1 < ITERS:
            cross, image_square = sums[-2:-1], sums[-1:]
            norm_next = norm_now - 2.0 * step_size * cross + step_size * step_size * image_square
            direction = residual + (norm_next / norm_now) * direction
            norm_now = norm_next
    return (weights, residual)


def solution(mesh):
    placed = (
        P("box", None),
        P("box", None),
        P("box", "rep", None, None),
        P("box", "rep"),
        P("box", None, None),
        P("box", None, None),
        P("box"),
        P("box", "rep", None, None),
        P("box", "rep"),
    )
    return jax.shard_map(
        local,
        mesh=mesh,
        in_specs=placed,
        out_specs=(P("box", None), P("box", None)),
        check_vma=False,
    )
```

```python
import jax
import jax.numpy as jnp
from jax import lax
from jax.sharding import PartitionSpec as P

ITERS = 2


def rep_sum(vector):
    count = lax.axis_size("rep")
    if count == 4:
        got = [
            lax.ppermute(vector, "rep", [(i, i ^ mask) for i in range(count)])
            for mask in (1, 2, 3)
        ]
        return (vector + got[0]) + (got[1] + got[2])
    if count & (count - 1) == 0:
        stride = 1
        while stride < count:
            pairs = [(i, i ^ stride) for i in range(count)]
            vector = vector + lax.ppermute(vector, "rep", pairs)
            stride *= 2
        return vector
    me = lax.axis_index("rep")
    pieces = [vector]
    for shift in range(1, count):
        pairs = [(i, (i + shift) % count) for i in range(count)]
        pieces.append(lax.ppermute(vector, "rep", pairs))
    ordered = jnp.stack(pieces)[(me - jnp.arange(count)) % count]
    return jnp.sum(ordered, axis=0)


def box_sum(values, width):
    count = lax.axis_size("box")
    sent = jnp.broadcast_to(values[None, :], (count, values.shape[0]))
    got = lax.all_to_all(sent, "box", 0, 0, tiled=True)
    wide = lax.optimization_barrier(jnp.broadcast_to(got[:, :, None], got.shape + (width,)))
    return jnp.sum(wide, axis=0)


def local(
    targets,
    noise_var,
    near_tiles,
    near_partners,
    leaf_bases,
    transfer,
    parents,
    coupling,
    coupling_partners,
):
    box_count, leaf = targets.shape
    node_count = coupling.shape[0]
    group_count = node_count - box_count
    rank_width = coupling.shape[2]
    box_devices = lax.axis_size("box")
    box_rank = lax.axis_index("box")
    all_nodes = box_devices * node_count
    near_valid = near_partners >= 0
    near_local = jnp.where(near_valid, near_partners - box_rank * box_count, 0)
    near_onehot = (
        (jnp.arange(2 * box_count, dtype=jnp.int32)[:, None] == near_local.reshape(1, -1))
        & near_valid.reshape(1, -1)
    ).astype(jnp.float32)
    parent_local = parents - box_rank * group_count
    parent_onehot = (
        jnp.arange(group_count, dtype=jnp.int32)[:, None] == parent_local[None, :]
    ).astype(jnp.float32)
    far_valid = coupling_partners >= 0
    far_index = jnp.where(far_valid, coupling_partners, 0)
    far_pick = (
        (jnp.arange(all_nodes, dtype=jnp.int32)[:, None] == far_index.reshape(1, -1))
        & far_valid.reshape(1, -1)
    )
    bf_zero = jnp.zeros((), jnp.bfloat16)
    devices = jnp.arange(box_devices, dtype=jnp.int32)
    below = (devices < box_rank)[:, None, None]
    above = (devices > box_rank)[:, None, None]
    near_size = box_count * leaf
    far_size = node_count * rank_width

    weights = jnp.zeros_like(targets)
    residual = targets
    direction = targets
    norm_now = None
    for iteration in range(ITERS):
        rounded = direction.astype(jnp.bfloat16)
        mirrored = jnp.einsum(
            "bsij,bi->bsj", near_tiles, rounded, preferred_element_type=jnp.float32
        )
        landed = jnp.dot(
            near_onehot, mirrored.reshape(-1, mirrored.shape[2]), precision=lax.Precision.HIGHEST
        )
        leaf_coef = jnp.einsum(
            "brl,bl->br", leaf_bases, rounded, preferred_element_type=jnp.float32
        ).astype(jnp.bfloat16)
        upward = jnp.einsum("brq,br->bq", transfer, leaf_coef, preferred_element_type=jnp.float32)
        group_coef = jnp.dot(parent_onehot, upward, precision=lax.Precision.HIGHEST).astype(
            jnp.bfloat16
        )
        node_coef = jnp.concatenate([leaf_coef, group_coef], axis=0)
        far_mirror = jnp.einsum(
            "nsab,na->nsb", coupling, node_coef, preferred_element_type=jnp.float32
        )
        far_mirror = far_mirror * far_valid[:, :, None].astype(jnp.float32)
        spread = jnp.dot(
            far_pick.astype(jnp.float32), far_mirror.reshape(-1, rank_width),
            precision=lax.Precision.HIGHEST,
        ).reshape(box_devices, node_count, rank_width)
        following = lax.ppermute(
            rounded, "box", [(i, i - 1) for i in range(1, box_devices)]
        )
        coef_wide = node_coef.astype(jnp.float32)
        far_send = jnp.where(below, coef_wide[None], spread)
        is_next = (devices == box_rank + 1)[:, None]
        near_send = jnp.where(is_next, landed[box_count:].reshape(1, -1), 0.0)
        got = lax.all_to_all(
            jnp.concatenate([far_send.reshape(box_devices, far_size), near_send], axis=1),
            "box", 0, 0, tiled=True,
        )
        got_far = got[:, :far_size].reshape(box_devices, node_count, rank_width)
        is_prev = (devices == box_rank - 1)[:, None]
        arrived = jnp.sum(jnp.where(is_prev, got[:, far_size:], 0.0), axis=0).reshape(box_count, leaf)
        mirror_in = jnp.sum(jnp.where(below, got_far, 0.0), axis=0)
        every_coef = jnp.where(
            above, got_far, jnp.where(devices[:, None, None] == box_rank, coef_wide[None], 0.0)
        ).astype(jnp.bfloat16).reshape(all_nodes, rank_width)

        extended = jnp.concatenate([rounded, following], axis=0)
        near_in = jnp.where(near_valid[:, :, None], extended[near_local], bf_zero)
        forward = jnp.einsum(
            "bsij,bsj->bi", near_tiles, near_in, preferred_element_type=jnp.float32
        )
        near_part = forward + landed[:box_count] + arrived
        partner_coef = jnp.dot(
            far_pick.T.astype(jnp.bfloat16), every_coef, preferred_element_type=jnp.float32
        ).astype(jnp.bfloat16).reshape(node_count, -1, rank_width)
        far_forward = jnp.einsum(
            "nsab,nsb->na", coupling, partner_coef, preferred_element_type=jnp.float32
        )
        far_part = far_forward + spread[box_rank] + mirror_in
        both = rep_sum(jnp.concatenate([near_part.reshape(-1), far_part.reshape(-1)]))
        near_total = both[:near_size].reshape(box_count, leaf)
        far_total = both[near_size:].reshape(node_count, rank_width)
        group_out = far_total[box_count:].astype(jnp.bfloat16)
        parent_pick = jnp.zeros((box_count, rank_width), jnp.bfloat16)
        for group in range(group_count):
            parent_pick = jnp.where((parent_local == group)[:, None], group_out[group][None], parent_pick)
        from_parent = jnp.einsum(
            "brq,bq->br", transfer, parent_pick, preferred_element_type=jnp.float32
        )
        downward = (far_total[:box_count] + from_parent).astype(jnp.bfloat16)
        far_field = jnp.einsum(
            "brl,br->bl", leaf_bases, downward, preferred_element_type=jnp.float32
        )
        image_vec = noise_var * direction + near_total + far_field
        partials = [direction * image_vec]
        if norm_now is None:
            partials.append(targets * targets)
        if iteration + 1 < ITERS:
            partials += [residual * image_vec, image_vec * image_vec]
        sums = box_sum(jnp.sum(jnp.stack(partials), axis=(1, 2)), leaf)
        curvature = sums[0:1]
        if norm_now is None:
            norm_now = sums[1:2]
        step_size = norm_now / curvature
        weights = weights + step_size * direction
        residual = residual - step_size * image_vec
        if iteration + 1 < ITERS:
            cross, image_square = sums[-2:-1], sums[-1:]
            norm_next = norm_now - 2.0 * step_size * cross + step_size * step_size * image_square
            direction = residual + (norm_next / norm_now) * direction
            norm_now = norm_next
    return (weights, residual)


def solution(mesh):
    placed = (
        P("box", None),
        P("box", None),
        P("box", "rep", None, None),
        P("box", "rep"),
        P("box", None, None),
        P("box", None, None),
        P("box"),
        P("box", "rep", None, None),
        P("box", "rep"),
    )
    return jax.shard_map(
        local,
        mesh=mesh,
        in_specs=placed,
        out_specs=(P("box", None), P("box", None)),
        check_vma=False,
    )
```

```python
import jax
import jax.numpy as jnp
from jax import lax
from jax.experimental import pallas as pl
from jax.sharding import PartitionSpec as P

ITERS = 2


def _mirror_kernel(tiles_ref, column_ref, out_ref):
    for b in range(tiles_ref.shape[0]):
        column = column_ref[b]
        for s in range(tiles_ref.shape[1]):
            tile = tiles_ref[b, s].astype(jnp.float32)
            out_ref[b, s:s + 1, :] = jnp.sum(tile * column, axis=0, keepdims=True)


def near_mirror(tiles, rounded):
    boxes, slots, leaf, _ = tiles.shape
    per_step = 4 if boxes % 4 == 0 else 1
    column = rounded.astype(jnp.float32)[:, :, None]
    return pl.pallas_call(
        _mirror_kernel,
        grid=(boxes // per_step,),
        in_specs=[
            pl.BlockSpec((per_step, slots, leaf, leaf), lambda i: (i, 0, 0, 0)),
            pl.BlockSpec((per_step, leaf, 1), lambda i: (i, 0, 0)),
        ],
        out_specs=pl.BlockSpec((per_step, slots, leaf), lambda i: (i, 0, 0)),
        out_shape=jax.ShapeDtypeStruct((boxes, slots, leaf), jnp.float32),
        cost_estimate=pl.CostEstimate(flops=2 * tiles.size, transcendentals=0,
                                      bytes_accessed=tiles.size * 2 + boxes * slots * leaf * 4),
    )(tiles, column)


def rep_sum(vector):
    count = lax.axis_size("rep")
    if count == 4:
        got = [
            lax.ppermute(vector, "rep", [(i, i ^ mask) for i in range(count)])
            for mask in (1, 2, 3)
        ]
        return (vector + got[0]) + (got[1] + got[2])
    if count & (count - 1) == 0:
        stride = 1
        while stride < count:
            pairs = [(i, i ^ stride) for i in range(count)]
            vector = vector + lax.ppermute(vector, "rep", pairs)
            stride *= 2
        return vector
    me = lax.axis_index("rep")
    pieces = [vector]
    for shift in range(1, count):
        pairs = [(i, (i + shift) % count) for i in range(count)]
        pieces.append(lax.ppermute(vector, "rep", pairs))
    ordered = jnp.stack(pieces)[(me - jnp.arange(count)) % count]
    return jnp.sum(ordered, axis=0)


def box_sum(values, width):
    count = lax.axis_size("box")
    sent = jnp.broadcast_to(values[None, :], (count, values.shape[0]))
    got = lax.all_to_all(sent, "box", 0, 0, tiled=True)
    wide = lax.optimization_barrier(jnp.broadcast_to(got[:, :, None], got.shape + (width,)))
    return jnp.sum(wide, axis=0)


def local(
    targets,
    noise_var,
    near_tiles,
    near_partners,
    leaf_bases,
    transfer,
    parents,
    coupling,
    coupling_partners,
):
    box_count, leaf = targets.shape
    node_count = coupling.shape[0]
    group_count = node_count - box_count
    rank_width = coupling.shape[2]
    box_devices = lax.axis_size("box")
    box_rank = lax.axis_index("box")
    all_nodes = box_devices * node_count
    near_valid = near_partners >= 0
    near_local = jnp.where(near_valid, near_partners - box_rank * box_count, 0)
    near_onehot = (
        (jnp.arange(2 * box_count, dtype=jnp.int32)[:, None] == near_local.reshape(1, -1))
        & near_valid.reshape(1, -1)
    ).astype(jnp.float32)
    parent_local = parents - box_rank * group_count
    parent_onehot = (
        jnp.arange(group_count, dtype=jnp.int32)[:, None] == parent_local[None, :]
    ).astype(jnp.float32)
    far_valid = coupling_partners >= 0
    far_index = jnp.where(far_valid, coupling_partners, 0)
    far_pick = (
        (jnp.arange(all_nodes, dtype=jnp.int32)[:, None] == far_index.reshape(1, -1))
        & far_valid.reshape(1, -1)
    )
    bf_zero = jnp.zeros((), jnp.bfloat16)
    devices = jnp.arange(box_devices, dtype=jnp.int32)
    below = (devices < box_rank)[:, None, None]
    above = (devices > box_rank)[:, None, None]
    near_size = box_count * leaf
    far_size = node_count * rank_width

    weights = jnp.zeros_like(targets)
    residual = targets
    direction = targets
    norm_now = None
    for iteration in range(ITERS):
        rounded = direction.astype(jnp.bfloat16)
        mirrored = near_mirror(near_tiles, rounded)
        landed = jnp.dot(
            near_onehot, mirrored.reshape(-1, mirrored.shape[2]), precision=lax.Precision.HIGHEST
        )
        leaf_coef = jnp.einsum(
            "brl,bl->br", leaf_bases, rounded, preferred_element_type=jnp.float32
        ).astype(jnp.bfloat16)
        upward = jnp.einsum("brq,br->bq", transfer, leaf_coef, preferred_element_type=jnp.float32)
        group_coef = jnp.dot(parent_onehot, upward, precision=lax.Precision.HIGHEST).astype(
            jnp.bfloat16
        )
        node_coef = jnp.concatenate([leaf_coef, group_coef], axis=0)
        far_mirror = jnp.einsum(
            "nsab,na->nsb", coupling, node_coef, preferred_element_type=jnp.float32
        )
        far_mirror = far_mirror * far_valid[:, :, None].astype(jnp.float32)
        spread = jnp.dot(
            far_pick.astype(jnp.float32), far_mirror.reshape(-1, rank_width),
            precision=lax.Precision.HIGHEST,
        ).reshape(box_devices, node_count, rank_width)
        following = lax.ppermute(
            rounded, "box", [(i, i - 1) for i in range(1, box_devices)]
        )
        coef_wide = node_coef.astype(jnp.float32)
        far_send = jnp.where(below, coef_wide[None], spread)
        is_next = (devices == box_rank + 1)[:, None]
        near_send = jnp.where(is_next, landed[box_count:].reshape(1, -1), 0.0)
        got = lax.all_to_all(
            jnp.concatenate([far_send.reshape(box_devices, far_size), near_send], axis=1),
            "box", 0, 0, tiled=True,
        )
        got_far = got[:, :far_size].reshape(box_devices, node_count, rank_width)
        is_prev = (devices == box_rank - 1)[:, None]
        arrived = jnp.sum(jnp.where(is_prev, got[:, far_size:], 0.0), axis=0).reshape(box_count, leaf)
        mirror_in = jnp.sum(jnp.where(below, got_far, 0.0), axis=0)
        every_coef = jnp.where(
            above, got_far, jnp.where(devices[:, None, None] == box_rank, coef_wide[None], 0.0)
        ).astype(jnp.bfloat16).reshape(all_nodes, rank_width)

        extended = jnp.concatenate([rounded, following], axis=0)
        near_in = jnp.where(near_valid[:, :, None], extended[near_local], bf_zero)
        forward = jnp.einsum(
            "bsij,bsj->bi", near_tiles, near_in, preferred_element_type=jnp.float32
        )
        near_part = forward + landed[:box_count] + arrived
        partner_coef = jnp.dot(
            far_pick.T.astype(jnp.bfloat16), every_coef, preferred_element_type=jnp.float32
        ).astype(jnp.bfloat16).reshape(node_count, -1, rank_width)
        far_forward = jnp.einsum(
            "nsab,nsb->na", coupling, partner_coef, preferred_element_type=jnp.float32
        )
        far_part = far_forward + spread[box_rank] + mirror_in
        both = rep_sum(jnp.concatenate([near_part.reshape(-1), far_part.reshape(-1)]))
        near_total = both[:near_size].reshape(box_count, leaf)
        far_total = both[near_size:].reshape(node_count, rank_width)
        group_out = far_total[box_count:].astype(jnp.bfloat16)
        parent_pick = jnp.zeros((box_count, rank_width), jnp.bfloat16)
        for group in range(group_count):
            parent_pick = jnp.where((parent_local == group)[:, None], group_out[group][None], parent_pick)
        from_parent = jnp.einsum(
            "brq,bq->br", transfer, parent_pick, preferred_element_type=jnp.float32
        )
        downward = (far_total[:box_count] + from_parent).astype(jnp.bfloat16)
        far_field = jnp.einsum(
            "brl,br->bl", leaf_bases, downward, preferred_element_type=jnp.float32
        )
        image_vec = noise_var * direction + near_total + far_field
        partials = [direction * image_vec]
        if norm_now is None:
            partials.append(targets * targets)
        if iteration + 1 < ITERS:
            partials += [residual * image_vec, image_vec * image_vec]
        sums = box_sum(jnp.sum(jnp.stack(partials), axis=(1, 2)), leaf)
        curvature = sums[0:1]
        if norm_now is None:
            norm_now = sums[1:2]
        step_size = norm_now / curvature
        weights = weights + step_size * direction
        residual = residual - step_size * image_vec
        if iteration + 1 < ITERS:
            cross, image_square = sums[-2:-1], sums[-1:]
            norm_next = norm_now - 2.0 * step_size * cross + step_size * step_size * image_square
            direction = residual + (norm_next / norm_now) * direction
            norm_now = norm_next
    return (weights, residual)


def solution(mesh):
    placed = (
        P("box", None),
        P("box", None),
        P("box", "rep", None, None),
        P("box", "rep"),
        P("box", None, None),
        P("box", None, None),
        P("box"),
        P("box", "rep", None, None),
        P("box", "rep"),
    )
    return jax.shard_map(
        local,
        mesh=mesh,
        in_specs=placed,
        out_specs=(P("box", None), P("box", None)),
        check_vma=False,
    )
```

```python
import jax
import jax.numpy as jnp
from jax import lax
from jax.sharding import PartitionSpec as P

ITERS = 2


def rep_sum(vector):
    count = lax.axis_size("rep")
    if count == 4:
        got = [
            lax.ppermute(vector, "rep", [(i, i ^ mask) for i in range(count)])
            for mask in (1, 2, 3)
        ]
        return (vector + got[0]) + (got[1] + got[2])
    if count & (count - 1) == 0:
        stride = 1
        while stride < count:
            pairs = [(i, i ^ stride) for i in range(count)]
            vector = vector + lax.ppermute(vector, "rep", pairs)
            stride *= 2
        return vector
    me = lax.axis_index("rep")
    pieces = [vector]
    for shift in range(1, count):
        pairs = [(i, (i + shift) % count) for i in range(count)]
        pieces.append(lax.ppermute(vector, "rep", pairs))
    ordered = jnp.stack(pieces)[(me - jnp.arange(count)) % count]
    return jnp.sum(ordered, axis=0)


def box_sum(values, width):
    count = lax.axis_size("box")
    sent = jnp.broadcast_to(values[None, :], (count, values.shape[0]))
    got = lax.all_to_all(sent, "box", 0, 0, tiled=True)
    wide = lax.optimization_barrier(jnp.broadcast_to(got[:, :, None], got.shape + (width,)))
    return jnp.sum(wide, axis=0)


def local(
    targets,
    noise_var,
    near_tiles,
    near_partners,
    leaf_bases,
    transfer,
    parents,
    coupling,
    coupling_partners,
):
    box_count, leaf = targets.shape
    node_count = coupling.shape[0]
    group_count = node_count - box_count
    rank_width = coupling.shape[2]
    box_devices = lax.axis_size("box")
    box_rank = lax.axis_index("box")
    all_nodes = box_devices * node_count
    near_valid = near_partners >= 0
    near_local = jnp.where(near_valid, near_partners - box_rank * box_count, 0)
    near_onehot = (
        (jnp.arange(2 * box_count, dtype=jnp.int32)[:, None] == near_local.reshape(1, -1))
        & near_valid.reshape(1, -1)
    ).astype(jnp.float32)
    parent_local = parents - box_rank * group_count
    parent_onehot = (
        jnp.arange(group_count, dtype=jnp.int32)[:, None] == parent_local[None, :]
    ).astype(jnp.float32)
    far_valid = coupling_partners >= 0
    far_index = jnp.where(far_valid, coupling_partners, 0)
    far_pick = (
        (jnp.arange(all_nodes, dtype=jnp.int32)[:, None] == far_index.reshape(1, -1))
        & far_valid.reshape(1, -1)
    )
    bf_zero = jnp.zeros((), jnp.bfloat16)
    devices = jnp.arange(box_devices, dtype=jnp.int32)
    below = (devices < box_rank)[:, None, None]
    above = (devices > box_rank)[:, None, None]
    near_size = box_count * leaf
    far_size = node_count * rank_width

    weights = jnp.zeros_like(targets)
    residual = targets
    direction = targets
    norm_now = None
    for iteration in range(ITERS):
        rounded = direction.astype(jnp.bfloat16)
        mirrored = jnp.einsum(
            "bsij,bi->bsj", near_tiles, rounded, preferred_element_type=jnp.float32
        )
        landed = jnp.dot(
            near_onehot, mirrored.reshape(-1, mirrored.shape[2]), precision=lax.Precision.HIGHEST
        )
        leaf_coef = jnp.einsum(
            "brl,bl->br", leaf_bases, rounded, preferred_element_type=jnp.float32
        ).astype(jnp.bfloat16)
        upward = jnp.einsum("brq,br->bq", transfer, leaf_coef, preferred_element_type=jnp.float32)
        group_coef = jnp.dot(parent_onehot, upward, precision=lax.Precision.HIGHEST).astype(
            jnp.bfloat16
        )
        node_coef = jnp.concatenate([leaf_coef, group_coef], axis=0)
        far_mirror = jnp.einsum(
            "nsab,na->nsb", coupling, node_coef, preferred_element_type=jnp.float32
        )
        far_mirror = far_mirror * far_valid[:, :, None].astype(jnp.float32)
        spread = jnp.dot(
            far_pick.astype(jnp.float32), far_mirror.reshape(-1, rank_width),
            precision=lax.Precision.HIGHEST,
        ).reshape(box_devices, node_count, rank_width)
        following = lax.ppermute(
            rounded, "box", [(i, i - 1) for i in range(1, box_devices)]
        )
        coef_wide = node_coef.astype(jnp.float32)
        far_send = jnp.where(below, coef_wide[None], spread)
        is_next = (devices == box_rank + 1)[:, None]
        near_send = jnp.where(is_next[:, None], landed[box_count:].reshape(1, 1, -1), 0.0)
        got = lax.all_to_all(
            jnp.concatenate([far_send.reshape(box_devices, 1, far_size), near_send], axis=2),
            "box", 0, 0, tiled=True,
        )
        got_far = got[:, 0, :far_size].reshape(box_devices, node_count, rank_width)
        is_prev = (devices == box_rank - 1)[:, None]
        arrived = jnp.sum(jnp.where(is_prev, got[:, 0, far_size:], 0.0), axis=0).reshape(box_count, leaf)
        mirror_in = jnp.sum(jnp.where(below, got_far, 0.0), axis=0)
        every_coef = jnp.where(
            above, got_far, jnp.where(devices[:, None, None] == box_rank, coef_wide[None], 0.0)
        ).astype(jnp.bfloat16).reshape(all_nodes, rank_width)

        extended = jnp.concatenate([rounded, following], axis=0)
        near_in = jnp.where(near_valid[:, :, None], extended[near_local], bf_zero)
        forward = jnp.einsum(
            "bsij,bsj->bi", near_tiles, near_in, preferred_element_type=jnp.float32
        )
        near_part = forward + landed[:box_count] + arrived
        partner_coef = jnp.dot(
            far_pick.T.astype(jnp.bfloat16), every_coef, preferred_element_type=jnp.float32
        ).astype(jnp.bfloat16).reshape(node_count, -1, rank_width)
        far_forward = jnp.einsum(
            "nsab,nsb->na", coupling, partner_coef, preferred_element_type=jnp.float32
        )
        far_part = far_forward + spread[box_rank] + mirror_in
        both = rep_sum(jnp.concatenate([near_part.reshape(-1), far_part.reshape(-1)]))
        near_total = both[:near_size].reshape(box_count, leaf)
        far_total = both[near_size:].reshape(node_count, rank_width)
        group_out = far_total[box_count:].astype(jnp.bfloat16)
        parent_pick = jnp.zeros((box_count, rank_width), jnp.bfloat16)
        for group in range(group_count):
            parent_pick = jnp.where((parent_local == group)[:, None], group_out[group][None], parent_pick)
        from_parent = jnp.einsum(
            "brq,bq->br", transfer, parent_pick, preferred_element_type=jnp.float32
        )
        downward = (far_total[:box_count] + from_parent).astype(jnp.bfloat16)
        far_field = jnp.einsum(
            "brl,br->bl", leaf_bases, downward, preferred_element_type=jnp.float32
        )
        image_vec = noise_var * direction + near_total + far_field
        partials = [direction * image_vec]
        if norm_now is None:
            partials.append(targets * targets)
        if iteration + 1 < ITERS:
            partials += [residual * image_vec, image_vec * image_vec]
        sums = box_sum(jnp.sum(jnp.stack(partials), axis=(1, 2)), leaf)
        curvature = sums[0:1]
        if norm_now is None:
            norm_now = sums[1:2]
        step_size = norm_now / curvature
        weights = weights + step_size * direction
        residual = residual - step_size * image_vec
        if iteration + 1 < ITERS:
            cross, image_square = sums[-2:-1], sums[-1:]
            norm_next = norm_now - 2.0 * step_size * cross + step_size * step_size * image_square
            direction = residual + (norm_next / norm_now) * direction
            norm_now = norm_next
    return (weights, residual)


def solution(mesh):
    placed = (
        P("box", None),
        P("box", None),
        P("box", "rep", None, None),
        P("box", "rep"),
        P("box", None, None),
        P("box", None, None),
        P("box"),
        P("box", "rep", None, None),
        P("box", "rep"),
    )
    return jax.shard_map(
        local,
        mesh=mesh,
        in_specs=placed,
        out_specs=(P("box", None), P("box", None)),
        check_vma=False,
    )
```

```python
import jax
import jax.numpy as jnp
from jax import lax
from jax.sharding import PartitionSpec as P

ITERS = 2


def rep_sum(vector):
    count = lax.axis_size("rep")
    if count == 4:
        got = [
            lax.ppermute(vector, "rep", [(i, i ^ mask) for i in range(count)])
            for mask in (1, 2, 3)
        ]
        return (vector + got[0]) + (got[1] + got[2])
    if count & (count - 1) == 0:
        stride = 1
        while stride < count:
            pairs = [(i, i ^ stride) for i in range(count)]
            vector = vector + lax.ppermute(vector, "rep", pairs)
            stride *= 2
        return vector
    me = lax.axis_index("rep")
    pieces = [vector]
    for shift in range(1, count):
        pairs = [(i, (i + shift) % count) for i in range(count)]
        pieces.append(lax.ppermute(vector, "rep", pairs))
    ordered = jnp.stack(pieces)[(me - jnp.arange(count)) % count]
    return jnp.sum(ordered, axis=0)


def box_sum(values, width):
    count = lax.axis_size("box")
    sent = jnp.broadcast_to(values[None, :], (count, values.shape[0]))
    got = lax.all_to_all(sent, "box", 0, 0, tiled=True)
    wide = lax.optimization_barrier(jnp.broadcast_to(got[:, :, None], got.shape + (width,)))
    return jnp.sum(wide, axis=0)


def local(
    targets,
    noise_var,
    near_tiles,
    near_partners,
    leaf_bases,
    transfer,
    parents,
    coupling,
    coupling_partners,
):
    box_count, leaf = targets.shape
    node_count = coupling.shape[0]
    group_count = node_count - box_count
    rank_width = coupling.shape[2]
    box_devices = lax.axis_size("box")
    box_rank = lax.axis_index("box")
    all_nodes = box_devices * node_count
    near_valid = near_partners >= 0
    near_local = jnp.where(near_valid, near_partners - box_rank * box_count, 0)
    near_onehot = (
        (jnp.arange(2 * box_count, dtype=jnp.int32)[:, None] == near_local.reshape(1, -1))
        & near_valid.reshape(1, -1)
    ).astype(jnp.float32)
    parent_local = parents - box_rank * group_count
    parent_onehot = (
        jnp.arange(group_count, dtype=jnp.int32)[:, None] == parent_local[None, :]
    ).astype(jnp.float32)
    far_valid = coupling_partners >= 0
    far_index = jnp.where(far_valid, coupling_partners, 0)
    far_pick = (
        (jnp.arange(all_nodes, dtype=jnp.int32)[:, None] == far_index.reshape(1, -1))
        & far_valid.reshape(1, -1)
    )
    bf_zero = jnp.zeros((), jnp.bfloat16)
    devices = jnp.arange(box_devices, dtype=jnp.int32)
    below = (devices < box_rank)[:, None, None]
    above = (devices > box_rank)[:, None, None]
    near_size = box_count * leaf
    far_size = node_count * rank_width

    weights = jnp.zeros_like(targets)
    residual = targets
    direction = targets
    norm_now = None
    for iteration in range(ITERS):
        rounded = direction.astype(jnp.bfloat16)
        following = lax.ppermute(
            rounded, "box", [(i, i - 1) for i in range(1, box_devices)]
        )
        mirror_field = rounded
        if iteration == 0:
            following, mirror_field = lax.optimization_barrier((following, rounded))
        mirrored = jnp.einsum(
            "bsij,bi->bsj", near_tiles, mirror_field, preferred_element_type=jnp.float32
        )
        landed = jnp.dot(
            near_onehot, mirrored.reshape(-1, mirrored.shape[2]), precision=lax.Precision.HIGHEST
        )
        leaf_coef = jnp.einsum(
            "brl,bl->br", leaf_bases, rounded, preferred_element_type=jnp.float32
        ).astype(jnp.bfloat16)
        upward = jnp.einsum("brq,br->bq", transfer, leaf_coef, preferred_element_type=jnp.float32)
        group_coef = jnp.dot(parent_onehot, upward, precision=lax.Precision.HIGHEST).astype(
            jnp.bfloat16
        )
        node_coef = jnp.concatenate([leaf_coef, group_coef], axis=0)
        far_mirror = jnp.einsum(
            "nsab,na->nsb", coupling, node_coef, preferred_element_type=jnp.float32
        )
        far_mirror = far_mirror * far_valid[:, :, None].astype(jnp.float32)
        spread = jnp.dot(
            far_pick.astype(jnp.float32), far_mirror.reshape(-1, rank_width),
            precision=lax.Precision.HIGHEST,
        ).reshape(box_devices, node_count, rank_width)
        coef_wide = node_coef.astype(jnp.float32)
        far_send = jnp.where(below, coef_wide[None], spread)
        is_next = (devices == box_rank + 1)[:, None]
        near_send = jnp.where(is_next[:, None], landed[box_count:].reshape(1, 1, -1), 0.0)
        got = lax.all_to_all(
            jnp.concatenate([far_send.reshape(box_devices, 1, far_size), near_send], axis=2),
            "box", 0, 0, tiled=True,
        )
        got_far = got[:, 0, :far_size].reshape(box_devices, node_count, rank_width)
        is_prev = (devices == box_rank - 1)[:, None]
        arrived = jnp.sum(jnp.where(is_prev, got[:, 0, far_size:], 0.0), axis=0).reshape(box_count, leaf)
        mirror_in = jnp.sum(jnp.where(below, got_far, 0.0), axis=0)
        every_coef = jnp.where(
            above, got_far, jnp.where(devices[:, None, None] == box_rank, coef_wide[None], 0.0)
        ).astype(jnp.bfloat16).reshape(all_nodes, rank_width)

        extended = jnp.concatenate([rounded, following], axis=0)
        near_in = jnp.where(near_valid[:, :, None], extended[near_local], bf_zero)
        forward = jnp.einsum(
            "bsij,bsj->bi", near_tiles, near_in, preferred_element_type=jnp.float32
        )
        near_part = forward + landed[:box_count] + arrived
        partner_coef = jnp.dot(
            far_pick.T.astype(jnp.bfloat16), every_coef, preferred_element_type=jnp.float32
        ).astype(jnp.bfloat16).reshape(node_count, -1, rank_width)
        far_forward = jnp.einsum(
            "nsab,nsb->na", coupling, partner_coef, preferred_element_type=jnp.float32
        )
        far_part = far_forward + spread[box_rank] + mirror_in
        both = rep_sum(jnp.concatenate([near_part.reshape(-1), far_part.reshape(-1)]))
        near_total = both[:near_size].reshape(box_count, leaf)
        far_total = both[near_size:].reshape(node_count, rank_width)
        group_out = far_total[box_count:].astype(jnp.bfloat16)
        parent_pick = jnp.zeros((box_count, rank_width), jnp.bfloat16)
        for group in range(group_count):
            parent_pick = jnp.where((parent_local == group)[:, None], group_out[group][None], parent_pick)
        from_parent = jnp.einsum(
            "brq,bq->br", transfer, parent_pick, preferred_element_type=jnp.float32
        )
        downward = (far_total[:box_count] + from_parent).astype(jnp.bfloat16)
        far_field = jnp.einsum(
            "brl,br->bl", leaf_bases, downward, preferred_element_type=jnp.float32
        )
        image_vec = noise_var * direction + near_total + far_field
        partials = [direction * image_vec]
        if norm_now is None:
            partials.append(targets * targets)
        if iteration + 1 < ITERS:
            partials += [residual * image_vec, image_vec * image_vec]
        sums = box_sum(jnp.sum(jnp.stack(partials), axis=(1, 2)), leaf)
        curvature = sums[0:1]
        if norm_now is None:
            norm_now = sums[1:2]
        step_size = norm_now / curvature
        weights = weights + step_size * direction
        residual = residual - step_size * image_vec
        if iteration + 1 < ITERS:
            cross, image_square = sums[-2:-1], sums[-1:]
            norm_next = norm_now - 2.0 * step_size * cross + step_size * step_size * image_square
            direction = residual + (norm_next / norm_now) * direction
            norm_now = norm_next
    return (weights, residual)


def solution(mesh):
    placed = (
        P("box", None),
        P("box", None),
        P("box", "rep", None, None),
        P("box", "rep"),
        P("box", None, None),
        P("box", None, None),
        P("box"),
        P("box", "rep", None, None),
        P("box", "rep"),
    )
    return jax.shard_map(
        local,
        mesh=mesh,
        in_specs=placed,
        out_specs=(P("box", None), P("box", None)),
        check_vma=False,
    )
```

```python
import jax
import jax.numpy as jnp
from jax import lax
from jax.sharding import PartitionSpec as P

ITERS = 2


def rep_sum(vector):
    count = lax.axis_size("rep")
    if count == 4:
        got = [
            lax.ppermute(vector, "rep", [(i, i ^ mask) for i in range(count)])
            for mask in (1, 2, 3)
        ]
        return (vector + got[0]) + (got[1] + got[2])
    if count & (count - 1) == 0:
        stride = 1
        while stride < count:
            pairs = [(i, i ^ stride) for i in range(count)]
            vector = vector + lax.ppermute(vector, "rep", pairs)
            stride *= 2
        return vector
    me = lax.axis_index("rep")
    pieces = [vector]
    for shift in range(1, count):
        pairs = [(i, (i + shift) % count) for i in range(count)]
        pieces.append(lax.ppermute(vector, "rep", pairs))
    ordered = jnp.stack(pieces)[(me - jnp.arange(count)) % count]
    return jnp.sum(ordered, axis=0)


def box_sum(values, width):
    count = lax.axis_size("box")
    sent = jnp.broadcast_to(values[None, :], (count, values.shape[0]))
    got = lax.all_to_all(sent, "box", 0, 0, tiled=True)
    wide = lax.optimization_barrier(jnp.broadcast_to(got[:, :, None], got.shape + (width,)))
    return jnp.sum(wide, axis=0)


def local(
    targets,
    noise_var,
    near_tiles,
    near_partners,
    leaf_bases,
    transfer,
    parents,
    coupling,
    coupling_partners,
):
    box_count, leaf = targets.shape
    node_count = coupling.shape[0]
    group_count = node_count - box_count
    rank_width = coupling.shape[2]
    box_devices = lax.axis_size("box")
    box_rank = lax.axis_index("box")
    all_nodes = box_devices * node_count
    near_valid = near_partners >= 0
    near_local = jnp.where(near_valid, near_partners - box_rank * box_count, 0)
    near_onehot = (
        (jnp.arange(2 * box_count, dtype=jnp.int32)[:, None] == near_local.reshape(1, -1))
        & near_valid.reshape(1, -1)
    ).astype(jnp.float32)
    parent_local = parents - box_rank * group_count
    parent_onehot = (
        jnp.arange(group_count, dtype=jnp.int32)[:, None] == parent_local[None, :]
    ).astype(jnp.float32)
    far_valid = coupling_partners >= 0
    far_index = jnp.where(far_valid, coupling_partners, 0)
    far_pick = (
        (jnp.arange(all_nodes, dtype=jnp.int32)[:, None] == far_index.reshape(1, -1))
        & far_valid.reshape(1, -1)
    )
    bf_zero = jnp.zeros((), jnp.bfloat16)
    devices = jnp.arange(box_devices, dtype=jnp.int32)
    below = (devices < box_rank)[:, None, None]
    above = (devices > box_rank)[:, None, None]
    near_size = box_count * leaf
    far_size = node_count * rank_width

    weights = jnp.zeros_like(targets)
    residual = targets
    direction = targets
    norm_now = None
    for iteration in range(ITERS):
        rounded = direction.astype(jnp.bfloat16)
        mirrored = jnp.einsum(
            "bsij,bi->bsj", near_tiles, rounded, preferred_element_type=jnp.float32
        )
        landed = jnp.dot(
            near_onehot, mirrored.reshape(-1, mirrored.shape[2]), precision=lax.Precision.HIGHEST
        )
        leaf_coef = jnp.einsum(
            "brl,bl->br", leaf_bases, rounded, preferred_element_type=jnp.float32
        ).astype(jnp.bfloat16)
        upward = jnp.einsum("brq,br->bq", transfer, leaf_coef, preferred_element_type=jnp.float32)
        group_coef = jnp.dot(parent_onehot, upward, precision=lax.Precision.HIGHEST).astype(
            jnp.bfloat16
        )
        node_coef = jnp.concatenate([leaf_coef, group_coef], axis=0)
        far_mirror = jnp.einsum(
            "nsab,na->nsb", coupling, node_coef, preferred_element_type=jnp.float32
        )
        far_mirror = far_mirror * far_valid[:, :, None].astype(jnp.float32)
        spread = jnp.dot(
            far_pick.astype(jnp.float32), far_mirror.reshape(-1, rank_width),
            precision=lax.Precision.HIGHEST,
        ).reshape(box_devices, node_count, rank_width)
        following = lax.ppermute(
            rounded, "box", [(i, i - 1) for i in range(1, box_devices)]
        )
        coef_wide = node_coef.astype(jnp.float32)
        far_send = jnp.where(below, coef_wide[None], spread)
        is_next = (devices == box_rank + 1)[:, None]
        near_send = jnp.where(is_next, landed[box_count:].reshape(1, -1), 0.0)
        got = lax.all_to_all(
            jnp.concatenate([far_send.reshape(box_devices, far_size), near_send], axis=1),
            "box", 0, 0, tiled=True,
        )
        got_far = got[:, :far_size].reshape(box_devices, node_count, rank_width)
        is_prev = (devices == box_rank - 1)[:, None]
        arrived = jnp.sum(jnp.where(is_prev, got[:, far_size:], 0.0), axis=0).reshape(box_count, leaf)
        mirror_in = jnp.sum(jnp.where(below, got_far, 0.0), axis=0)
        every_coef = jnp.where(
            above, got_far, jnp.where(devices[:, None, None] == box_rank, coef_wide[None], 0.0)
        ).astype(jnp.bfloat16).reshape(all_nodes, rank_width)

        extended = jnp.concatenate([rounded, following], axis=0)
        near_in = jnp.where(near_valid[:, :, None], extended[near_local], bf_zero)
        forward = jnp.einsum(
            "bsij,bsj->bi", near_tiles, near_in, preferred_element_type=jnp.float32
        )
        near_part = forward + landed[:box_count] + arrived
        partner_coef = jnp.dot(
            far_pick.T.astype(jnp.bfloat16), every_coef, preferred_element_type=jnp.float32
        ).astype(jnp.bfloat16).reshape(node_count, -1, rank_width)
        far_forward = jnp.einsum(
            "nsab,nsb->na", coupling, partner_coef, preferred_element_type=jnp.float32
        )
        far_part = far_forward + spread[box_rank] + mirror_in
        far_total = rep_sum(far_part)
        near_total = rep_sum(near_part)
        group_out = far_total[box_count:].astype(jnp.bfloat16)
        parent_pick = jnp.zeros((box_count, rank_width), jnp.bfloat16)
        for group in range(group_count):
            parent_pick = jnp.where((parent_local == group)[:, None], group_out[group][None], parent_pick)
        from_parent = jnp.einsum(
            "brq,bq->br", transfer, parent_pick, preferred_element_type=jnp.float32
        )
        downward = (far_total[:box_count] + from_parent).astype(jnp.bfloat16)
        far_field = jnp.einsum(
            "brl,br->bl", leaf_bases, downward, preferred_element_type=jnp.float32
        )
        image_vec = noise_var * direction + near_total + far_field
        partials = [direction * image_vec]
        if norm_now is None:
            partials.append(targets * targets)
        if iteration + 1 < ITERS:
            partials += [residual * image_vec, image_vec * image_vec]
        sums = box_sum(jnp.sum(jnp.stack(partials), axis=(1, 2)), leaf)
        curvature = sums[0:1]
        if norm_now is None:
            norm_now = sums[1:2]
        step_size = norm_now / curvature
        weights = weights + step_size * direction
        residual = residual - step_size * image_vec
        if iteration + 1 < ITERS:
            cross, image_square = sums[-2:-1], sums[-1:]
            norm_next = norm_now - 2.0 * step_size * cross + step_size * step_size * image_square
            direction = residual + (norm_next / norm_now) * direction
            norm_now = norm_next
    return (weights, residual)


def solution(mesh):
    placed = (
        P("box", None),
        P("box", None),
        P("box", "rep", None, None),
        P("box", "rep"),
        P("box", None, None),
        P("box", None, None),
        P("box"),
        P("box", "rep", None, None),
        P("box", "rep"),
    )
    return jax.shard_map(
        local,
        mesh=mesh,
        in_specs=placed,
        out_specs=(P("box", None), P("box", None)),
        check_vma=False,
    )
```

```python
import jax
import jax.numpy as jnp
from jax import lax
from jax.sharding import PartitionSpec as P

ITERS = 2


def rep_sum(vector):
    count = lax.axis_size("rep")
    if count == 4:
        got = [
            lax.ppermute(vector, "rep", [(i, i ^ mask) for i in range(count)])
            for mask in (1, 2, 3)
        ]
        return (vector + got[0]) + (got[1] + got[2])
    if count & (count - 1) == 0:
        stride = 1
        while stride < count:
            pairs = [(i, i ^ stride) for i in range(count)]
            vector = vector + lax.ppermute(vector, "rep", pairs)
            stride *= 2
        return vector
    me = lax.axis_index("rep")
    pieces = [vector]
    for shift in range(1, count):
        pairs = [(i, (i + shift) % count) for i in range(count)]
        pieces.append(lax.ppermute(vector, "rep", pairs))
    ordered = jnp.stack(pieces)[(me - jnp.arange(count)) % count]
    return jnp.sum(ordered, axis=0)


def box_sum(values, width):
    count = lax.axis_size("box")
    sent = jnp.broadcast_to(values[None, :], (count, values.shape[0]))
    got = lax.all_to_all(sent, "box", 0, 0, tiled=True)
    wide = lax.optimization_barrier(jnp.broadcast_to(got[:, :, None], got.shape + (width,)))
    return jnp.sum(wide, axis=0)


def local(
    targets,
    noise_var,
    near_tiles,
    near_partners,
    leaf_bases,
    transfer,
    parents,
    coupling,
    coupling_partners,
):
    box_count, leaf = targets.shape
    node_count = coupling.shape[0]
    group_count = node_count - box_count
    rank_width = coupling.shape[2]
    box_devices = lax.axis_size("box")
    box_rank = lax.axis_index("box")
    all_nodes = box_devices * node_count
    near_valid = near_partners >= 0
    near_local = jnp.where(near_valid, near_partners - box_rank * box_count, 0)
    near_onehot = (
        (jnp.arange(2 * box_count, dtype=jnp.int32)[:, None] == near_local.reshape(1, -1))
        & near_valid.reshape(1, -1)
    ).astype(jnp.float32)
    parent_local = parents - box_rank * group_count
    parent_onehot = (
        jnp.arange(group_count, dtype=jnp.int32)[:, None] == parent_local[None, :]
    ).astype(jnp.float32)
    far_valid = coupling_partners >= 0
    far_index = jnp.where(far_valid, coupling_partners, 0)
    far_pick = (
        (jnp.arange(all_nodes, dtype=jnp.int32)[:, None] == far_index.reshape(1, -1))
        & far_valid.reshape(1, -1)
    )
    bf_zero = jnp.zeros((), jnp.bfloat16)
    devices = jnp.arange(box_devices, dtype=jnp.int32)
    below = (devices < box_rank)[:, None, None]
    above = (devices > box_rank)[:, None, None]
    near_size = box_count * leaf
    far_size = node_count * rank_width

    weights = jnp.zeros_like(targets)
    residual = targets
    direction = targets
    norm_now = None
    for iteration in range(ITERS):
        rounded = direction.astype(jnp.bfloat16)
        mirrored = jnp.einsum(
            "bsij,bi->bsj", near_tiles, rounded, preferred_element_type=jnp.float32
        )
        landed = jnp.dot(
            near_onehot, mirrored.reshape(-1, mirrored.shape[2]), precision=lax.Precision.HIGHEST
        )
        leaf_coef = jnp.einsum(
            "brl,bl->br", leaf_bases, rounded, preferred_element_type=jnp.float32
        ).astype(jnp.bfloat16)
        upward = jnp.einsum("brq,br->bq", transfer, leaf_coef, preferred_element_type=jnp.float32)
        group_coef = jnp.dot(parent_onehot, upward, precision=lax.Precision.HIGHEST).astype(
            jnp.bfloat16
        )
        node_coef = jnp.concatenate([leaf_coef, group_coef], axis=0)
        far_mirror = jnp.einsum(
            "nsab,na->nsb", coupling, node_coef, preferred_element_type=jnp.float32
        )
        far_mirror = far_mirror * far_valid[:, :, None].astype(jnp.float32)
        spread = jnp.dot(
            far_pick.astype(jnp.float32), far_mirror.reshape(-1, rank_width),
            precision=lax.Precision.HIGHEST,
        ).reshape(box_devices, node_count, rank_width)
        following = lax.ppermute(
            rounded, "box", [(i, i - 1) for i in range(1, box_devices)]
        )
        coef_wide = node_coef.astype(jnp.float32)
        far_send = jnp.where(below, coef_wide[None], spread)
        is_next = (devices == box_rank + 1)[:, None]
        near_send = jnp.where(is_next, landed[box_count:].reshape(1, -1), 0.0)
        got = lax.all_to_all(
            jnp.concatenate([far_send.reshape(box_devices, far_size), near_send], axis=1),
            "box", 0, 0, tiled=True,
        )
        got_far = got[:, :far_size].reshape(box_devices, node_count, rank_width)
        is_prev = (devices == box_rank - 1)[:, None]
        arrived = jnp.sum(jnp.where(is_prev, got[:, far_size:], 0.0), axis=0).reshape(box_count, leaf)
        mirror_in = jnp.sum(jnp.where(below, got_far, 0.0), axis=0)
        every_coef = jnp.where(
            above, got_far, jnp.where(devices[:, None, None] == box_rank, coef_wide[None], 0.0)
        ).astype(jnp.bfloat16).reshape(all_nodes, rank_width)

        extended = jnp.concatenate([rounded, following], axis=0)
        near_in = jnp.dot(
            near_onehot.T.astype(jnp.bfloat16), extended, preferred_element_type=jnp.float32
        ).reshape(near_tiles.shape[0], near_tiles.shape[1], 1, leaf)
        forward = jnp.sum(near_tiles.astype(jnp.float32) * near_in, axis=(1, 3))
        near_part = forward + landed[:box_count] + arrived
        partner_coef = jnp.dot(
            far_pick.T.astype(jnp.bfloat16), every_coef, preferred_element_type=jnp.float32
        ).astype(jnp.bfloat16).reshape(node_count, -1, rank_width)
        far_forward = jnp.einsum(
            "nsab,nsb->na", coupling, partner_coef, preferred_element_type=jnp.float32
        )
        far_part = far_forward + spread[box_rank] + mirror_in
        both = rep_sum(jnp.concatenate([near_part.reshape(-1), far_part.reshape(-1)]))
        near_total = both[:near_size].reshape(box_count, leaf)
        far_total = both[near_size:].reshape(node_count, rank_width)
        group_out = far_total[box_count:].astype(jnp.bfloat16)
        parent_pick = jnp.zeros((box_count, rank_width), jnp.bfloat16)
        for group in range(group_count):
            parent_pick = jnp.where((parent_local == group)[:, None], group_out[group][None], parent_pick)
        from_parent = jnp.einsum(
            "brq,bq->br", transfer, parent_pick, preferred_element_type=jnp.float32
        )
        downward = (far_total[:box_count] + from_parent).astype(jnp.bfloat16)
        far_field = jnp.einsum(
            "brl,br->bl", leaf_bases, downward, preferred_element_type=jnp.float32
        )
        image_vec = noise_var * direction + near_total + far_field
        partials = [direction * image_vec]
        if norm_now is None:
            partials.append(targets * targets)
        if iteration + 1 < ITERS:
            partials += [residual * image_vec, image_vec * image_vec]
        sums = box_sum(jnp.sum(jnp.stack(partials), axis=(1, 2)), leaf)
        curvature = sums[0:1]
        if norm_now is None:
            norm_now = sums[1:2]
        step_size = norm_now / curvature
        weights = weights + step_size * direction
        residual = residual - step_size * image_vec
        if iteration + 1 < ITERS:
            cross, image_square = sums[-2:-1], sums[-1:]
            norm_next = norm_now - 2.0 * step_size * cross + step_size * step_size * image_square
            direction = residual + (norm_next / norm_now) * direction
            norm_now = norm_next
    return (weights, residual)


def solution(mesh):
    placed = (
        P("box", None),
        P("box", None),
        P("box", "rep", None, None),
        P("box", "rep"),
        P("box", None, None),
        P("box", None, None),
        P("box"),
        P("box", "rep", None, None),
        P("box", "rep"),
    )
    return jax.shard_map(
        local,
        mesh=mesh,
        in_specs=placed,
        out_specs=(P("box", None), P("box", None)),
        check_vma=False,
    )
```

```python
import jax
import jax.numpy as jnp
from jax import lax
from jax.sharding import PartitionSpec as P

ITERS = 2


def rep_sum(vector):
    count = lax.axis_size("rep")
    if count == 4:
        got = [
            lax.ppermute(vector, "rep", [(i, i ^ mask) for i in range(count)])
            for mask in (1, 2, 3)
        ]
        return (vector + got[0]) + (got[1] + got[2])
    if count & (count - 1) == 0:
        stride = 1
        while stride < count:
            pairs = [(i, i ^ stride) for i in range(count)]
            vector = vector + lax.ppermute(vector, "rep", pairs)
            stride *= 2
        return vector
    me = lax.axis_index("rep")
    pieces = [vector]
    for shift in range(1, count):
        pairs = [(i, (i + shift) % count) for i in range(count)]
        pieces.append(lax.ppermute(vector, "rep", pairs))
    ordered = jnp.stack(pieces)[(me - jnp.arange(count)) % count]
    return jnp.sum(ordered, axis=0)


def box_sum(values, width):
    count = lax.axis_size("box")
    sent = jnp.broadcast_to(values[None, :], (count, values.shape[0]))
    got = lax.all_to_all(sent, "box", 0, 0, tiled=True)
    wide = lax.optimization_barrier(jnp.broadcast_to(got[:, :, None], got.shape + (width,)))
    return jnp.sum(wide, axis=0)


def local(
    targets,
    noise_var,
    near_tiles,
    near_partners,
    leaf_bases,
    transfer,
    parents,
    coupling,
    coupling_partners,
):
    box_count, leaf = targets.shape
    node_count = coupling.shape[0]
    group_count = node_count - box_count
    rank_width = coupling.shape[2]
    box_devices = lax.axis_size("box")
    box_rank = lax.axis_index("box")
    all_nodes = box_devices * node_count
    near_valid = near_partners >= 0
    near_local = jnp.where(near_valid, near_partners - box_rank * box_count, 0)
    near_onehot = (
        (jnp.arange(2 * box_count, dtype=jnp.int32)[:, None] == near_local.reshape(1, -1))
        & near_valid.reshape(1, -1)
    ).astype(jnp.float32)
    parent_local = parents - box_rank * group_count
    parent_onehot = (
        jnp.arange(group_count, dtype=jnp.int32)[:, None] == parent_local[None, :]
    ).astype(jnp.float32)
    far_valid = coupling_partners >= 0
    far_index = jnp.where(far_valid, coupling_partners, 0)
    far_pick = (
        (jnp.arange(all_nodes, dtype=jnp.int32)[:, None] == far_index.reshape(1, -1))
        & far_valid.reshape(1, -1)
    )
    bf_zero = jnp.zeros((), jnp.bfloat16)
    devices = jnp.arange(box_devices, dtype=jnp.int32)
    below = (devices < box_rank)[:, None, None]
    above = (devices > box_rank)[:, None, None]
    near_size = box_count * leaf
    far_size = node_count * rank_width

    weights = jnp.zeros_like(targets)
    residual = targets
    direction = targets
    norm_now = None
    for iteration in range(ITERS):
        rounded = direction.astype(jnp.bfloat16)
        mirrored = jnp.einsum(
            "bsij,bi->bsj", near_tiles, rounded, preferred_element_type=jnp.float32
        )
        landed = jnp.dot(
            near_onehot, mirrored.reshape(-1, mirrored.shape[2]), precision=lax.Precision.HIGHEST
        )
        leaf_coef = jnp.sum(
            leaf_bases.astype(jnp.float32) * rounded.astype(jnp.float32)[:, None, :], axis=2
        ).astype(jnp.bfloat16)
        upward = jnp.einsum("brq,br->bq", transfer, leaf_coef, preferred_element_type=jnp.float32)
        group_coef = jnp.dot(parent_onehot, upward, precision=lax.Precision.HIGHEST).astype(
            jnp.bfloat16
        )
        node_coef = jnp.concatenate([leaf_coef, group_coef], axis=0)
        far_mirror = jnp.einsum(
            "nsab,na->nsb", coupling, node_coef, preferred_element_type=jnp.float32
        )
        far_mirror = far_mirror * far_valid[:, :, None].astype(jnp.float32)
        spread = jnp.dot(
            far_pick.astype(jnp.float32), far_mirror.reshape(-1, rank_width),
            precision=lax.Precision.HIGHEST,
        ).reshape(box_devices, node_count, rank_width)
        following = lax.ppermute(
            rounded, "box", [(i, i - 1) for i in range(1, box_devices)]
        )
        coef_wide = node_coef.astype(jnp.float32)
        far_send = jnp.where(below, coef_wide[None], spread)
        is_next = (devices == box_rank + 1)[:, None]
        near_send = jnp.where(is_next, landed[box_count:].reshape(1, -1), 0.0)
        got = lax.all_to_all(
            jnp.concatenate([far_send.reshape(box_devices, far_size), near_send], axis=1),
            "box", 0, 0, tiled=True,
        )
        got_far = got[:, :far_size].reshape(box_devices, node_count, rank_width)
        is_prev = (devices == box_rank - 1)[:, None]
        arrived = jnp.sum(jnp.where(is_prev, got[:, far_size:], 0.0), axis=0).reshape(box_count, leaf)
        mirror_in = jnp.sum(jnp.where(below, got_far, 0.0), axis=0)
        every_coef = jnp.where(
            above, got_far, jnp.where(devices[:, None, None] == box_rank, coef_wide[None], 0.0)
        ).astype(jnp.bfloat16).reshape(all_nodes, rank_width)

        extended = jnp.concatenate([rounded, following], axis=0)
        near_in = jnp.dot(
            near_onehot.T.astype(jnp.bfloat16), extended, preferred_element_type=jnp.float32
        ).reshape(near_tiles.shape[0], near_tiles.shape[1], 1, leaf)
        forward = jnp.sum(near_tiles.astype(jnp.float32) * near_in, axis=(1, 3))
        near_part = forward + landed[:box_count] + arrived
        partner_coef = jnp.dot(
            far_pick.T.astype(jnp.bfloat16), every_coef, preferred_element_type=jnp.float32
        ).astype(jnp.bfloat16).reshape(node_count, -1, rank_width)
        far_forward = jnp.einsum(
            "nsab,nsb->na", coupling, partner_coef, preferred_element_type=jnp.float32
        )
        far_part = far_forward + spread[box_rank] + mirror_in
        both = rep_sum(jnp.concatenate([near_part.reshape(-1), far_part.reshape(-1)]))
        near_total = both[:near_size].reshape(box_count, leaf)
        far_total = both[near_size:].reshape(node_count, rank_width)
        group_out = far_total[box_count:].astype(jnp.bfloat16)
        parent_pick = jnp.zeros((box_count, rank_width), jnp.bfloat16)
        for group in range(group_count):
            parent_pick = jnp.where((parent_local == group)[:, None], group_out[group][None], parent_pick)
        from_parent = jnp.einsum(
            "brq,bq->br", transfer, parent_pick, preferred_element_type=jnp.float32
        )
        downward = (far_total[:box_count] + from_parent).astype(jnp.bfloat16)
        far_field = jnp.einsum(
            "brl,br->bl", leaf_bases, downward, preferred_element_type=jnp.float32
        )
        image_vec = noise_var * direction + near_total + far_field
        partials = [direction * image_vec]
        if norm_now is None:
            partials.append(targets * targets)
        if iteration + 1 < ITERS:
            partials += [residual * image_vec, image_vec * image_vec]
        sums = box_sum(jnp.sum(jnp.stack(partials), axis=(1, 2)), leaf)
        curvature = sums[0:1]
        if norm_now is None:
            norm_now = sums[1:2]
        step_size = norm_now / curvature
        weights = weights + step_size * direction
        residual = residual - step_size * image_vec
        if iteration + 1 < ITERS:
            cross, image_square = sums[-2:-1], sums[-1:]
            norm_next = norm_now - 2.0 * step_size * cross + step_size * step_size * image_square
            direction = residual + (norm_next / norm_now) * direction
            norm_now = norm_next
    return (weights, residual)


def solution(mesh):
    placed = (
        P("box", None),
        P("box", None),
        P("box", "rep", None, None),
        P("box", "rep"),
        P("box", None, None),
        P("box", None, None),
        P("box"),
        P("box", "rep", None, None),
        P("box", "rep"),
    )
    return jax.shard_map(
        local,
        mesh=mesh,
        in_specs=placed,
        out_specs=(P("box", None), P("box", None)),
        check_vma=False,
    )
```

```python
import jax
import jax.numpy as jnp
from jax import lax
from jax.sharding import PartitionSpec as P

ITERS = 2


def rep_sum(vector):
    count = lax.axis_size("rep")
    if count == 4:
        got = [
            lax.ppermute(vector, "rep", [(i, i ^ mask) for i in range(count)])
            for mask in (1, 2, 3)
        ]
        return (vector + got[0]) + (got[1] + got[2])
    if count & (count - 1) == 0:
        stride = 1
        while stride < count:
            pairs = [(i, i ^ stride) for i in range(count)]
            vector = vector + lax.ppermute(vector, "rep", pairs)
            stride *= 2
        return vector
    me = lax.axis_index("rep")
    pieces = [vector]
    for shift in range(1, count):
        pairs = [(i, (i + shift) % count) for i in range(count)]
        pieces.append(lax.ppermute(vector, "rep", pairs))
    ordered = jnp.stack(pieces)[(me - jnp.arange(count)) % count]
    return jnp.sum(ordered, axis=0)


def box_sum(values, width):
    count = lax.axis_size("box")
    sent = jnp.broadcast_to(values[None, :], (count, values.shape[0]))
    got = lax.all_to_all(sent, "box", 0, 0, tiled=True)
    wide = lax.optimization_barrier(jnp.broadcast_to(got[:, :, None], got.shape + (width,)))
    return jnp.sum(wide, axis=0)


def local(
    targets,
    noise_var,
    near_tiles,
    near_partners,
    leaf_bases,
    transfer,
    parents,
    coupling,
    coupling_partners,
):
    box_count, leaf = targets.shape
    node_count = coupling.shape[0]
    group_count = node_count - box_count
    rank_width = coupling.shape[2]
    box_devices = lax.axis_size("box")
    box_rank = lax.axis_index("box")
    all_nodes = box_devices * node_count
    near_valid = near_partners >= 0
    near_local = jnp.where(near_valid, near_partners - box_rank * box_count, 0)
    near_onehot = (
        (jnp.arange(2 * box_count, dtype=jnp.int32)[:, None] == near_local.reshape(1, -1))
        & near_valid.reshape(1, -1)
    ).astype(jnp.float32)
    parent_local = parents - box_rank * group_count
    parent_onehot = (
        jnp.arange(group_count, dtype=jnp.int32)[:, None] == parent_local[None, :]
    ).astype(jnp.float32)
    far_valid = coupling_partners >= 0
    far_index = jnp.where(far_valid, coupling_partners, 0)
    far_pick = (
        (jnp.arange(all_nodes, dtype=jnp.int32)[:, None] == far_index.reshape(1, -1))
        & far_valid.reshape(1, -1)
    )
    bf_zero = jnp.zeros((), jnp.bfloat16)
    devices = jnp.arange(box_devices, dtype=jnp.int32)
    below = (devices < box_rank)[:, None, None]
    above = (devices > box_rank)[:, None, None]
    near_size = box_count * leaf
    far_size = node_count * rank_width

    weights = jnp.zeros_like(targets)
    residual = targets
    direction = targets
    norm_now = None
    for iteration in range(ITERS):
        rounded = direction.astype(jnp.bfloat16)
        mirrored = jnp.einsum(
            "bsij,bi->bsj", near_tiles, rounded, preferred_element_type=jnp.float32
        )
        landed = jnp.dot(
            near_onehot, mirrored.reshape(-1, mirrored.shape[2]), precision=lax.Precision.HIGHEST
        )
        leaf_coef = jnp.sum(
            leaf_bases.astype(jnp.float32) * rounded.astype(jnp.float32)[:, None, :], axis=2
        ).astype(jnp.bfloat16)
        upward = jnp.einsum("brq,br->bq", transfer, leaf_coef, preferred_element_type=jnp.float32)
        group_coef = jnp.dot(parent_onehot, upward, precision=lax.Precision.HIGHEST).astype(
            jnp.bfloat16
        )
        node_coef = jnp.concatenate([leaf_coef, group_coef], axis=0)
        far_mirror = jnp.einsum(
            "nsab,na->nsb", coupling, node_coef, preferred_element_type=jnp.float32
        )
        far_mirror = far_mirror * far_valid[:, :, None].astype(jnp.float32)
        spread = jnp.dot(
            far_pick.astype(jnp.float32), far_mirror.reshape(-1, rank_width),
            precision=lax.Precision.HIGHEST,
        ).reshape(box_devices, node_count, rank_width)
        following = lax.ppermute(
            rounded, "box", [(i, i - 1) for i in range(1, box_devices)]
        )
        coef_wide = node_coef.astype(jnp.float32)
        far_send = jnp.where(below, coef_wide[None], spread)
        is_next = (devices == box_rank + 1)[:, None]
        near_send = jnp.where(is_next, landed[box_count:].reshape(1, -1), 0.0)
        got = lax.all_to_all(
            jnp.concatenate([far_send.reshape(box_devices, far_size), near_send], axis=1),
            "box", 0, 0, tiled=True,
        )
        got_far = got[:, :far_size].reshape(box_devices, node_count, rank_width)
        is_prev = (devices == box_rank - 1)[:, None]
        arrived = jnp.sum(jnp.where(is_prev, got[:, far_size:], 0.0), axis=0).reshape(box_count, leaf)
        mirror_in = jnp.sum(jnp.where(below, got_far, 0.0), axis=0)
        every_coef = jnp.where(
            above, got_far, jnp.where(devices[:, None, None] == box_rank, coef_wide[None], 0.0)
        ).astype(jnp.bfloat16).reshape(all_nodes, rank_width)

        extended = jnp.concatenate([rounded, following], axis=0)
        near_in = jnp.dot(
            near_onehot.T.astype(jnp.bfloat16), extended, preferred_element_type=jnp.float32
        ).reshape(near_tiles.shape[0], near_tiles.shape[1], 1, leaf)
        forward = jnp.sum(near_tiles.astype(jnp.float32) * near_in, axis=(1, 3))
        near_part = forward + landed[:box_count] + arrived
        partner_coef = jnp.dot(
            far_pick.T.astype(jnp.bfloat16), every_coef, preferred_element_type=jnp.float32
        ).astype(jnp.bfloat16).reshape(node_count, -1, rank_width)
        far_forward = jnp.einsum(
            "nsab,nsb->na", coupling, partner_coef, preferred_element_type=jnp.float32
        )
        far_part = far_forward + spread[box_rank] + mirror_in
        both = rep_sum(jnp.concatenate([near_part.reshape(-1), far_part.reshape(-1)]))
        near_total = both[:near_size].reshape(box_count, leaf)
        far_total = both[near_size:].reshape(node_count, rank_width)
        group_out = far_total[box_count:].astype(jnp.bfloat16)
        parent_pick = jnp.zeros((box_count, rank_width), jnp.bfloat16)
        for group in range(group_count):
            parent_pick = jnp.where((parent_local == group)[:, None], group_out[group][None], parent_pick)
        from_parent = jnp.sum(
            transfer.astype(jnp.float32) * parent_pick.astype(jnp.float32)[:, None, :], axis=2
        )
        downward = (far_total[:box_count] + from_parent).astype(jnp.bfloat16)
        far_field = jnp.sum(
            leaf_bases.astype(jnp.float32) * downward.astype(jnp.float32)[:, :, None], axis=1
        )
        image_vec = noise_var * direction + near_total + far_field
        partials = [direction * image_vec]
        if norm_now is None:
            partials.append(targets * targets)
        if iteration + 1 < ITERS:
            partials += [residual * image_vec, image_vec * image_vec]
        sums = box_sum(jnp.sum(jnp.stack(partials), axis=(1, 2)), leaf)
        curvature = sums[0:1]
        if norm_now is None:
            norm_now = sums[1:2]
        step_size = norm_now / curvature
        weights = weights + step_size * direction
        residual = residual - step_size * image_vec
        if iteration + 1 < ITERS:
            cross, image_square = sums[-2:-1], sums[-1:]
            norm_next = norm_now - 2.0 * step_size * cross + step_size * step_size * image_square
            direction = residual + (norm_next / norm_now) * direction
            norm_now = norm_next
    return (weights, residual)


def solution(mesh):
    placed = (
        P("box", None),
        P("box", None),
        P("box", "rep", None, None),
        P("box", "rep"),
        P("box", None, None),
        P("box", None, None),
        P("box"),
        P("box", "rep", None, None),
        P("box", "rep"),
    )
    return jax.shard_map(
        local,
        mesh=mesh,
        in_specs=placed,
        out_specs=(P("box", None), P("box", None)),
        check_vma=False,
    )
```

```python
import jax
import jax.numpy as jnp
from jax import lax
from jax.sharding import PartitionSpec as P

ITERS = 2


def rep_sum(vector):
    count = lax.axis_size("rep")
    if count == 4:
        got = [
            lax.ppermute(vector, "rep", [(i, i ^ mask) for i in range(count)])
            for mask in (1, 2, 3)
        ]
        return (vector + got[0]) + (got[1] + got[2])
    if count & (count - 1) == 0:
        stride = 1
        while stride < count:
            pairs = [(i, i ^ stride) for i in range(count)]
            vector = vector + lax.ppermute(vector, "rep", pairs)
            stride *= 2
        return vector
    me = lax.axis_index("rep")
    pieces = [vector]
    for shift in range(1, count):
        pairs = [(i, (i + shift) % count) for i in range(count)]
        pieces.append(lax.ppermute(vector, "rep", pairs))
    ordered = jnp.stack(pieces)[(me - jnp.arange(count)) % count]
    return jnp.sum(ordered, axis=0)


def box_sum(values, width):
    count = lax.axis_size("box")
    sent = jnp.broadcast_to(values[None, :], (count, values.shape[0]))
    got = lax.all_to_all(sent, "box", 0, 0, tiled=True)
    wide = lax.optimization_barrier(jnp.broadcast_to(got[:, :, None], got.shape + (width,)))
    return jnp.sum(wide, axis=0)


def local(
    targets,
    noise_var,
    near_tiles,
    near_partners,
    leaf_bases,
    transfer,
    parents,
    coupling,
    coupling_partners,
):
    box_count, leaf = targets.shape
    node_count = coupling.shape[0]
    group_count = node_count - box_count
    rank_width = coupling.shape[2]
    box_devices = lax.axis_size("box")
    box_rank = lax.axis_index("box")
    all_nodes = box_devices * node_count
    near_valid = near_partners >= 0
    near_local = jnp.where(near_valid, near_partners - box_rank * box_count, 0)
    near_onehot = (
        (jnp.arange(2 * box_count, dtype=jnp.int32)[:, None] == near_local.reshape(1, -1))
        & near_valid.reshape(1, -1)
    ).astype(jnp.float32)
    parent_local = parents - box_rank * group_count
    parent_onehot = (
        jnp.arange(group_count, dtype=jnp.int32)[:, None] == parent_local[None, :]
    ).astype(jnp.float32)
    far_valid = coupling_partners >= 0
    far_index = jnp.where(far_valid, coupling_partners, 0)
    far_pick = (
        (jnp.arange(all_nodes, dtype=jnp.int32)[:, None] == far_index.reshape(1, -1))
        & far_valid.reshape(1, -1)
    )
    bf_zero = jnp.zeros((), jnp.bfloat16)
    devices = jnp.arange(box_devices, dtype=jnp.int32)
    below = (devices < box_rank)[:, None, None]
    above = (devices > box_rank)[:, None, None]
    near_size = box_count * leaf
    far_size = node_count * rank_width

    weights = jnp.zeros_like(targets)
    residual = targets
    direction = targets
    norm_now = None
    for iteration in range(ITERS):
        rounded = direction.astype(jnp.bfloat16)
        mirrored = jnp.einsum(
            "bsij,bi->bsj", near_tiles, rounded, preferred_element_type=jnp.float32
        )
        landed = jnp.dot(
            near_onehot, mirrored.reshape(-1, mirrored.shape[2]), precision=lax.Precision.HIGHEST
        )
        leaf_coef = jnp.sum(
            leaf_bases.astype(jnp.float32) * rounded.astype(jnp.float32)[:, None, :], axis=2
        ).astype(jnp.bfloat16)
        upward = jnp.sum(
            transfer.astype(jnp.float32) * leaf_coef.astype(jnp.float32)[:, :, None], axis=1
        )
        group_coef = jnp.dot(parent_onehot, upward, precision=lax.Precision.HIGHEST).astype(
            jnp.bfloat16
        )
        node_coef = jnp.concatenate([leaf_coef, group_coef], axis=0)
        far_mirror = jnp.sum(
            coupling.astype(jnp.float32) * node_coef.astype(jnp.float32)[:, None, :, None], axis=2
        )
        far_mirror = far_mirror * far_valid[:, :, None].astype(jnp.float32)
        spread = jnp.dot(
            far_pick.astype(jnp.float32), far_mirror.reshape(-1, rank_width),
            precision=lax.Precision.HIGHEST,
        ).reshape(box_devices, node_count, rank_width)
        following = lax.ppermute(
            rounded, "box", [(i, i - 1) for i in range(1, box_devices)]
        )
        coef_wide = node_coef.astype(jnp.float32)
        far_send = jnp.where(below, coef_wide[None], spread)
        is_next = (devices == box_rank + 1)[:, None]
        near_send = jnp.where(is_next, landed[box_count:].reshape(1, -1), 0.0)
        got = lax.all_to_all(
            jnp.concatenate([far_send.reshape(box_devices, far_size), near_send], axis=1),
            "box", 0, 0, tiled=True,
        )
        got_far = got[:, :far_size].reshape(box_devices, node_count, rank_width)
        is_prev = (devices == box_rank - 1)[:, None]
        arrived = jnp.sum(jnp.where(is_prev, got[:, far_size:], 0.0), axis=0).reshape(box_count, leaf)
        mirror_in = jnp.sum(jnp.where(below, got_far, 0.0), axis=0)
        every_coef = jnp.where(
            above, got_far, jnp.where(devices[:, None, None] == box_rank, coef_wide[None], 0.0)
        ).astype(jnp.bfloat16).reshape(all_nodes, rank_width)

        extended = jnp.concatenate([rounded, following], axis=0)
        near_in = jnp.dot(
            near_onehot.T.astype(jnp.bfloat16), extended, preferred_element_type=jnp.float32
        ).reshape(near_tiles.shape[0], near_tiles.shape[1], 1, leaf)
        forward = jnp.sum(near_tiles.astype(jnp.float32) * near_in, axis=(1, 3))
        near_part = forward + landed[:box_count] + arrived
        partner_coef = jnp.dot(
            far_pick.T.astype(jnp.bfloat16), every_coef, preferred_element_type=jnp.float32
        ).astype(jnp.bfloat16).reshape(node_count, -1, rank_width)
        far_forward = jnp.sum(
            coupling.astype(jnp.float32) * partner_coef.astype(jnp.float32)[:, :, None, :],
            axis=(1, 3),
        )
        far_part = far_forward + spread[box_rank] + mirror_in
        both = rep_sum(jnp.concatenate([near_part.reshape(-1), far_part.reshape(-1)]))
        near_total = both[:near_size].reshape(box_count, leaf)
        far_total = both[near_size:].reshape(node_count, rank_width)
        group_out = far_total[box_count:].astype(jnp.bfloat16)
        parent_pick = jnp.zeros((box_count, rank_width), jnp.bfloat16)
        for group in range(group_count):
            parent_pick = jnp.where((parent_local == group)[:, None], group_out[group][None], parent_pick)
        from_parent = jnp.einsum(
            "brq,bq->br", transfer, parent_pick, preferred_element_type=jnp.float32
        )
        downward = (far_total[:box_count] + from_parent).astype(jnp.bfloat16)
        far_field = jnp.einsum(
            "brl,br->bl", leaf_bases, downward, preferred_element_type=jnp.float32
        )
        image_vec = noise_var * direction + near_total + far_field
        partials = [direction * image_vec]
        if norm_now is None:
            partials.append(targets * targets)
        if iteration + 1 < ITERS:
            partials += [residual * image_vec, image_vec * image_vec]
        sums = box_sum(jnp.sum(jnp.stack(partials), axis=(1, 2)), leaf)
        curvature = sums[0:1]
        if norm_now is None:
            norm_now = sums[1:2]
        step_size = norm_now / curvature
        weights = weights + step_size * direction
        residual = residual - step_size * image_vec
        if iteration + 1 < ITERS:
            cross, image_square = sums[-2:-1], sums[-1:]
            norm_next = norm_now - 2.0 * step_size * cross + step_size * step_size * image_square
            direction = residual + (norm_next / norm_now) * direction
            norm_now = norm_next
    return (weights, residual)


def solution(mesh):
    placed = (
        P("box", None),
        P("box", None),
        P("box", "rep", None, None),
        P("box", "rep"),
        P("box", None, None),
        P("box", None, None),
        P("box"),
        P("box", "rep", None, None),
        P("box", "rep"),
    )
    return jax.shard_map(
        local,
        mesh=mesh,
        in_specs=placed,
        out_specs=(P("box", None), P("box", None)),
        check_vma=False,
    )
```

```python
import jax
import jax.numpy as jnp
from jax import lax
from jax.sharding import PartitionSpec as P

ITERS = 2


def rep_sum(vector):
    count = lax.axis_size("rep")
    if count == 4:
        got = [
            lax.ppermute(vector, "rep", [(i, i ^ mask) for i in range(count)])
            for mask in (1, 2, 3)
        ]
        return (vector + got[0]) + (got[1] + got[2])
    if count & (count - 1) == 0:
        stride = 1
        while stride < count:
            pairs = [(i, i ^ stride) for i in range(count)]
            vector = vector + lax.ppermute(vector, "rep", pairs)
            stride *= 2
        return vector
    me = lax.axis_index("rep")
    pieces = [vector]
    for shift in range(1, count):
        pairs = [(i, (i + shift) % count) for i in range(count)]
        pieces.append(lax.ppermute(vector, "rep", pairs))
    ordered = jnp.stack(pieces)[(me - jnp.arange(count)) % count]
    return jnp.sum(ordered, axis=0)


def box_sum(values, width):
    count = lax.axis_size("box")
    sent = jnp.broadcast_to(values[None, :], (count, values.shape[0]))
    got = lax.all_to_all(sent, "box", 0, 0, tiled=True)
    wide = lax.optimization_barrier(jnp.broadcast_to(got[:, :, None], got.shape + (width,)))
    return jnp.sum(wide, axis=0)


def local(
    targets,
    noise_var,
    near_tiles,
    near_partners,
    leaf_bases,
    transfer,
    parents,
    coupling,
    coupling_partners,
):
    box_count, leaf = targets.shape
    node_count = coupling.shape[0]
    group_count = node_count - box_count
    rank_width = coupling.shape[2]
    box_devices = lax.axis_size("box")
    box_rank = lax.axis_index("box")
    all_nodes = box_devices * node_count
    near_valid = near_partners >= 0
    near_local = jnp.where(near_valid, near_partners - box_rank * box_count, 0)
    near_onehot = (
        (jnp.arange(2 * box_count, dtype=jnp.int32)[:, None] == near_local.reshape(1, -1))
        & near_valid.reshape(1, -1)
    ).astype(jnp.float32)
    parent_local = parents - box_rank * group_count
    parent_onehot = (
        jnp.arange(group_count, dtype=jnp.int32)[:, None] == parent_local[None, :]
    ).astype(jnp.float32)
    far_valid = coupling_partners >= 0
    far_index = jnp.where(far_valid, coupling_partners, 0)
    far_pick = (
        (jnp.arange(all_nodes, dtype=jnp.int32)[:, None] == far_index.reshape(1, -1))
        & far_valid.reshape(1, -1)
    )
    bf_zero = jnp.zeros((), jnp.bfloat16)
    devices = jnp.arange(box_devices, dtype=jnp.int32)
    below = (devices < box_rank)[:, None, None]
    above = (devices > box_rank)[:, None, None]
    near_size = box_count * leaf
    far_size = node_count * rank_width

    weights = jnp.zeros_like(targets)
    residual = targets
    direction = targets
    norm_now = None
    for iteration in range(ITERS):
        rounded = direction.astype(jnp.bfloat16)
        mirrored = jnp.sum(
            near_tiles.astype(jnp.float32) * rounded.astype(jnp.float32)[:, None, :, None], axis=2
        )
        landed = jnp.dot(
            near_onehot, mirrored.reshape(-1, mirrored.shape[2]), precision=lax.Precision.HIGHEST
        )
        leaf_coef = jnp.sum(
            leaf_bases.astype(jnp.float32) * rounded.astype(jnp.float32)[:, None, :], axis=2
        ).astype(jnp.bfloat16)
        upward = jnp.einsum("brq,br->bq", transfer, leaf_coef, preferred_element_type=jnp.float32)
        group_coef = jnp.dot(parent_onehot, upward, precision=lax.Precision.HIGHEST).astype(
            jnp.bfloat16
        )
        node_coef = jnp.concatenate([leaf_coef, group_coef], axis=0)
        far_mirror = jnp.einsum(
            "nsab,na->nsb", coupling, node_coef, preferred_element_type=jnp.float32
        )
        far_mirror = far_mirror * far_valid[:, :, None].astype(jnp.float32)
        spread = jnp.dot(
            far_pick.astype(jnp.float32), far_mirror.reshape(-1, rank_width),
            precision=lax.Precision.HIGHEST,
        ).reshape(box_devices, node_count, rank_width)
        following = lax.ppermute(
            rounded, "box", [(i, i - 1) for i in range(1, box_devices)]
        )
        coef_wide = node_coef.astype(jnp.float32)
        far_send = jnp.where(below, coef_wide[None], spread)
        is_next = (devices == box_rank + 1)[:, None]
        near_send = jnp.where(is_next, landed[box_count:].reshape(1, -1), 0.0)
        got = lax.all_to_all(
            jnp.concatenate([far_send.reshape(box_devices, far_size), near_send], axis=1),
            "box", 0, 0, tiled=True,
        )
        got_far = got[:, :far_size].reshape(box_devices, node_count, rank_width)
        is_prev = (devices == box_rank - 1)[:, None]
        arrived = jnp.sum(jnp.where(is_prev, got[:, far_size:], 0.0), axis=0).reshape(box_count, leaf)
        mirror_in = jnp.sum(jnp.where(below, got_far, 0.0), axis=0)
        every_coef = jnp.where(
            above, got_far, jnp.where(devices[:, None, None] == box_rank, coef_wide[None], 0.0)
        ).astype(jnp.bfloat16).reshape(all_nodes, rank_width)

        extended = jnp.concatenate([rounded, following], axis=0)
        near_in = jnp.dot(
            near_onehot.T.astype(jnp.bfloat16), extended, preferred_element_type=jnp.float32
        ).reshape(near_tiles.shape[0], near_tiles.shape[1], 1, leaf)
        forward = jnp.sum(near_tiles.astype(jnp.float32) * near_in, axis=(1, 3))
        near_part = forward + landed[:box_count] + arrived
        partner_coef = jnp.dot(
            far_pick.T.astype(jnp.bfloat16), every_coef, preferred_element_type=jnp.float32
        ).astype(jnp.bfloat16).reshape(node_count, -1, rank_width)
        far_forward = jnp.einsum(
            "nsab,nsb->na", coupling, partner_coef, preferred_element_type=jnp.float32
        )
        far_part = far_forward + spread[box_rank] + mirror_in
        both = rep_sum(jnp.concatenate([near_part.reshape(-1), far_part.reshape(-1)]))
        near_total = both[:near_size].reshape(box_count, leaf)
        far_total = both[near_size:].reshape(node_count, rank_width)
        group_out = far_total[box_count:].astype(jnp.bfloat16)
        parent_pick = jnp.zeros((box_count, rank_width), jnp.bfloat16)
        for group in range(group_count):
            parent_pick = jnp.where((parent_local == group)[:, None], group_out[group][None], parent_pick)
        from_parent = jnp.einsum(
            "brq,bq->br", transfer, parent_pick, preferred_element_type=jnp.float32
        )
        downward = (far_total[:box_count] + from_parent).astype(jnp.bfloat16)
        far_field = jnp.einsum(
            "brl,br->bl", leaf_bases, downward, preferred_element_type=jnp.float32
        )
        image_vec = noise_var * direction + near_total + far_field
        partials = [direction * image_vec]
        if norm_now is None:
            partials.append(targets * targets)
        if iteration + 1 < ITERS:
            partials += [residual * image_vec, image_vec * image_vec]
        sums = box_sum(jnp.sum(jnp.stack(partials), axis=(1, 2)), leaf)
        curvature = sums[0:1]
        if norm_now is None:
            norm_now = sums[1:2]
        step_size = norm_now / curvature
        weights = weights + step_size * direction
        residual = residual - step_size * image_vec
        if iteration + 1 < ITERS:
            cross, image_square = sums[-2:-1], sums[-1:]
            norm_next = norm_now - 2.0 * step_size * cross + step_size * step_size * image_square
            direction = residual + (norm_next / norm_now) * direction
            norm_now = norm_next
    return (weights, residual)


def solution(mesh):
    placed = (
        P("box", None),
        P("box", None),
        P("box", "rep", None, None),
        P("box", "rep"),
        P("box", None, None),
        P("box", None, None),
        P("box"),
        P("box", "rep", None, None),
        P("box", "rep"),
    )
    return jax.shard_map(
        local,
        mesh=mesh,
        in_specs=placed,
        out_specs=(P("box", None), P("box", None)),
        check_vma=False,
    )
```

```python
import jax
import jax.numpy as jnp
from jax import lax
from jax.sharding import PartitionSpec as P

ITERS = 2


def rep_sum(vector):
    count = lax.axis_size("rep")
    if count == 4:
        got = [
            lax.ppermute(vector, "rep", [(i, i ^ mask) for i in range(count)])
            for mask in (1, 2, 3)
        ]
        return (vector + got[0]) + (got[1] + got[2])
    if count & (count - 1) == 0:
        stride = 1
        while stride < count:
            pairs = [(i, i ^ stride) for i in range(count)]
            vector = vector + lax.ppermute(vector, "rep", pairs)
            stride *= 2
        return vector
    me = lax.axis_index("rep")
    pieces = [vector]
    for shift in range(1, count):
        pairs = [(i, (i + shift) % count) for i in range(count)]
        pieces.append(lax.ppermute(vector, "rep", pairs))
    ordered = jnp.stack(pieces)[(me - jnp.arange(count)) % count]
    return jnp.sum(ordered, axis=0)


def box_sum(values, width):
    count = lax.axis_size("box")
    sent = jnp.broadcast_to(values[None, :], (count, values.shape[0]))
    got = lax.all_to_all(sent, "box", 0, 0, tiled=True)
    wide = lax.optimization_barrier(jnp.broadcast_to(got[:, :, None], got.shape + (width,)))
    return jnp.sum(wide, axis=0)


def local(
    targets,
    noise_var,
    near_tiles,
    near_partners,
    leaf_bases,
    transfer,
    parents,
    coupling,
    coupling_partners,
):
    box_count, leaf = targets.shape
    node_count = coupling.shape[0]
    group_count = node_count - box_count
    rank_width = coupling.shape[2]
    box_devices = lax.axis_size("box")
    box_rank = lax.axis_index("box")
    all_nodes = box_devices * node_count
    near_valid = near_partners >= 0
    near_local = jnp.where(near_valid, near_partners - box_rank * box_count, 0)
    near_onehot = (
        (jnp.arange(2 * box_count, dtype=jnp.int32)[:, None] == near_local.reshape(1, -1))
        & near_valid.reshape(1, -1)
    ).astype(jnp.float32)
    parent_local = parents - box_rank * group_count
    parent_onehot = (
        jnp.arange(group_count, dtype=jnp.int32)[:, None] == parent_local[None, :]
    ).astype(jnp.float32)
    far_valid = coupling_partners >= 0
    far_index = jnp.where(far_valid, coupling_partners, 0)
    far_pick = (
        (jnp.arange(all_nodes, dtype=jnp.int32)[:, None] == far_index.reshape(1, -1))
        & far_valid.reshape(1, -1)
    )
    bf_zero = jnp.zeros((), jnp.bfloat16)
    devices = jnp.arange(box_devices, dtype=jnp.int32)
    below = (devices < box_rank)[:, None, None]
    above = (devices > box_rank)[:, None, None]
    near_size = box_count * leaf
    far_size = node_count * rank_width

    weights = jnp.zeros_like(targets)
    residual = targets
    direction = targets
    norm_now = None
    for iteration in range(ITERS):
        rounded = direction.astype(jnp.bfloat16)
        mirrored = jnp.einsum(
            "bsij,bi->bsj", near_tiles, rounded, preferred_element_type=jnp.float32
        )
        landed = jnp.dot(
            near_onehot, mirrored.reshape(-1, mirrored.shape[2]), precision=lax.Precision.HIGHEST
        )
        leaf_coef = jnp.sum(
            leaf_bases.astype(jnp.float32) * rounded.astype(jnp.float32)[:, None, :], axis=2
        ).astype(jnp.bfloat16)
        upward = jnp.einsum("brq,br->bq", transfer, leaf_coef, preferred_element_type=jnp.float32)
        group_coef = jnp.dot(parent_onehot, upward, precision=lax.Precision.HIGHEST).astype(
            jnp.bfloat16
        )
        node_coef = jnp.concatenate([leaf_coef, group_coef], axis=0)
        far_mirror = jnp.einsum(
            "nsab,na->nsb", coupling, node_coef, preferred_element_type=jnp.float32
        )
        far_mirror = far_mirror * far_valid[:, :, None].astype(jnp.float32)
        spread = jnp.dot(
            far_pick.astype(jnp.float32), far_mirror.reshape(-1, rank_width),
            precision=lax.Precision.HIGHEST,
        ).reshape(box_devices, node_count, rank_width)
        following = lax.ppermute(
            rounded, "box", [(i, i - 1) for i in range(1, box_devices)]
        )
        coef_wide = node_coef.astype(jnp.float32)
        far_send = jnp.where(below, coef_wide[None], spread)
        is_next = (devices == box_rank + 1)[:, None]
        near_send = jnp.where(is_next, landed[box_count:].reshape(1, -1), 0.0)
        got = lax.all_to_all(
            jnp.concatenate([far_send.reshape(box_devices, far_size), near_send], axis=1),
            "box", 0, 0, tiled=True,
        )
        got_far = got[:, :far_size].reshape(box_devices, node_count, rank_width)
        is_prev = (devices == box_rank - 1)[:, None]
        arrived = jnp.sum(jnp.where(is_prev, got[:, far_size:], 0.0), axis=0).reshape(box_count, leaf)
        mirror_in = jnp.sum(jnp.where(below, got_far, 0.0), axis=0)
        every_coef = jnp.where(
            above, got_far, jnp.where(devices[:, None, None] == box_rank, coef_wide[None], 0.0)
        ).astype(jnp.bfloat16).reshape(all_nodes, rank_width)

        extended = jnp.concatenate([rounded, following], axis=0)
        near_in = jnp.dot(
            near_onehot.T.astype(jnp.bfloat16), extended, preferred_element_type=jnp.float32
        ).reshape(near_tiles.shape[0], near_tiles.shape[1], 1, leaf)
        forward = jnp.sum(near_tiles.astype(jnp.float32) * near_in, axis=(1, 3))
        near_part = forward + landed[:box_count] + arrived
        partner_coef = jnp.dot(
            far_pick.T.astype(jnp.bfloat16), every_coef, preferred_element_type=jnp.float32
        ).astype(jnp.bfloat16).reshape(node_count, -1, rank_width)
        far_forward = jnp.einsum(
            "nsab,nsb->na", coupling, partner_coef, preferred_element_type=jnp.float32
        )
        far_part = far_forward + spread[box_rank] + mirror_in
        far_rows = far_size // leaf if far_size % leaf == 0 else None
        if far_rows is not None:
            both = rep_sum(jnp.concatenate([near_part, far_part.reshape(far_rows, leaf)], axis=0))
            near_total = both[:box_count]
            far_total = both[box_count:].reshape(node_count, rank_width)
        else:
            both = rep_sum(jnp.concatenate([near_part.reshape(-1), far_part.reshape(-1)]))
            near_total = both[:near_size].reshape(box_count, leaf)
            far_total = both[near_size:].reshape(node_count, rank_width)
        group_out = far_total[box_count:].astype(jnp.bfloat16)
        parent_pick = jnp.zeros((box_count, rank_width), jnp.bfloat16)
        for group in range(group_count):
            parent_pick = jnp.where((parent_local == group)[:, None], group_out[group][None], parent_pick)
        from_parent = jnp.einsum(
            "brq,bq->br", transfer, parent_pick, preferred_element_type=jnp.float32
        )
        downward = (far_total[:box_count] + from_parent).astype(jnp.bfloat16)
        far_field = jnp.einsum(
            "brl,br->bl", leaf_bases, downward, preferred_element_type=jnp.float32
        )
        image_vec = noise_var * direction + near_total + far_field
        partials = [direction * image_vec]
        if norm_now is None:
            partials.append(targets * targets)
        if iteration + 1 < ITERS:
            partials += [residual * image_vec, image_vec * image_vec]
        sums = box_sum(jnp.sum(jnp.stack(partials), axis=(1, 2)), leaf)
        curvature = sums[0:1]
        if norm_now is None:
            norm_now = sums[1:2]
        step_size = norm_now / curvature
        weights = weights + step_size * direction
        residual = residual - step_size * image_vec
        if iteration + 1 < ITERS:
            cross, image_square = sums[-2:-1], sums[-1:]
            norm_next = norm_now - 2.0 * step_size * cross + step_size * step_size * image_square
            direction = residual + (norm_next / norm_now) * direction
            norm_now = norm_next
    return (weights, residual)


def solution(mesh):
    placed = (
        P("box", None),
        P("box", None),
        P("box", "rep", None, None),
        P("box", "rep"),
        P("box", None, None),
        P("box", None, None),
        P("box"),
        P("box", "rep", None, None),
        P("box", "rep"),
    )
    return jax.shard_map(
        local,
        mesh=mesh,
        in_specs=placed,
        out_specs=(P("box", None), P("box", None)),
        check_vma=False,
    )
```

```python
import jax
import jax.numpy as jnp
from jax import lax
from jax.sharding import PartitionSpec as P

ITERS = 2


def rep_sum(vector):
    count = lax.axis_size("rep")
    if count == 4:
        got = [
            lax.ppermute(vector, "rep", [(i, i ^ mask) for i in range(count)])
            for mask in (1, 2, 3)
        ]
        return (vector + got[0]) + (got[1] + got[2])
    if count & (count - 1) == 0:
        stride = 1
        while stride < count:
            pairs = [(i, i ^ stride) for i in range(count)]
            vector = vector + lax.ppermute(vector, "rep", pairs)
            stride *= 2
        return vector
    me = lax.axis_index("rep")
    pieces = [vector]
    for shift in range(1, count):
        pairs = [(i, (i + shift) % count) for i in range(count)]
        pieces.append(lax.ppermute(vector, "rep", pairs))
    ordered = jnp.stack(pieces)[(me - jnp.arange(count)) % count]
    return jnp.sum(ordered, axis=0)


def box_sum(values, width):
    count = lax.axis_size("box")
    sent = jnp.broadcast_to(values[None, :], (count, values.shape[0]))
    got = lax.all_to_all(sent, "box", 0, 0, tiled=True)
    wide = lax.optimization_barrier(jnp.broadcast_to(got[:, :, None], got.shape + (width,)))
    return jnp.sum(wide, axis=0)


def local(
    targets,
    noise_var,
    near_tiles,
    near_partners,
    leaf_bases,
    transfer,
    parents,
    coupling,
    coupling_partners,
):
    box_count, leaf = targets.shape
    node_count = coupling.shape[0]
    group_count = node_count - box_count
    rank_width = coupling.shape[2]
    box_devices = lax.axis_size("box")
    box_rank = lax.axis_index("box")
    all_nodes = box_devices * node_count
    near_valid = near_partners >= 0
    near_local = jnp.where(near_valid, near_partners - box_rank * box_count, 0)
    near_onehot = (
        (jnp.arange(2 * box_count, dtype=jnp.int32)[:, None] == near_local.reshape(1, -1))
        & near_valid.reshape(1, -1)
    ).astype(jnp.float32)
    parent_local = parents - box_rank * group_count
    parent_onehot = (
        jnp.arange(group_count, dtype=jnp.int32)[:, None] == parent_local[None, :]
    ).astype(jnp.float32)
    far_valid = coupling_partners >= 0
    far_index = jnp.where(far_valid, coupling_partners, 0)
    far_pick = (
        (jnp.arange(all_nodes, dtype=jnp.int32)[:, None] == far_index.reshape(1, -1))
        & far_valid.reshape(1, -1)
    )
    bf_zero = jnp.zeros((), jnp.bfloat16)
    devices = jnp.arange(box_devices, dtype=jnp.int32)
    below = (devices < box_rank)[:, None, None]
    above = (devices > box_rank)[:, None, None]
    near_size = box_count * leaf
    far_size = node_count * rank_width

    weights = jnp.zeros_like(targets)
    residual = targets
    direction = targets
    norm_now = None
    for iteration in range(ITERS):
        rounded = direction.astype(jnp.bfloat16)
        mirrored = jnp.einsum(
            "bsij,bi->bsj", near_tiles, rounded, preferred_element_type=jnp.float32
        )
        landed = jnp.dot(
            near_onehot, mirrored.reshape(-1, mirrored.shape[2]), precision=lax.Precision.HIGHEST
        )
        leaf_coef = jnp.sum(
            leaf_bases.astype(jnp.float32) * rounded.astype(jnp.float32)[:, None, :], axis=2
        ).astype(jnp.bfloat16)
        upward = jnp.einsum("brq,br->bq", transfer, leaf_coef, preferred_element_type=jnp.float32)
        group_coef = jnp.dot(parent_onehot, upward, precision=lax.Precision.HIGHEST).astype(
            jnp.bfloat16
        )
        node_coef = jnp.concatenate([leaf_coef, group_coef], axis=0)
        far_mirror = jnp.einsum(
            "nsab,na->nsb", coupling, node_coef, preferred_element_type=jnp.float32
        )
        far_mirror = far_mirror * far_valid[:, :, None].astype(jnp.float32)
        spread = jnp.dot(
            far_pick.astype(jnp.float32), far_mirror.reshape(-1, rank_width),
            precision=lax.Precision.HIGHEST,
        ).reshape(box_devices, node_count, rank_width)
        following = lax.ppermute(
            rounded, "box", [(i, i - 1) for i in range(1, box_devices)]
        )
        coef_wide = node_coef.astype(jnp.float32)
        far_send = jnp.where(below, coef_wide[None], spread)
        is_next = (devices == box_rank + 1)[:, None]
        near_send = jnp.where(is_next, landed[box_count:].reshape(1, -1), 0.0)
        got = lax.all_to_all(
            jnp.concatenate([far_send.reshape(box_devices, far_size), near_send], axis=1),
            "box", 0, 0, tiled=True,
        )
        got_far = got[:, :far_size].reshape(box_devices, node_count, rank_width)
        is_prev = (devices == box_rank - 1)[:, None]
        arrived = jnp.sum(jnp.where(is_prev, got[:, far_size:], 0.0), axis=0).reshape(box_count, leaf)
        mirror_in = jnp.sum(jnp.where(below, got_far, 0.0), axis=0)
        every_coef = jnp.where(
            above, got_far, jnp.where(devices[:, None, None] == box_rank, coef_wide[None], 0.0)
        ).astype(jnp.bfloat16).reshape(all_nodes, rank_width)

        extended = jnp.concatenate([rounded, following], axis=0)
        near_in = jnp.dot(
            near_onehot.T.astype(jnp.bfloat16), extended, preferred_element_type=jnp.float32
        ).reshape(near_tiles.shape[0], near_tiles.shape[1], 1, leaf)
        forward = jnp.sum(near_tiles.astype(jnp.float32) * near_in, axis=(1, 3))
        near_part = forward + landed[:box_count] + arrived
        partner_coef = jnp.dot(
            far_pick.T.astype(jnp.bfloat16), every_coef, preferred_element_type=jnp.float32
        ).astype(jnp.bfloat16).reshape(node_count, -1, rank_width)
        far_forward = jnp.sum(
            coupling.astype(jnp.float32) * partner_coef.astype(jnp.float32)[:, :, None, :],
            axis=(1, 3),
        )
        far_part = far_forward + spread[box_rank] + mirror_in
        both = rep_sum(jnp.concatenate([near_part.reshape(-1), far_part.reshape(-1)]))
        near_total = both[:near_size].reshape(box_count, leaf)
        far_total = both[near_size:].reshape(node_count, rank_width)
        group_out = far_total[box_count:].astype(jnp.bfloat16)
        parent_pick = jnp.zeros((box_count, rank_width), jnp.bfloat16)
        for group in range(group_count):
            parent_pick = jnp.where((parent_local == group)[:, None], group_out[group][None], parent_pick)
        from_parent = jnp.einsum(
            "brq,bq->br", transfer, parent_pick, preferred_element_type=jnp.float32
        )
        downward = (far_total[:box_count] + from_parent).astype(jnp.bfloat16)
        far_field = jnp.einsum(
            "brl,br->bl", leaf_bases, downward, preferred_element_type=jnp.float32
        )
        image_vec = noise_var * direction + near_total + far_field
        partials = [direction * image_vec]
        if norm_now is None:
            partials.append(targets * targets)
        if iteration + 1 < ITERS:
            partials += [residual * image_vec, image_vec * image_vec]
        sums = box_sum(jnp.sum(jnp.stack(partials), axis=(1, 2)), leaf)
        curvature = sums[0:1]
        if norm_now is None:
            norm_now = sums[1:2]
        step_size = norm_now / curvature
        weights = weights + step_size * direction
        residual = residual - step_size * image_vec
        if iteration + 1 < ITERS:
            cross, image_square = sums[-2:-1], sums[-1:]
            norm_next = norm_now - 2.0 * step_size * cross + step_size * step_size * image_square
            direction = residual + (norm_next / norm_now) * direction
            norm_now = norm_next
    return (weights, residual)


def solution(mesh):
    placed = (
        P("box", None),
        P("box", None),
        P("box", "rep", None, None),
        P("box", "rep"),
        P("box", None, None),
        P("box", None, None),
        P("box"),
        P("box", "rep", None, None),
        P("box", "rep"),
    )
    return jax.shard_map(
        local,
        mesh=mesh,
        in_specs=placed,
        out_specs=(P("box", None), P("box", None)),
        check_vma=False,
    )
```

```python
import jax
import jax.numpy as jnp
from jax import lax
from jax.sharding import PartitionSpec as P

ITERS = 2


def rep_sum(vector):
    count = lax.axis_size("rep")
    if count == 4:
        got = [
            lax.ppermute(vector, "rep", [(i, i ^ mask) for i in range(count)])
            for mask in (1, 2, 3)
        ]
        return (vector + got[0]) + (got[1] + got[2])
    if count & (count - 1) == 0:
        stride = 1
        while stride < count:
            pairs = [(i, i ^ stride) for i in range(count)]
            vector = vector + lax.ppermute(vector, "rep", pairs)
            stride *= 2
        return vector
    me = lax.axis_index("rep")
    pieces = [vector]
    for shift in range(1, count):
        pairs = [(i, (i + shift) % count) for i in range(count)]
        pieces.append(lax.ppermute(vector, "rep", pairs))
    ordered = jnp.stack(pieces)[(me - jnp.arange(count)) % count]
    return jnp.sum(ordered, axis=0)


def box_sum(values, width):
    count = lax.axis_size("box")
    sent = jnp.broadcast_to(values[None, :], (count, values.shape[0]))
    got = lax.all_to_all(sent, "box", 0, 0, tiled=True)
    wide = lax.optimization_barrier(jnp.broadcast_to(got[:, :, None], got.shape + (width,)))
    return jnp.sum(wide, axis=0)


def local(
    targets,
    noise_var,
    near_tiles,
    near_partners,
    leaf_bases,
    transfer,
    parents,
    coupling,
    coupling_partners,
):
    box_count, leaf = targets.shape
    node_count = coupling.shape[0]
    group_count = node_count - box_count
    rank_width = coupling.shape[2]
    box_devices = lax.axis_size("box")
    box_rank = lax.axis_index("box")
    all_nodes = box_devices * node_count
    near_valid = near_partners >= 0
    near_local = jnp.where(near_valid, near_partners - box_rank * box_count, 0)
    near_onehot = (
        (jnp.arange(2 * box_count, dtype=jnp.int32)[:, None] == near_local.reshape(1, -1))
        & near_valid.reshape(1, -1)
    ).astype(jnp.float32)
    parent_local = parents - box_rank * group_count
    parent_onehot = (
        jnp.arange(group_count, dtype=jnp.int32)[:, None] == parent_local[None, :]
    ).astype(jnp.float32)
    far_valid = coupling_partners >= 0
    far_index = jnp.where(far_valid, coupling_partners, 0)
    far_pick = (
        (jnp.arange(all_nodes, dtype=jnp.int32)[:, None] == far_index.reshape(1, -1))
        & far_valid.reshape(1, -1)
    )
    bf_zero = jnp.zeros((), jnp.bfloat16)
    devices = jnp.arange(box_devices, dtype=jnp.int32)
    below = (devices < box_rank)[:, None, None]
    above = (devices > box_rank)[:, None, None]
    near_size = box_count * leaf
    far_size = node_count * rank_width

    weights = jnp.zeros_like(targets)
    residual = targets
    direction = targets
    norm_now = None
    for iteration in range(ITERS):
        rounded = direction.astype(jnp.bfloat16)
        mirrored = jnp.einsum(
            "bsij,bi->bsj", near_tiles, rounded, preferred_element_type=jnp.float32
        )
        landed = jnp.dot(
            near_onehot, mirrored.reshape(-1, mirrored.shape[2]), precision=lax.Precision.HIGHEST
        )
        leaf_coef = jnp.sum(
            leaf_bases.astype(jnp.float32) * rounded.astype(jnp.float32)[:, None, :], axis=2
        ).astype(jnp.bfloat16)
        upward = jnp.sum(
            transfer.astype(jnp.float32) * leaf_coef.astype(jnp.float32)[:, :, None], axis=1
        )
        group_coef = jnp.dot(parent_onehot, upward, precision=lax.Precision.HIGHEST).astype(
            jnp.bfloat16
        )
        node_coef = jnp.concatenate([leaf_coef, group_coef], axis=0)
        far_mirror = jnp.einsum(
            "nsab,na->nsb", coupling, node_coef, preferred_element_type=jnp.float32
        )
        far_mirror = far_mirror * far_valid[:, :, None].astype(jnp.float32)
        spread = jnp.dot(
            far_pick.astype(jnp.float32), far_mirror.reshape(-1, rank_width),
            precision=lax.Precision.HIGHEST,
        ).reshape(box_devices, node_count, rank_width)
        following = lax.ppermute(
            rounded, "box", [(i, i - 1) for i in range(1, box_devices)]
        )
        coef_wide = node_coef.astype(jnp.float32)
        far_send = jnp.where(below, coef_wide[None], spread)
        is_next = (devices == box_rank + 1)[:, None]
        near_send = jnp.where(is_next, landed[box_count:].reshape(1, -1), 0.0)
        got = lax.all_to_all(
            jnp.concatenate([far_send.reshape(box_devices, far_size), near_send], axis=1),
            "box", 0, 0, tiled=True,
        )
        got_far = got[:, :far_size].reshape(box_devices, node_count, rank_width)
        is_prev = (devices == box_rank - 1)[:, None]
        arrived = jnp.sum(jnp.where(is_prev, got[:, far_size:], 0.0), axis=0).reshape(box_count, leaf)
        mirror_in = jnp.sum(jnp.where(below, got_far, 0.0), axis=0)
        every_coef = jnp.where(
            above, got_far, jnp.where(devices[:, None, None] == box_rank, coef_wide[None], 0.0)
        ).astype(jnp.bfloat16).reshape(all_nodes, rank_width)

        extended = jnp.concatenate([rounded, following], axis=0)
        near_in = jnp.dot(
            near_onehot.T.astype(jnp.bfloat16), extended, preferred_element_type=jnp.float32
        ).reshape(near_tiles.shape[0], near_tiles.shape[1], 1, leaf)
        forward = jnp.sum(near_tiles.astype(jnp.float32) * near_in, axis=(1, 3))
        near_part = forward + landed[:box_count] + arrived
        partner_coef = jnp.dot(
            far_pick.T.astype(jnp.bfloat16), every_coef, preferred_element_type=jnp.float32
        ).astype(jnp.bfloat16).reshape(node_count, -1, rank_width)
        far_forward = jnp.einsum(
            "nsab,nsb->na", coupling, partner_coef, preferred_element_type=jnp.float32
        )
        far_part = far_forward + spread[box_rank] + mirror_in
        both = rep_sum(jnp.concatenate([near_part.reshape(-1), far_part.reshape(-1)]))
        near_total = both[:near_size].reshape(box_count, leaf)
        far_total = both[near_size:].reshape(node_count, rank_width)
        group_out = far_total[box_count:].astype(jnp.bfloat16)
        parent_pick = jnp.zeros((box_count, rank_width), jnp.bfloat16)
        for group in range(group_count):
            parent_pick = jnp.where((parent_local == group)[:, None], group_out[group][None], parent_pick)
        from_parent = jnp.einsum(
            "brq,bq->br", transfer, parent_pick, preferred_element_type=jnp.float32
        )
        downward = (far_total[:box_count] + from_parent).astype(jnp.bfloat16)
        far_field = jnp.einsum(
            "brl,br->bl", leaf_bases, downward, preferred_element_type=jnp.float32
        )
        image_vec = noise_var * direction + near_total + far_field
        partials = [direction * image_vec]
        if norm_now is None:
            partials.append(targets * targets)
        if iteration + 1 < ITERS:
            partials += [residual * image_vec, image_vec * image_vec]
        sums = box_sum(jnp.sum(jnp.stack(partials), axis=(1, 2)), leaf)
        curvature = sums[0:1]
        if norm_now is None:
            norm_now = sums[1:2]
        step_size = norm_now / curvature
        weights = weights + step_size * direction
        residual = residual - step_size * image_vec
        if iteration + 1 < ITERS:
            cross, image_square = sums[-2:-1], sums[-1:]
            norm_next = norm_now - 2.0 * step_size * cross + step_size * step_size * image_square
            direction = residual + (norm_next / norm_now) * direction
            norm_now = norm_next
    return (weights, residual)


def solution(mesh):
    placed = (
        P("box", None),
        P("box", None),
        P("box", "rep", None, None),
        P("box", "rep"),
        P("box", None, None),
        P("box", None, None),
        P("box"),
        P("box", "rep", None, None),
        P("box", "rep"),
    )
    return jax.shard_map(
        local,
        mesh=mesh,
        in_specs=placed,
        out_specs=(P("box", None), P("box", None)),
        check_vma=False,
    )
```

```python
import jax
import jax.numpy as jnp
from jax import lax
from jax.sharding import PartitionSpec as P

ITERS = 2


def rep_sum(vector):
    count = lax.axis_size("rep")
    if count == 4:
        got = [
            lax.ppermute(vector, "rep", [(i, i ^ mask) for i in range(count)])
            for mask in (1, 2, 3)
        ]
        return (vector + got[0]) + (got[1] + got[2])
    if count & (count - 1) == 0:
        stride = 1
        while stride < count:
            pairs = [(i, i ^ stride) for i in range(count)]
            vector = vector + lax.ppermute(vector, "rep", pairs)
            stride *= 2
        return vector
    me = lax.axis_index("rep")
    pieces = [vector]
    for shift in range(1, count):
        pairs = [(i, (i + shift) % count) for i in range(count)]
        pieces.append(lax.ppermute(vector, "rep", pairs))
    ordered = jnp.stack(pieces)[(me - jnp.arange(count)) % count]
    return jnp.sum(ordered, axis=0)


def box_sum(values, width):
    count = lax.axis_size("box")
    sent = jnp.broadcast_to(values[None, :], (count, values.shape[0]))
    got = lax.all_to_all(sent, "box", 0, 0, tiled=True)
    wide = lax.optimization_barrier(jnp.broadcast_to(got[:, :, None], got.shape + (width,)))
    return jnp.sum(wide, axis=0)


def local(
    targets,
    noise_var,
    near_tiles,
    near_partners,
    leaf_bases,
    transfer,
    parents,
    coupling,
    coupling_partners,
):
    box_count, leaf = targets.shape
    node_count = coupling.shape[0]
    group_count = node_count - box_count
    rank_width = coupling.shape[2]
    box_devices = lax.axis_size("box")
    box_rank = lax.axis_index("box")
    all_nodes = box_devices * node_count
    near_valid = near_partners >= 0
    near_local = jnp.where(near_valid, near_partners - box_rank * box_count, 0)
    near_onehot = (
        (jnp.arange(2 * box_count, dtype=jnp.int32)[:, None] == near_local.reshape(1, -1))
        & near_valid.reshape(1, -1)
    ).astype(jnp.float32)
    parent_local = parents - box_rank * group_count
    parent_onehot = (
        jnp.arange(group_count, dtype=jnp.int32)[:, None] == parent_local[None, :]
    ).astype(jnp.float32)
    far_valid = coupling_partners >= 0
    far_index = jnp.where(far_valid, coupling_partners, 0)
    far_pick = (
        (jnp.arange(all_nodes, dtype=jnp.int32)[:, None] == far_index.reshape(1, -1))
        & far_valid.reshape(1, -1)
    )
    bf_zero = jnp.zeros((), jnp.bfloat16)
    devices = jnp.arange(box_devices, dtype=jnp.int32)
    below = (devices < box_rank)[:, None, None]
    above = (devices > box_rank)[:, None, None]
    near_size = box_count * leaf
    far_size = node_count * rank_width

    weights = jnp.zeros_like(targets)
    residual = targets
    direction = targets
    norm_now = None
    for iteration in range(ITERS):
        rounded = direction.astype(jnp.bfloat16)
        mirrored = jnp.einsum(
            "bsij,bi->bsj", near_tiles, rounded, preferred_element_type=jnp.float32
        )
        landed = jnp.dot(
            near_onehot, mirrored.reshape(-1, mirrored.shape[2]), precision=lax.Precision.HIGHEST
        )
        leaf_coef = jnp.sum(
            leaf_bases.astype(jnp.float32) * rounded.astype(jnp.float32)[:, None, :], axis=2
        ).astype(jnp.bfloat16)
        upward = jnp.einsum("brq,br->bq", transfer, leaf_coef, preferred_element_type=jnp.float32)
        group_coef = jnp.dot(parent_onehot, upward, precision=lax.Precision.HIGHEST).astype(
            jnp.bfloat16
        )
        node_coef = jnp.concatenate([leaf_coef, group_coef], axis=0)
        far_mirror = jnp.einsum(
            "nsab,na->nsb", coupling, node_coef, preferred_element_type=jnp.float32
        )
        far_mirror = far_mirror * far_valid[:, :, None].astype(jnp.float32)
        spread = jnp.dot(
            far_pick.astype(jnp.float32), far_mirror.reshape(-1, rank_width),
            precision=lax.Precision.HIGHEST,
        ).reshape(box_devices, node_count, rank_width)
        following = lax.ppermute(
            rounded, "box", [(i, i - 1) for i in range(1, box_devices)]
        )
        coef_wide = node_coef.astype(jnp.float32)
        far_send = jnp.where(below, coef_wide[None], spread)
        is_next = (devices == box_rank + 1)[:, None]
        near_send = jnp.where(is_next, landed[box_count:].reshape(1, -1), 0.0)
        got = lax.all_to_all(
            jnp.concatenate([far_send.reshape(box_devices, far_size), near_send], axis=1),
            "box", 0, 0, tiled=True,
        )
        got_far = got[:, :far_size].reshape(box_devices, node_count, rank_width)
        is_prev = (devices == box_rank - 1)[:, None]
        arrived = jnp.sum(jnp.where(is_prev, got[:, far_size:], 0.0), axis=0).reshape(box_count, leaf)
        mirror_in = jnp.sum(jnp.where(below, got_far, 0.0), axis=0)
        every_coef = jnp.where(
            above, got_far, jnp.where(devices[:, None, None] == box_rank, coef_wide[None], 0.0)
        ).astype(jnp.bfloat16).reshape(all_nodes, rank_width)

        extended = jnp.concatenate([rounded, following], axis=0)
        near_in = jnp.dot(
            near_onehot.T.astype(jnp.bfloat16), extended, preferred_element_type=jnp.float32
        ).reshape(near_tiles.shape[0], near_tiles.shape[1], 1, leaf)
        forward = jnp.sum(near_tiles.astype(jnp.float32) * near_in, axis=(1, 3))
        near_part = forward + landed[:box_count] + arrived
        partner_coef = jnp.dot(
            far_pick.T.astype(jnp.bfloat16), every_coef, preferred_element_type=jnp.float32
        ).astype(jnp.bfloat16).reshape(node_count, -1, rank_width)
        far_forward = jnp.einsum(
            "nsab,nsb->na", coupling, partner_coef, preferred_element_type=jnp.float32
        )
        far_part = far_forward + spread[box_rank] + mirror_in
        both = rep_sum(jnp.concatenate([near_part.reshape(-1), far_part.reshape(-1)]))
        near_total = both[:near_size].reshape(box_count, leaf)
        far_total = both[near_size:].reshape(node_count, rank_width)
        group_out = far_total[box_count:].astype(jnp.bfloat16)
        parent_pick = jnp.dot(
            parent_onehot.T.astype(jnp.bfloat16), group_out, preferred_element_type=jnp.float32
        ).astype(jnp.bfloat16)
        from_parent = jnp.einsum(
            "brq,bq->br", transfer, parent_pick, preferred_element_type=jnp.float32
        )
        downward = (far_total[:box_count] + from_parent).astype(jnp.bfloat16)
        far_field = jnp.einsum(
            "brl,br->bl", leaf_bases, downward, preferred_element_type=jnp.float32
        )
        image_vec = noise_var * direction + near_total + far_field
        partials = [direction * image_vec]
        if norm_now is None:
            partials.append(targets * targets)
        if iteration + 1 < ITERS:
            partials += [residual * image_vec, image_vec * image_vec]
        sums = box_sum(jnp.sum(jnp.stack(partials), axis=(1, 2)), leaf)
        curvature = sums[0:1]
        if norm_now is None:
            norm_now = sums[1:2]
        step_size = norm_now / curvature
        weights = weights + step_size * direction
        residual = residual - step_size * image_vec
        if iteration + 1 < ITERS:
            cross, image_square = sums[-2:-1], sums[-1:]
            norm_next = norm_now - 2.0 * step_size * cross + step_size * step_size * image_square
            direction = residual + (norm_next / norm_now) * direction
            norm_now = norm_next
    return (weights, residual)


def solution(mesh):
    placed = (
        P("box", None),
        P("box", None),
        P("box", "rep", None, None),
        P("box", "rep"),
        P("box", None, None),
        P("box", None, None),
        P("box"),
        P("box", "rep", None, None),
        P("box", "rep"),
    )
    return jax.shard_map(
        local,
        mesh=mesh,
        in_specs=placed,
        out_specs=(P("box", None), P("box", None)),
        check_vma=False,
    )
```

```python
import jax
import jax.numpy as jnp
from jax import lax
from jax.sharding import PartitionSpec as P

ITERS = 2


def rep_sum(vector):
    count = lax.axis_size("rep")
    if count == 4:
        got = [
            lax.ppermute(vector, "rep", [(i, i ^ mask) for i in range(count)])
            for mask in (1, 2, 3)
        ]
        return (vector + got[0]) + (got[1] + got[2])
    if count & (count - 1) == 0:
        stride = 1
        while stride < count:
            pairs = [(i, i ^ stride) for i in range(count)]
            vector = vector + lax.ppermute(vector, "rep", pairs)
            stride *= 2
        return vector
    me = lax.axis_index("rep")
    pieces = [vector]
    for shift in range(1, count):
        pairs = [(i, (i + shift) % count) for i in range(count)]
        pieces.append(lax.ppermute(vector, "rep", pairs))
    ordered = jnp.stack(pieces)[(me - jnp.arange(count)) % count]
    return jnp.sum(ordered, axis=0)


def box_sum(values, width):
    count = lax.axis_size("box")
    sent = jnp.broadcast_to(values[None, :], (count, values.shape[0]))
    got = lax.all_to_all(sent, "box", 0, 0, tiled=True)
    total = jnp.sum(got, axis=0)
    return lax.optimization_barrier(jnp.broadcast_to(total[:, None], total.shape + (width,)))


def local(
    targets,
    noise_var,
    near_tiles,
    near_partners,
    leaf_bases,
    transfer,
    parents,
    coupling,
    coupling_partners,
):
    box_count, leaf = targets.shape
    node_count = coupling.shape[0]
    group_count = node_count - box_count
    rank_width = coupling.shape[2]
    box_devices = lax.axis_size("box")
    box_rank = lax.axis_index("box")
    all_nodes = box_devices * node_count
    near_valid = near_partners >= 0
    near_local = jnp.where(near_valid, near_partners - box_rank * box_count, 0)
    near_onehot = (
        (jnp.arange(2 * box_count, dtype=jnp.int32)[:, None] == near_local.reshape(1, -1))
        & near_valid.reshape(1, -1)
    ).astype(jnp.float32)
    parent_local = parents - box_rank * group_count
    parent_onehot = (
        jnp.arange(group_count, dtype=jnp.int32)[:, None] == parent_local[None, :]
    ).astype(jnp.float32)
    far_valid = coupling_partners >= 0
    far_index = jnp.where(far_valid, coupling_partners, 0)
    far_pick = (
        (jnp.arange(all_nodes, dtype=jnp.int32)[:, None] == far_index.reshape(1, -1))
        & far_valid.reshape(1, -1)
    )
    bf_zero = jnp.zeros((), jnp.bfloat16)
    devices = jnp.arange(box_devices, dtype=jnp.int32)
    below = (devices < box_rank)[:, None, None]
    above = (devices > box_rank)[:, None, None]
    near_size = box_count * leaf
    far_size = node_count * rank_width

    weights = jnp.zeros_like(targets)
    residual = targets
    direction = targets
    norm_now = None
    for iteration in range(ITERS):
        rounded = direction.astype(jnp.bfloat16)
        mirrored = jnp.einsum(
            "bsij,bi->bsj", near_tiles, rounded, preferred_element_type=jnp.float32
        )
        landed = jnp.dot(
            near_onehot, mirrored.reshape(-1, mirrored.shape[2]), precision=lax.Precision.HIGHEST
        )
        leaf_coef = jnp.sum(
            leaf_bases.astype(jnp.float32) * rounded.astype(jnp.float32)[:, None, :], axis=2
        ).astype(jnp.bfloat16)
        upward = jnp.einsum("brq,br->bq", transfer, leaf_coef, preferred_element_type=jnp.float32)
        group_coef = jnp.dot(parent_onehot, upward, precision=lax.Precision.HIGHEST).astype(
            jnp.bfloat16
        )
        node_coef = jnp.concatenate([leaf_coef, group_coef], axis=0)
        far_mirror = jnp.einsum(
            "nsab,na->nsb", coupling, node_coef, preferred_element_type=jnp.float32
        )
        far_mirror = far_mirror * far_valid[:, :, None].astype(jnp.float32)
        spread = jnp.dot(
            far_pick.astype(jnp.float32), far_mirror.reshape(-1, rank_width),
            precision=lax.Precision.HIGHEST,
        ).reshape(box_devices, node_count, rank_width)
        following = lax.ppermute(
            rounded, "box", [(i, i - 1) for i in range(1, box_devices)]
        )
        coef_wide = node_coef.astype(jnp.float32)
        far_send = jnp.where(below, coef_wide[None], spread)
        is_next = (devices == box_rank + 1)[:, None]
        near_send = jnp.where(is_next, landed[box_count:].reshape(1, -1), 0.0)
        got = lax.all_to_all(
            jnp.concatenate([far_send.reshape(box_devices, far_size), near_send], axis=1),
            "box", 0, 0, tiled=True,
        )
        got_far = got[:, :far_size].reshape(box_devices, node_count, rank_width)
        is_prev = (devices == box_rank - 1)[:, None]
        arrived = jnp.sum(jnp.where(is_prev, got[:, far_size:], 0.0), axis=0).reshape(box_count, leaf)
        mirror_in = jnp.sum(jnp.where(below, got_far, 0.0), axis=0)
        every_coef = jnp.where(
            above, got_far, jnp.where(devices[:, None, None] == box_rank, coef_wide[None], 0.0)
        ).astype(jnp.bfloat16).reshape(all_nodes, rank_width)

        extended = jnp.concatenate([rounded, following], axis=0)
        near_in = jnp.dot(
            near_onehot.T.astype(jnp.bfloat16), extended, preferred_element_type=jnp.float32
        ).reshape(near_tiles.shape[0], near_tiles.shape[1], 1, leaf)
        forward = jnp.sum(near_tiles.astype(jnp.float32) * near_in, axis=(1, 3))
        near_part = forward + landed[:box_count] + arrived
        partner_coef = jnp.dot(
            far_pick.T.astype(jnp.bfloat16), every_coef, preferred_element_type=jnp.float32
        ).astype(jnp.bfloat16).reshape(node_count, -1, rank_width)
        far_forward = jnp.einsum(
            "nsab,nsb->na", coupling, partner_coef, preferred_element_type=jnp.float32
        )
        far_part = far_forward + spread[box_rank] + mirror_in
        both = rep_sum(jnp.concatenate([near_part.reshape(-1), far_part.reshape(-1)]))
        near_total = both[:near_size].reshape(box_count, leaf)
        far_total = both[near_size:].reshape(node_count, rank_width)
        group_out = far_total[box_count:].astype(jnp.bfloat16)
        parent_pick = jnp.zeros((box_count, rank_width), jnp.bfloat16)
        for group in range(group_count):
            parent_pick = jnp.where((parent_local == group)[:, None], group_out[group][None], parent_pick)
        from_parent = jnp.einsum(
            "brq,bq->br", transfer, parent_pick, preferred_element_type=jnp.float32
        )
        downward = (far_total[:box_count] + from_parent).astype(jnp.bfloat16)
        far_field = jnp.einsum(
            "brl,br->bl", leaf_bases, downward, preferred_element_type=jnp.float32
        )
        image_vec = noise_var * direction + near_total + far_field
        partials = [direction * image_vec]
        if norm_now is None:
            partials.append(targets * targets)
        if iteration + 1 < ITERS:
            partials += [residual * image_vec, image_vec * image_vec]
        sums = box_sum(jnp.sum(jnp.stack(partials), axis=(1, 2)), leaf)
        curvature = sums[0:1]
        if norm_now is None:
            norm_now = sums[1:2]
        step_size = norm_now / curvature
        weights = weights + step_size * direction
        residual = residual - step_size * image_vec
        if iteration + 1 < ITERS:
            cross, image_square = sums[-2:-1], sums[-1:]
            norm_next = norm_now - 2.0 * step_size * cross + step_size * step_size * image_square
            direction = residual + (norm_next / norm_now) * direction
            norm_now = norm_next
    return (weights, residual)


def solution(mesh):
    placed = (
        P("box", None),
        P("box", None),
        P("box", "rep", None, None),
        P("box", "rep"),
        P("box", None, None),
        P("box", None, None),
        P("box"),
        P("box", "rep", None, None),
        P("box", "rep"),
    )
    return jax.shard_map(
        local,
        mesh=mesh,
        in_specs=placed,
        out_specs=(P("box", None), P("box", None)),
        check_vma=False,
    )
```

```python
import jax
import jax.numpy as jnp
from jax import lax
from jax.sharding import PartitionSpec as P

ITERS = 2


def rep_sum(vector):
    count = lax.axis_size("rep")
    if count == 4:
        got = [
            lax.ppermute(vector, "rep", [(i, i ^ mask) for i in range(count)])
            for mask in (1, 2, 3)
        ]
        return (vector + got[0]) + (got[1] + got[2])
    if count & (count - 1) == 0:
        stride = 1
        while stride < count:
            pairs = [(i, i ^ stride) for i in range(count)]
            vector = vector + lax.ppermute(vector, "rep", pairs)
            stride *= 2
        return vector
    me = lax.axis_index("rep")
    pieces = [vector]
    for shift in range(1, count):
        pairs = [(i, (i + shift) % count) for i in range(count)]
        pieces.append(lax.ppermute(vector, "rep", pairs))
    ordered = jnp.stack(pieces)[(me - jnp.arange(count)) % count]
    return jnp.sum(ordered, axis=0)


def box_sum(values, width):
    count = lax.axis_size("box")
    sent = jnp.broadcast_to(values[None, :], (count, values.shape[0]))
    got = lax.all_to_all(sent, "box", 0, 0, tiled=True)
    wide = lax.optimization_barrier(jnp.broadcast_to(got[:, :, None], got.shape + (width,)))
    return jnp.sum(wide, axis=0)


def local(
    targets,
    noise_var,
    near_tiles,
    near_partners,
    leaf_bases,
    transfer,
    parents,
    coupling,
    coupling_partners,
):
    box_count, leaf = targets.shape
    node_count = coupling.shape[0]
    group_count = node_count - box_count
    rank_width = coupling.shape[2]
    box_devices = lax.axis_size("box")
    box_rank = lax.axis_index("box")
    all_nodes = box_devices * node_count
    near_valid = near_partners >= 0
    near_local = jnp.where(near_valid, near_partners - box_rank * box_count, 0)
    near_onehot = (
        (jnp.arange(2 * box_count, dtype=jnp.int32)[:, None] == near_local.reshape(1, -1))
        & near_valid.reshape(1, -1)
    ).astype(jnp.float32)
    parent_local = parents - box_rank * group_count
    parent_onehot = (
        jnp.arange(group_count, dtype=jnp.int32)[:, None] == parent_local[None, :]
    ).astype(jnp.float32)
    far_valid = coupling_partners >= 0
    far_index = jnp.where(far_valid, coupling_partners, 0)
    far_pick = (
        (jnp.arange(all_nodes, dtype=jnp.int32)[:, None] == far_index.reshape(1, -1))
        & far_valid.reshape(1, -1)
    )
    bf_zero = jnp.zeros((), jnp.bfloat16)
    devices = jnp.arange(box_devices, dtype=jnp.int32)
    below = (devices < box_rank)[:, None, None]
    above = (devices > box_rank)[:, None, None]
    near_size = box_count * leaf
    far_size = node_count * rank_width

    weights = jnp.zeros_like(targets)
    residual = targets
    direction = targets
    norm_now = None
    for iteration in range(ITERS):
        rounded = direction.astype(jnp.bfloat16)
        mirrored = jnp.einsum(
            "bsij,bi->bsj", near_tiles, rounded, preferred_element_type=jnp.float32
        )
        landed = jnp.dot(
            near_onehot, mirrored.reshape(-1, mirrored.shape[2]), precision=lax.Precision.HIGHEST
        )
        leaf_coef = jnp.sum(
            leaf_bases.astype(jnp.float32) * rounded.astype(jnp.float32)[:, None, :], axis=2
        ).astype(jnp.bfloat16)
        upward = jnp.einsum("brq,br->bq", transfer, leaf_coef, preferred_element_type=jnp.float32)
        group_coef = jnp.dot(parent_onehot, upward, precision=lax.Precision.HIGHEST).astype(
            jnp.bfloat16
        )
        node_coef = jnp.concatenate([leaf_coef, group_coef], axis=0)
        far_mirror = jnp.einsum(
            "nsab,na->nsb", coupling, node_coef, preferred_element_type=jnp.float32
        )
        far_mirror = far_mirror * far_valid[:, :, None].astype(jnp.float32)
        spread = jnp.dot(
            far_pick.astype(jnp.float32), far_mirror.reshape(-1, rank_width),
            precision=lax.Precision.HIGHEST,
        ).reshape(box_devices, node_count, rank_width)
        following = lax.ppermute(
            rounded, "box", [(i, i - 1) for i in range(1, box_devices)]
        )
        coef_wide = node_coef.astype(jnp.float32)
        far_send = jnp.where(below, coef_wide[None], spread)
        is_next = (devices == box_rank + 1)[:, None]
        near_send = jnp.where(is_next, landed[box_count:].reshape(1, -1), 0.0)
        got = lax.all_to_all(
            jnp.concatenate([far_send.reshape(box_devices, far_size), near_send], axis=1),
            "box", 0, 0, tiled=True,
        )
        got_far = got[:, :far_size].reshape(box_devices, node_count, rank_width)
        is_prev = (devices == box_rank - 1)[:, None]
        arrived = jnp.sum(jnp.where(is_prev, got[:, far_size:], 0.0), axis=0).reshape(box_count, leaf)
        mirror_in = jnp.sum(jnp.where(below, got_far, 0.0), axis=0)
        every_coef = jnp.where(
            above, got_far, jnp.where(devices[:, None, None] == box_rank, coef_wide[None], 0.0)
        ).astype(jnp.bfloat16).reshape(all_nodes, rank_width)

        extended = jnp.concatenate([rounded, following], axis=0)
        near_in = jnp.dot(
            near_onehot.T.astype(jnp.bfloat16), extended, preferred_element_type=jnp.float32
        ).reshape(near_tiles.shape[0], near_tiles.shape[1], 1, leaf)
        forward = jnp.sum(near_tiles.astype(jnp.float32) * near_in, axis=(1, 3))
        near_part = forward + landed[:box_count] + arrived
        partner_coef = jnp.dot(
            far_pick.T.astype(jnp.bfloat16), every_coef, preferred_element_type=jnp.float32
        ).astype(jnp.bfloat16).reshape(node_count, -1, rank_width)
        far_forward = jnp.einsum(
            "nsab,nsb->na", coupling, partner_coef, preferred_element_type=jnp.float32
        )
        far_part = far_forward + spread[box_rank] + mirror_in
        both = rep_sum(jnp.concatenate([near_part.reshape(-1), far_part.reshape(-1)]))
        near_total = both[:near_size].reshape(box_count, leaf)
        far_total = both[near_size:].reshape(node_count, rank_width)
        group_out = far_total[box_count:].astype(jnp.bfloat16)
        parent_pick = jnp.zeros((box_count, rank_width), jnp.bfloat16)
        for group in range(group_count):
            parent_pick = jnp.where((parent_local == group)[:, None], group_out[group][None], parent_pick)
        from_parent = jnp.einsum(
            "brq,bq->br", transfer, parent_pick, preferred_element_type=jnp.float32
        )
        downward = (far_total[:box_count] + from_parent).astype(jnp.bfloat16)
        far_field = jnp.sum(
            leaf_bases.astype(jnp.float32) * downward.astype(jnp.float32)[:, :, None], axis=1
        )
        image_vec = noise_var * direction + near_total + far_field
        partials = [direction * image_vec]
        if norm_now is None:
            partials.append(targets * targets)
        if iteration + 1 < ITERS:
            partials += [residual * image_vec, image_vec * image_vec]
        sums = box_sum(jnp.sum(jnp.stack(partials), axis=(1, 2)), leaf)
        curvature = sums[0:1]
        if norm_now is None:
            norm_now = sums[1:2]
        step_size = norm_now / curvature
        weights = weights + step_size * direction
        residual = residual - step_size * image_vec
        if iteration + 1 < ITERS:
            cross, image_square = sums[-2:-1], sums[-1:]
            norm_next = norm_now - 2.0 * step_size * cross + step_size * step_size * image_square
            direction = residual + (norm_next / norm_now) * direction
            norm_now = norm_next
    return (weights, residual)


def solution(mesh):
    placed = (
        P("box", None),
        P("box", None),
        P("box", "rep", None, None),
        P("box", "rep"),
        P("box", None, None),
        P("box", None, None),
        P("box"),
        P("box", "rep", None, None),
        P("box", "rep"),
    )
    return jax.shard_map(
        local,
        mesh=mesh,
        in_specs=placed,
        out_specs=(P("box", None), P("box", None)),
        check_vma=False,
    )
```
